32 devices in a mesh: zone: 2 (over core), axial: 2 (over y), azim: 8 (over z, x).
Axes of the slice: x: 2, y: 2, z: 4, core: 2. Of those that a mesh axis runs over, the one named last changes fastest.
Arguments:
- adjoint: float32 [2, 5, 4, 4, 4, 2048], P('zone', None, None, None, None, ('axial', 'azim')), may hold values from -6 to 6
- flow_prim: bfloat16 [2, 5, 4, 4, 4, 2048], P('zone', None, None, None, None, ('axial', 'azim')), may hold values from -0.75 to 1.5, as said below
- intersection_shift: int32 [4, 4096], P(None, ('axial', 'azim')), may hold values from -8 to 7
- weight_index: int32 [4, 4096], P(None, ('axial', 'azim')), may hold values from 0 to 127
- mortar_weights: float32 [128], replicated, may hold values from 0.2 to 0.6
- sector_offset: int32 [1], replicated, may hold values from 0 to 127
Outputs:
- adjoint_rate: float32 [2, 5, 4, 4, 4, 2048], P('zone', None, None, None, None, ('axial', 'azim'))
- next_adjoint: float32 [2, 5, 4, 4, 4, 2048], P('zone', None, None, None, None, ('axial', 'azim'))
The draws below stay inside these ranges and needn't reach their ends.
Inputs may be any that keep to these rules, and one draw needn't show every extreme that they name: Entry k of stator interface row (a, t) names the rotor interface point at axial point a and azimuthal point (t + sector_offset + intersection_shift) modulo 128. `flow_prim`: channels are density, three velocity components and pressure; density lies in 0.6 to 1.4, pressure in 0.5 to 1.5, velocity components in -0.75 to 0.75.
All inputs are finite; a program needn't handle non-finite values.
Results may differ from the reference program's by a relative error of at most 0.0003.
Values sent between devices are 32-bit elements; how exact they have to be, the bound alone decides.
No kernel may reach another device: no remote copies, remote signals or barrier semaphores. Data moves between devices by JAX's collectives and lax.ppermute only.
A program may use at most 128 MiB of HBM per device.

```python
import math
import jax
import jax.numpy as jnp
from jax import lax

EA = 4
ET = 4
ER = 8
INTERSECTIONS = 4
NW = 128
ELEMS = 2048
NTP = 128
ROWS = 4096
N_AXIAL = 2
N_AZIM = 8


def draw_flow_prim(key, part):
    subkeys = jax.random.split(key, 3)
    lead_shape = (2, 1, 4, 4, 4, ELEMS)
    vel_shape = (2, 3, 4, 4, 4, ELEMS)
    density = jax.random.uniform(subkeys[0], lead_shape, jnp.float32, 0.7, 1.3)
    velocity = jnp.clip(0.25 * jax.random.normal(subkeys[1], vel_shape, jnp.float32), -0.75, 0.75)
    pressure = jax.random.uniform(subkeys[2], lead_shape, jnp.float32, 0.6, 1.4)
    return jnp.concatenate([density, velocity, pressure], axis=1).astype(jnp.bfloat16)


def touch_ends(entries, own_key, least, largest):
    longest = entries.shape.index(max(entries.shape))
    spots = []
    for shift in (0, 1):
        where = [jax.random.randint(jax.random.fold_in(own_key, axis), (), 0, length) for axis, length in enumerate(entries.shape)]
        where[longest] = (where[longest] + shift) % entries.shape[longest]
        spots.append(tuple(where))
    return entries.at[spots[0]].set(least).at[spots[1]].set(largest)


def level_of(own_key, dims, shards, low, largest):
    def one(dim, blocks):
        heights = jax.random.uniform(jax.random.fold_in(jax.random.fold_in(own_key, 6), dim), (blocks,), jnp.float32, low / len(shards), largest / len(shards))
        return jnp.repeat(jnp.exp(heights), dims[dim] // blocks).reshape((-1,) + (1,) * (len(dims) - dim - 1))

    loudness = one(*shards[0])
    for cut in shards[1:]:
        loudness = loudness * one(*cut)
    return loudness


def gaussian(stream_key, extent, scale, limit, cuts=(), held_as=jnp.bfloat16):
    factor_of = level_of(stream_key, extent, cuts, -0.22, 0.18) if cuts else 1.0
    values = jax.random.normal(stream_key, extent, jnp.float32) * scale * factor_of
    return jnp.minimum(jnp.maximum(values, -limit), limit).astype(held_as)


def setup_inputs(seed: int = 0) -> dict:
    streams_of = jax.random.split(jax.random.key(seed), 7)
    return {
        "adjoint": gaussian(streams_of[0], (2, 5, 4, 4, 4, ELEMS), 1.0, 6.0, ((0, 2), (5, 16)), jnp.float32),
        "flow_prim": draw_flow_prim(jax.random.fold_in(streams_of[6], 71), 0),
        "intersection_shift": touch_ends(jax.random.randint(streams_of[2], (INTERSECTIONS, ROWS), -2 * ET, 2 * ET), jax.random.fold_in(streams_of[2], 1), -2 * ET, (2 * ET) - 1).astype(jnp.int32),
        "weight_index": touch_ends(jax.random.randint(streams_of[3], (INTERSECTIONS, ROWS), 0, NW), jax.random.fold_in(streams_of[3], 1), 0, NW - 1).astype(jnp.int32),
        "mortar_weights": jnp.clip(jax.random.uniform(streams_of[4], (NW,), jnp.float32, 0.2, 0.6), 0.2, 0.6),
        "sector_offset": jax.random.randint(streams_of[5], (1,), 0, NTP).astype(jnp.int32),
    }


GAMMA = 1.4
METRIC = 0.1
SECTION_STEP = 0.5

def gauss_nodes():
    root_term = math.sqrt(6.0 / 5.0)
    inner_node = math.sqrt(3.0 / 7.0 - 2.0 / 7.0 * root_term)
    outer_node = math.sqrt(3.0 / 7.0 + 2.0 / 7.0 * root_term)
    return [-outer_node, -inner_node, inner_node, outer_node]

def lagrange_value(node_list, column, position):
    result = 1.0
    for factor_index in range(4):
        if factor_index != column:
            result = result * (position - node_list[factor_index]) / (node_list[column] - node_list[factor_index])
    return result

def lagrange_slope(node_list, column, position):
    total = 0.0
    for skipped in range(4):
        if skipped == column:
            continue
        term = 1.0 / (node_list[column] - node_list[skipped])
        for factor_index in range(4):
            if factor_index != column and factor_index != skipped:
                term = term * (position - node_list[factor_index]) / (node_list[column] - node_list[factor_index])
        total = total + term
    return total

def basis_tables():
    node_list = gauss_nodes()
    derivs = [[lagrange_slope(node_list, column, node_list[source]) for column in range(4)] for source in range(4)]
    left_vals = [lagrange_value(node_list, column, -1.0) for column in range(4)]
    right_vals = [lagrange_value(node_list, column, 1.0) for column in range(4)]
    third_slope = [(15.0 * value * value - 3.0) / 2.0 for value in node_list]
    fourth_slope = [(35.0 * value ** 3 - 15.0 * value) / 2.0 for value in node_list]
    left_corr = [-0.5 * (third_slope[source] - fourth_slope[source]) for source in range(4)]
    right_corr = [0.5 * (third_slope[source] + fourth_slope[source]) for source in range(4)]
    return (derivs, left_vals, right_vals, left_corr, right_corr)

def apply_points(adj_field, matrix, point_dim):
    slab_list = [lax.index_in_dim(adj_field, source, point_dim, keepdims=False) for source in range(4)]
    outputs = []
    for target in range(4):
        running = slab_list[0] * float(matrix[0][target])
        for source in range(1, 4):
            running = running + slab_list[source] * float(matrix[source][target])
        outputs.append(running)
    return jnp.stack(outputs, axis=point_dim)

def face_moment(adj_field, vector, point_dim):
    running = lax.index_in_dim(adj_field, 0, point_dim, keepdims=False) * float(vector[0])
    for source in range(1, 4):
        running = running + lax.index_in_dim(adj_field, source, point_dim, keepdims=False) * float(vector[source])
    return running

def lift_face(face_vals, vector, point_dim):
    return jnp.stack([face_vals * float(vector[target]) for target in range(4)], axis=point_dim)

def conserved(primitive):
    density = primitive[0]
    velocity = primitive[1:4]
    pressure = primitive[4]
    energy = pressure / (GAMMA - 1.0) + 0.5 * density * lax.optimization_barrier(jnp.sum(velocity * velocity, axis=0))
    return jnp.concatenate([density[None], density[None] * velocity, energy[None]], axis=0)

def euler_flux(cons_state, direction):
    density = cons_state[0]
    momentum = cons_state[1:4]
    energy = cons_state[4]
    velocity = momentum / density[None]
    pressure = (GAMMA - 1.0) * (energy - 0.5 * lax.optimization_barrier(jnp.sum(momentum * velocity, axis=0)))
    normal_speed = velocity[direction]
    columns = [momentum[direction]]
    for component in range(3):
        if component == direction:
            columns.append(momentum[component] * normal_speed + pressure)
        else:
            columns.append(momentum[component] * normal_speed)
    columns.append((energy + pressure) * normal_speed)
    return jnp.stack(columns, axis=0)

def transpose_flux(cons_state, cotangent, direction):
    unused, pullback = jax.vjp(lambda current: euler_flux(current, direction), cons_state)
    return pullback(cotangent)[0]

def section_rate(adj_field, cons_state, left_moments, right_moments, next_left, prev_right):
    derivs, left_vals, right_vals, left_corr, right_corr = basis_tables()
    rate_sum = jnp.zeros_like(adj_field)
    for direction in range(3):
        point_dim = 1 + direction
        bracket = apply_points(adj_field, derivs, point_dim)
        bracket = bracket + 0.5 * lift_face(next_left[direction] - right_moments[direction], right_vals, point_dim)
        bracket = bracket + 0.5 * lift_face(prev_right[direction] - left_moments[direction], left_vals, point_dim)
        rate_sum = rate_sum - METRIC * transpose_flux(cons_state, bracket, direction)
    return rate_sum

def all_moments(adj_field):
    derivs, left_vals, right_vals, left_corr, right_corr = basis_tables()
    left_moments = [face_moment(adj_field, left_corr, 1 + direction) for direction in range(3)]
    right_moments = [face_moment(adj_field, right_corr, 1 + direction) for direction in range(3)]
    return (left_moments, right_moments)

def faces_to_rows(face_vals):
    axial_elems = face_vals.shape[3]
    azim_elems = face_vals.shape[4]
    return face_vals.transpose(0, 3, 1, 4, 2).reshape(5, 4 * axial_elems, 4 * azim_elems)

def rows_to_face(rows_vals, axial_elems, azim_elems):
    return rows_vals.reshape(5, axial_elems, 4, azim_elems, 4).transpose(0, 2, 4, 1, 3)

def to_grid(array):
    blocks = array.reshape(2, 5, 4, 4, 4, N_AXIAL, N_AZIM, EA, ET, ER)
    blocks = blocks.transpose(0, 1, 2, 3, 4, 5, 7, 6, 8, 9)
    return blocks.reshape(2, 5, 4, 4, 4, N_AXIAL * EA, N_AZIM * ET, ER)

def from_grid(grid):
    blocks = grid.reshape(2, 5, 4, 4, 4, N_AXIAL, EA, N_AZIM, ET, ER)
    blocks = blocks.transpose(0, 1, 2, 3, 4, 5, 7, 6, 8, 9)
    return blocks.reshape(2, 5, 4, 4, 4, ELEMS)

def rows_grid(lists):
    blocks = lists.reshape(INTERSECTIONS, N_AXIAL, N_AZIM, 4 * EA, 4 * ET)
    return blocks.transpose(0, 1, 3, 2, 4).reshape(INTERSECTIONS, N_AXIAL * 4 * EA, N_AZIM * 4 * ET)

def reference(adjoint, flow_prim, intersection_shift, weight_index, mortar_weights, sector_offset):
    grid_adjoint = to_grid(adjoint)
    grid_flow = to_grid(flow_prim.astype(jnp.float32))
    moments_zone = [all_moments(grid_adjoint[zone_index]) for zone_index in range(2)]
    rotor_rows = faces_to_rows(moments_zone[0][1][2][..., -1])
    stator_rows = faces_to_rows(moments_zone[1][0][2][..., 0])
    axial_points = 4 * EA * N_AXIAL
    cycle_points = 4 * ET * N_AZIM
    shifts_grid = rows_grid(intersection_shift)
    index_grid = rows_grid(weight_index)
    t_global = jnp.arange(cycle_points, dtype=jnp.int32)[None, :]
    axial_index = jnp.arange(axial_points, dtype=jnp.int32)[:, None]
    incoming = jnp.zeros((5, axial_points, cycle_points), jnp.float32)
    returned_flat = jnp.zeros((5, axial_points * cycle_points), jnp.float32)
    for member in range(INTERSECTIONS):
        positions = (t_global + sector_offset[0] + shifts_grid[member]) % cycle_points
        weight = mortar_weights[index_grid[member]]
        picked = jnp.take_along_axis(rotor_rows, jnp.broadcast_to(positions[None], rotor_rows.shape), axis=2)
        incoming = incoming + weight[None] * picked
        flat_index = (axial_index * cycle_points + positions).reshape(-1)
        returned_flat = returned_flat.at[:, flat_index].add((weight[None] * stator_rows).reshape(5, -1))
    returned = returned_flat.reshape(5, axial_points, cycle_points)
    rates = []
    for zone_index in range(2):
        adj_field = grid_adjoint[zone_index]
        cons_state = conserved(grid_flow[zone_index])
        left_moments, right_moments = moments_zone[zone_index]
        zero_axial = jnp.zeros_like(left_moments[0][:, :, :, :1])
        zero_radial = jnp.zeros_like(left_moments[2][..., :1])
        if zone_index == 0:
            outer_face = rows_to_face(returned, N_AXIAL * EA, N_AZIM * ET)[..., None]
            inner_face = zero_radial
        else:
            outer_face = zero_radial
            inner_face = rows_to_face(incoming, N_AXIAL * EA, N_AZIM * ET)[..., None]
        next_left = [jnp.concatenate([left_moments[0][:, :, :, 1:], zero_axial], axis=3), jnp.roll(left_moments[1], -1, axis=4), jnp.concatenate([left_moments[2][..., 1:], outer_face], axis=5)]
        prev_right = [jnp.concatenate([zero_axial, right_moments[0][:, :, :, :-1]], axis=3), jnp.roll(right_moments[1], 1, axis=4), jnp.concatenate([inner_face, right_moments[2][..., :-1]], axis=5)]
        rates.append(section_rate(adj_field, cons_state, left_moments, right_moments, next_left, prev_right))
    adjoint_rate = from_grid(jnp.stack(rates))
    next_adjoint = adjoint + SECTION_STEP * adjoint_rate
    return (adjoint_rate, next_adjoint)
```

```python
import math

import jax
import jax.numpy as jnp
from jax import lax
from jax.sharding import PartitionSpec as P

EA = 4
ET = 4
ER = 8
INTERSECTIONS = 4
NW = 128
AP = 16
TP = 16


GAMMA = 1.4
METRIC = 0.1
SECTION_STEP = 0.5


def gauss_nodes():
    root_term = math.sqrt(6.0 / 5.0)
    inner_node = math.sqrt(3.0 / 7.0 - 2.0 / 7.0 * root_term)
    outer_node = math.sqrt(3.0 / 7.0 + 2.0 / 7.0 * root_term)
    return [-outer_node, -inner_node, inner_node, outer_node]


def lagrange_value(node_list, column, position):
    result = 1.0
    for factor_index in range(4):
        if factor_index != column:
            result = (
                result
                * (position - node_list[factor_index])
                / (node_list[column] - node_list[factor_index])
            )
    return result


def lagrange_slope(node_list, column, position):
    total = 0.0
    for skipped in range(4):
        if skipped == column:
            continue
        term = 1.0 / (node_list[column] - node_list[skipped])
        for factor_index in range(4):
            if factor_index != column and factor_index != skipped:
                term = (
                    term
                    * (position - node_list[factor_index])
                    / (node_list[column] - node_list[factor_index])
                )
        total = total + term
    return total


def basis_tables():
    node_list = gauss_nodes()
    derivs = [
        [lagrange_slope(node_list, column, node_list[source]) for column in range(4)]
        for source in range(4)
    ]
    left_vals = [lagrange_value(node_list, column, -1.0) for column in range(4)]
    right_vals = [lagrange_value(node_list, column, 1.0) for column in range(4)]
    third_slope = [(15.0 * value * value - 3.0) / 2.0 for value in node_list]
    fourth_slope = [(35.0 * value**3 - 15.0 * value) / 2.0 for value in node_list]
    left_corr = [-0.5 * (third_slope[source] - fourth_slope[source]) for source in range(4)]
    right_corr = [0.5 * (third_slope[source] + fourth_slope[source]) for source in range(4)]
    return (derivs, left_vals, right_vals, left_corr, right_corr)


def apply_points(adj_field, matrix, point_dim):
    slab_list = [
        lax.index_in_dim(adj_field, source, point_dim, keepdims=False) for source in range(4)
    ]
    outputs = []
    for target in range(4):
        running = slab_list[0] * float(matrix[0][target])
        for source in range(1, 4):
            running = running + slab_list[source] * float(matrix[source][target])
        outputs.append(running)
    return jnp.stack(outputs, axis=point_dim)


def face_moment(adj_field, vector, point_dim):
    running = lax.index_in_dim(adj_field, 0, point_dim, keepdims=False) * float(vector[0])
    for source in range(1, 4):
        running = running + lax.index_in_dim(adj_field, source, point_dim, keepdims=False) * float(
            vector[source]
        )
    return running


def lift_face(face_vals, vector, point_dim):
    return jnp.stack([face_vals * float(vector[target]) for target in range(4)], axis=point_dim)


def conserved(primitive):
    density = primitive[0]
    velocity = primitive[1:4]
    pressure = primitive[4]
    energy = pressure / (GAMMA - 1.0) + 0.5 * density * jnp.sum(velocity * velocity, axis=0)
    return jnp.concatenate([density[None], density[None] * velocity, energy[None]], axis=0)


def euler_flux(cons_state, direction):
    density = cons_state[0]
    momentum = cons_state[1:4]
    energy = cons_state[4]
    velocity = momentum / density[None]
    pressure = (GAMMA - 1.0) * (energy - 0.5 * jnp.sum(momentum * velocity, axis=0))
    normal_speed = velocity[direction]
    columns = [momentum[direction]]
    for component in range(3):
        if component == direction:
            columns.append(momentum[component] * normal_speed + pressure)
        else:
            columns.append(momentum[component] * normal_speed)
    columns.append((energy + pressure) * normal_speed)
    return jnp.stack(columns, axis=0)


def transpose_flux(cons_state, cotangent, direction):
    unused, pullback = jax.vjp(lambda current: euler_flux(current, direction), cons_state)
    return pullback(cotangent)[0]


def section_rate(adj_field, cons_state, left_moments, right_moments, next_left, prev_right):
    derivs, left_vals, right_vals, left_corr, right_corr = basis_tables()
    rate_sum = jnp.zeros_like(adj_field)
    for direction in range(3):
        point_dim = 1 + direction
        bracket = apply_points(adj_field, derivs, point_dim)
        bracket = bracket + 0.5 * lift_face(
            next_left[direction] - right_moments[direction], right_vals, point_dim
        )
        bracket = bracket + 0.5 * lift_face(
            prev_right[direction] - left_moments[direction], left_vals, point_dim
        )
        rate_sum = rate_sum - METRIC * transpose_flux(cons_state, bracket, direction)
    return rate_sum


def all_moments(adj_field):
    derivs, left_vals, right_vals, left_corr, right_corr = basis_tables()
    left_moments = [face_moment(adj_field, left_corr, 1 + direction) for direction in range(3)]
    right_moments = [face_moment(adj_field, right_corr, 1 + direction) for direction in range(3)]
    return (left_moments, right_moments)


def faces_to_rows(face_vals):
    axial_elems = face_vals.shape[3]
    azim_elems = face_vals.shape[4]
    return face_vals.transpose(0, 3, 1, 4, 2).reshape(5, 4 * axial_elems, 4 * azim_elems)


def rows_to_face(rows_vals, axial_elems, azim_elems):
    return rows_vals.reshape(5, axial_elems, 4, azim_elems, 4).transpose(0, 2, 4, 1, 3)


def shift_sum(window, coefs, lo):
    total = None
    for offset, coef in coefs:
        term = coef[None] * window[:, :, lo + offset : lo + offset + TP]
        total = term if total is None else total + term
    return total


def local(adjoint, flow_prim, intersection_shift, weight_index, mortar_weights, sector_offset):
    elem_count = EA * ET * ER
    n_axial = lax.axis_size("axial")
    n_azim = lax.axis_size("azim")
    adj_field = adjoint[0]
    cons_state = conserved(flow_prim[0].astype(jnp.float32))
    left_moments, right_moments = all_moments(adj_field)
    is_rotor = lax.axis_index("zone") == 0
    face_shape = (5, 4, 4, EA, ET, ER)
    ax_span = ET * ER
    upper_axial = lax.ppermute(
        left_moments[0][..., :ax_span], "axial", [(i + 1, i) for i in range(n_axial - 1)]
    )
    lower_axial = lax.ppermute(
        right_moments[0][..., elem_count - ax_span :],
        "axial",
        [(i, i + 1) for i in range(n_axial - 1)],
    )
    next_axial = jnp.concatenate([left_moments[0][..., ax_span:], upper_axial], axis=-1)
    prev_axial = jnp.concatenate([lower_axial, right_moments[0][..., : elem_count - ax_span]], axis=-1)
    left_az = left_moments[1].reshape(face_shape)
    right_az = right_moments[1].reshape(face_shape)
    upper_azim = lax.ppermute(
        left_az[:, :, :, :, :1], "azim", [((j + 1) % n_azim, j) for j in range(n_azim)]
    )
    lower_azim = lax.ppermute(
        right_az[:, :, :, :, ET - 1 :], "azim", [(j, (j + 1) % n_azim) for j in range(n_azim)]
    )
    next_azim = jnp.concatenate([left_az[:, :, :, :, 1:], upper_azim], axis=4).reshape(
        5, 4, 4, elem_count
    )
    prev_azim = jnp.concatenate([lower_azim, right_az[:, :, :, :, : ET - 1]], axis=4).reshape(
        5, 4, 4, elem_count
    )
    left_rad = left_moments[2].reshape(face_shape)
    right_rad = right_moments[2].reshape(face_shape)
    own_face = jnp.where(is_rotor, right_rad[..., -1], left_rad[..., 0])
    own_rows = faces_to_rows(own_face)
    shifts_local = intersection_shift.reshape(INTERSECTIONS, AP, TP)
    table_match = weight_index[:, :, None] == jnp.arange(NW, dtype=jnp.int32)[None, None, :]
    weights_local = jnp.sum(
        jnp.where(table_match, mortar_weights[None, None, :], 0.0), axis=2
    ).reshape(INTERSECTIONS, AP, TP)
    offset = sector_offset[0]
    turn = (offset + TP // 2) // TP
    residue = offset - turn * TP
    offsets_k = residue + shifts_local
    coefs = []
    for rel in range(-TP, TP - 1):
        coef = jnp.where(offsets_k[0] == rel, weights_local[0], 0.0)
        for member in range(1, INTERSECTIONS):
            coef = coef + jnp.where(offsets_k[member] == rel, weights_local[member], 0.0)
        coefs.append((rel, coef))
    contrib = None
    for rel, coef in coefs:
        term = jnp.pad(coef[None] * own_rows, ((0, 0), (0, 0), (TP + rel, TP - rel)))
        contrib = term if contrib is None else contrib + term
    received = []
    for dist in range(n_azim):
        gap = (dist - turn) % n_azim
        piece = jnp.where(
            gap == n_azim - 1,
            contrib[:, :, :TP],
            jnp.where(gap == 0, contrib[:, :, TP : 2 * TP], contrib[:, :, 2 * TP :]),
        )
        payload = jnp.where(is_rotor, own_rows, piece)
        pairs = [(j, n_azim + (j - dist) % n_azim) for j in range(n_azim)] + [
            (n_azim + j, (j + dist) % n_azim) for j in range(n_azim)
        ]
        received.append(lax.ppermute(payload, ("zone", "azim"), pairs))
    stacked = jnp.stack(received)
    picked = [
        lax.dynamic_index_in_dim(stacked, (turn + step) % n_azim, 0, keepdims=False)
        for step in (-1, 0, 1)
    ]
    returned = picked[0] + picked[1] + picked[2]
    window = jnp.concatenate(picked, axis=2)
    incoming = shift_sum(window, coefs, TP)
    outer_face = jnp.where(is_rotor, rows_to_face(returned, EA, ET), 0.0)
    inner_face = jnp.where(is_rotor, 0.0, rows_to_face(incoming, EA, ET))
    next_radial = jnp.concatenate([left_rad[..., 1:], outer_face[..., None]], axis=5).reshape(
        5, 4, 4, elem_count
    )
    prev_radial = jnp.concatenate([inner_face[..., None], right_rad[..., :-1]], axis=5).reshape(
        5, 4, 4, elem_count
    )
    next_left = [next_axial, next_azim, next_radial]
    prev_right = [prev_axial, prev_azim, prev_radial]
    rate_sum = section_rate(
        adj_field, cons_state, left_moments, right_moments, next_left, prev_right
    )
    adjoint_rate = rate_sum.reshape(1, 5, 4, 4, 4, elem_count)
    next_adjoint = adjoint + SECTION_STEP * adjoint_rate
    return (adjoint_rate, next_adjoint)


def solution(mesh):
    placed = (
        P("zone", None, None, None, None, ("axial", "azim")),
        P("zone", None, None, None, None, ("axial", "azim")),
        P(None, ("axial", "azim")),
        P(None, ("axial", "azim")),
        P(),
        P(),
    )
    return jax.shard_map(
        local,
        mesh=mesh,
        in_specs=placed,
        out_specs=(
            P("zone", None, None, None, None, ("axial", "azim")),
            P("zone", None, None, None, None, ("axial", "azim")),
        ),
        check_vma=False,
    )
```

```python
import math

import jax
import jax.numpy as jnp
from jax import lax
from jax.experimental import pallas as pl
from jax.experimental.pallas import tpu as pltpu
from jax.sharding import PartitionSpec as P

EA = 4
ET = 4
ER = 8
INTERSECTIONS = 4
NW = 128
AP = 16
TP = 16


GAMMA = 1.4
METRIC = 0.1
SECTION_STEP = 0.5


def gauss_nodes():
    root_term = math.sqrt(6.0 / 5.0)
    inner_node = math.sqrt(3.0 / 7.0 - 2.0 / 7.0 * root_term)
    outer_node = math.sqrt(3.0 / 7.0 + 2.0 / 7.0 * root_term)
    return [-outer_node, -inner_node, inner_node, outer_node]


def lagrange_value(node_list, column, position):
    result = 1.0
    for factor_index in range(4):
        if factor_index != column:
            result = (
                result
                * (position - node_list[factor_index])
                / (node_list[column] - node_list[factor_index])
            )
    return result


def lagrange_slope(node_list, column, position):
    total = 0.0
    for skipped in range(4):
        if skipped == column:
            continue
        term = 1.0 / (node_list[column] - node_list[skipped])
        for factor_index in range(4):
            if factor_index != column and factor_index != skipped:
                term = (
                    term
                    * (position - node_list[factor_index])
                    / (node_list[column] - node_list[factor_index])
                )
        total = total + term
    return total


def basis_tables():
    node_list = gauss_nodes()
    derivs = [
        [lagrange_slope(node_list, column, node_list[source]) for column in range(4)]
        for source in range(4)
    ]
    left_vals = [lagrange_value(node_list, column, -1.0) for column in range(4)]
    right_vals = [lagrange_value(node_list, column, 1.0) for column in range(4)]
    third_slope = [(15.0 * value * value - 3.0) / 2.0 for value in node_list]
    fourth_slope = [(35.0 * value**3 - 15.0 * value) / 2.0 for value in node_list]
    left_corr = [-0.5 * (third_slope[source] - fourth_slope[source]) for source in range(4)]
    right_corr = [0.5 * (third_slope[source] + fourth_slope[source]) for source in range(4)]
    return (derivs, left_vals, right_vals, left_corr, right_corr)


def apply_points(adj_field, matrix, point_dim):
    slab_list = [
        lax.index_in_dim(adj_field, source, point_dim, keepdims=False) for source in range(4)
    ]
    outputs = []
    for target in range(4):
        running = slab_list[0] * float(matrix[0][target])
        for source in range(1, 4):
            running = running + slab_list[source] * float(matrix[source][target])
        outputs.append(running)
    return jnp.stack(outputs, axis=point_dim)


def face_moment(adj_field, vector, point_dim):
    running = lax.index_in_dim(adj_field, 0, point_dim, keepdims=False) * float(vector[0])
    for source in range(1, 4):
        running = running + lax.index_in_dim(adj_field, source, point_dim, keepdims=False) * float(
            vector[source]
        )
    return running


def lift_face(face_vals, vector, point_dim):
    return jnp.stack([face_vals * float(vector[target]) for target in range(4)], axis=point_dim)


def conserved(primitive):
    density = primitive[0]
    velocity = primitive[1:4]
    pressure = primitive[4]
    energy = pressure / (GAMMA - 1.0) + 0.5 * density * jnp.sum(velocity * velocity, axis=0)
    return jnp.concatenate([density[None], density[None] * velocity, energy[None]], axis=0)


def euler_flux(cons_state, direction):
    density = cons_state[0]
    momentum = cons_state[1:4]
    energy = cons_state[4]
    velocity = momentum / density[None]
    pressure = (GAMMA - 1.0) * (energy - 0.5 * jnp.sum(momentum * velocity, axis=0))
    normal_speed = velocity[direction]
    columns = [momentum[direction]]
    for component in range(3):
        if component == direction:
            columns.append(momentum[component] * normal_speed + pressure)
        else:
            columns.append(momentum[component] * normal_speed)
    columns.append((energy + pressure) * normal_speed)
    return jnp.stack(columns, axis=0)


def transpose_flux(cons_state, cotangent, direction):
    unused, pullback = jax.vjp(lambda current: euler_flux(current, direction), cons_state)
    return pullback(cotangent)[0]


def section_rate(adj_field, cons_state, left_moments, right_moments, next_left, prev_right):
    derivs, left_vals, right_vals, left_corr, right_corr = basis_tables()
    rate_sum = jnp.zeros_like(adj_field)
    for direction in range(3):
        point_dim = 1 + direction
        bracket = apply_points(adj_field, derivs, point_dim)
        bracket = bracket + 0.5 * lift_face(
            next_left[direction] - right_moments[direction], right_vals, point_dim
        )
        bracket = bracket + 0.5 * lift_face(
            prev_right[direction] - left_moments[direction], left_vals, point_dim
        )
        rate_sum = rate_sum - METRIC * transpose_flux(cons_state, bracket, direction)
    return rate_sum


def all_moments(adj_field):
    derivs, left_vals, right_vals, left_corr, right_corr = basis_tables()
    left_moments = [face_moment(adj_field, left_corr, 1 + direction) for direction in range(3)]
    right_moments = [face_moment(adj_field, right_corr, 1 + direction) for direction in range(3)]
    return (left_moments, right_moments)


def faces_to_rows(face_vals):
    axial_elems = face_vals.shape[3]
    azim_elems = face_vals.shape[4]
    return face_vals.transpose(0, 3, 1, 4, 2).reshape(5, 4 * axial_elems, 4 * azim_elems)


def rows_to_face(rows_vals, axial_elems, azim_elems):
    return rows_vals.reshape(5, axial_elems, 4, azim_elems, 4).transpose(0, 2, 4, 1, 3)


def shift_sum(window, coefs, lo):
    total = None
    for offset, coef in coefs:
        term = coef[None] * window[:, :, lo + offset : lo + offset + TP]
        total = term if total is None else total + term
    return total


def lane_roll(value, shift):
    return pltpu.roll(value, shift % 128, value.ndim - 1)


def sweep(field, weights, pick):
    total = field[pick(0)] * float(weights[0])
    for source in range(1, 4):
        total = total + field[pick(source)] * float(weights[source])
    return total


def column(values, shape):
    rows = lax.broadcasted_iota(jnp.int32, shape, 2)
    out = jnp.full(shape, float(values[3]), jnp.float32)
    for index in range(3):
        out = jnp.where(rows == index, float(values[index]), out)
    return out


def rate_kernel(
    adj_ref, flow_ref, up_ax_ref, down_ax_ref, up_az_ref, down_az_ref, outer_ref, inner_ref,
    rate_ref, next_ref,
):
    derivs, left_vals, right_vals, left_corr, right_corr = basis_tables()
    shape = (4, 4, 4, 128)
    lane = lax.broadcasted_iota(jnp.int32, shape, 3)
    flat_lane = lax.broadcasted_iota(jnp.int32, (4, 4, 128), 2)
    az_flat = flat_lane // ER % ET
    radial_lane = lane % ER
    brackets = [[None] * 5 for _ in range(3)]
    for chan in range(5):
        field = adj_ref[0, chan]
        left0 = sweep(field, left_corr, lambda i: (i,))
        right0 = sweep(field, right_corr, lambda i: (i,))
        next0 = lane_roll(jnp.where(flat_lane < ET * ER, up_ax_ref[chan], left0), -ET * ER)
        prev0 = lane_roll(jnp.where(flat_lane >= (EA - 1) * ET * ER, down_ax_ref[chan], right0), ET * ER)
        jump_r = 0.5 * (next0 - right0)
        jump_l = 0.5 * (prev0 - left0)
        slabs = []
        for target in range(4):
            slab = sweep(field, [derivs[i][target] for i in range(4)], lambda i: (i,))
            slabs.append(slab + jump_r * float(right_vals[target]) + jump_l * float(left_vals[target]))
        brackets[0][chan] = jnp.stack(slabs, axis=0)
        pick1 = lambda i: (slice(None), i)
        left1 = sweep(field, left_corr, pick1)
        right1 = sweep(field, right_corr, pick1)
        next1 = lane_roll(
            jnp.where(az_flat == 0, lane_roll(up_az_ref[chan], ET * ER), left1), -ER
        )
        prev1 = lane_roll(
            jnp.where(az_flat == ET - 1, lane_roll(down_az_ref[chan], -ET * ER), right1), ER
        )
        jump_r = 0.5 * (next1 - right1)
        jump_l = 0.5 * (prev1 - left1)
        slabs = []
        for target in range(4):
            slab = sweep(field, [derivs[i][target] for i in range(4)], pick1)
            slabs.append(slab + jump_r * float(right_vals[target]) + jump_l * float(left_vals[target]))
        brackets[1][chan] = jnp.stack(slabs, axis=1)
        points = [jnp.broadcast_to(field[:, :, i : i + 1, :], shape) for i in range(4)]
        left2 = sweep(points, left_corr, lambda i: i)
        right2 = sweep(points, right_corr, lambda i: i)
        next2 = jnp.where(radial_lane == ER - 1, outer_ref[chan], lane_roll(left2, -1))
        prev2 = jnp.where(radial_lane == 0, inner_ref[chan], lane_roll(right2, 1))
        bracket = 0.5 * (next2 - right2) * column(right_vals, shape)
        bracket = bracket + 0.5 * (prev2 - left2) * column(left_vals, shape)
        for source in range(4):
            bracket = bracket + points[source] * column(derivs[source], shape)
        brackets[2][chan] = bracket
    prim = [flow_ref[0, chan].astype(jnp.float32) for chan in range(5)]
    density = prim[0]
    speed_sq = prim[1] * prim[1] + prim[2] * prim[2] + prim[3] * prim[3]
    energy = prim[4] / (GAMMA - 1.0) + 0.5 * density * speed_sq
    momentum = [density * prim[1 + k] for k in range(3)]
    velocity = [momentum[k] / density for k in range(3)]
    kinetic = momentum[0] * velocity[0] + momentum[1] * velocity[1] + momentum[2] * velocity[2]
    pressure = (GAMMA - 1.0) * (energy - 0.5 * kinetic)
    enthalpy = (energy + pressure) / density
    vel_sq = velocity[0] * velocity[0] + velocity[1] * velocity[1] + velocity[2] * velocity[2]
    grad = [None] * 5
    for direction in range(3):
        cot = brackets[direction]
        normal = velocity[direction]
        dotted = cot[1] * velocity[0] + cot[2] * velocity[1] + cot[3] * velocity[2] + cot[4] * enthalpy
        weight = cot[1 + direction] + cot[4] * normal
        terms = [
            0.5 * (GAMMA - 1.0) * vel_sq * weight - dotted * normal,
            None,
            None,
            None,
            (GAMMA - 1.0) * weight + cot[4] * normal,
        ]
        for k in range(3):
            term = cot[1 + k] * normal - (GAMMA - 1.0) * weight * velocity[k]
            if k == direction:
                term = term + (cot[0] + dotted)
            terms[1 + k] = term
        for chan in range(5):
            grad[chan] = terms[chan] if grad[chan] is None else grad[chan] + terms[chan]
    for chan in range(5):
        rate = -METRIC * grad[chan]
        rate_ref[0, chan] = rate
        next_ref[0, chan] = adj_ref[0, chan] + SECTION_STEP * rate


def local(adjoint, flow_prim, intersection_shift, weight_index, mortar_weights, sector_offset):
    n_axial = lax.axis_size("axial")
    n_azim = lax.axis_size("azim")
    adj_field = adjoint[0]
    derivs, left_vals, right_vals, left_corr, right_corr = basis_tables()
    left_ax = face_moment(adj_field, left_corr, 1)
    right_ax = face_moment(adj_field, right_corr, 1)
    left_az = face_moment(adj_field, left_corr, 2)
    right_az = face_moment(adj_field, right_corr, 2)
    is_rotor = lax.axis_index("zone") == 0
    up_ax = lax.ppermute(left_ax, "axial", [(i + 1, i) for i in range(n_axial - 1)])
    down_ax = lax.ppermute(right_ax, "axial", [(i, i + 1) for i in range(n_axial - 1)])
    up_az = lax.ppermute(left_az, "azim", [((j + 1) % n_azim, j) for j in range(n_azim)])
    down_az = lax.ppermute(right_az, "azim", [(j, (j + 1) % n_azim) for j in range(n_azim)])
    face_shape = (5, 4, 4, EA, ET, ER)
    outer_moment = face_moment(adj_field, right_corr, 3).reshape(face_shape)[..., ER - 1]
    inner_moment = face_moment(adj_field, left_corr, 3).reshape(face_shape)[..., 0]
    own_rows = faces_to_rows(jnp.where(is_rotor, outer_moment, inner_moment))
    shifts_local = intersection_shift.reshape(INTERSECTIONS, AP, TP)
    table_match = weight_index[:, :, None] == jnp.arange(NW, dtype=jnp.int32)[None, None, :]
    weights_local = jnp.sum(
        jnp.where(table_match, mortar_weights[None, None, :], 0.0), axis=2
    ).reshape(INTERSECTIONS, AP, TP)
    offset = sector_offset[0]
    turn = (offset + TP // 2) // TP
    residue = offset - turn * TP
    offsets_k = residue + shifts_local
    coefs = []
    for rel in range(-TP, TP - 1):
        coef = jnp.where(offsets_k[0] == rel, weights_local[0], 0.0)
        for member in range(1, INTERSECTIONS):
            coef = coef + jnp.where(offsets_k[member] == rel, weights_local[member], 0.0)
        coefs.append((rel, coef))
    contrib = None
    for rel, coef in coefs:
        term = jnp.pad(coef[None] * own_rows, ((0, 0), (0, 0), (TP + rel, TP - rel)))
        contrib = term if contrib is None else contrib + term
    received = []
    for dist in range(n_azim):
        gap = (dist - turn) % n_azim
        piece = jnp.where(
            gap == n_azim - 1,
            contrib[:, :, :TP],
            jnp.where(gap == 0, contrib[:, :, TP : 2 * TP], contrib[:, :, 2 * TP :]),
        )
        payload = jnp.where(is_rotor, own_rows, piece)
        pairs = [(j, n_azim + (j - dist) % n_azim) for j in range(n_azim)] + [
            (n_azim + j, (j + dist) % n_azim) for j in range(n_azim)
        ]
        received.append(lax.ppermute(payload, ("zone", "azim"), pairs))
    stacked = jnp.stack(received)
    picked = [
        lax.dynamic_index_in_dim(stacked, (turn + step) % n_azim, 0, keepdims=False)
        for step in (-1, 0, 1)
    ]
    returned = picked[0] + picked[1] + picked[2]
    window = jnp.concatenate(picked, axis=2)
    incoming = shift_sum(window, coefs, TP)
    iface = rows_to_face(jnp.where(is_rotor, returned, incoming), EA, ET)
    iface = jnp.broadcast_to(
        iface[:, :, :, None, :, :, None], (5, 4, 4, 4, EA, ET, ER)
    ).reshape(5, 4, 4, 4, EA * ET * ER)
    outer = jnp.where(is_rotor, iface, 0.0)
    inner = jnp.where(is_rotor, 0.0, iface)
    field_shape = jax.ShapeDtypeStruct(adjoint.shape, jnp.float32)
    adjoint_rate, next_adjoint = pl.pallas_call(
        rate_kernel, out_shape=(field_shape, field_shape)
    )(adjoint, flow_prim, up_ax, down_ax, up_az, down_az, outer, inner)
    return (adjoint_rate, next_adjoint)


def solution(mesh):
    placed = (
        P("zone", None, None, None, None, ("axial", "azim")),
        P("zone", None, None, None, None, ("axial", "azim")),
        P(None, ("axial", "azim")),
        P(None, ("axial", "azim")),
        P(),
        P(),
    )
    return jax.shard_map(
        local,
        mesh=mesh,
        in_specs=placed,
        out_specs=(
            P("zone", None, None, None, None, ("axial", "azim")),
            P("zone", None, None, None, None, ("axial", "azim")),
        ),
        check_vma=False,
    )
```

```python
import math

import jax
import jax.numpy as jnp
from jax import lax
from jax.experimental import pallas as pl
from jax.experimental.pallas import tpu as pltpu
from jax.sharding import PartitionSpec as P

EA = 4
ET = 4
ER = 8
INTERSECTIONS = 4
NW = 128
AP = 16
TP = 16


GAMMA = 1.4
METRIC = 0.1
SECTION_STEP = 0.5


def gauss_nodes():
    root_term = math.sqrt(6.0 / 5.0)
    inner_node = math.sqrt(3.0 / 7.0 - 2.0 / 7.0 * root_term)
    outer_node = math.sqrt(3.0 / 7.0 + 2.0 / 7.0 * root_term)
    return [-outer_node, -inner_node, inner_node, outer_node]


def lagrange_value(node_list, column, position):
    result = 1.0
    for factor_index in range(4):
        if factor_index != column:
            result = (
                result
                * (position - node_list[factor_index])
                / (node_list[column] - node_list[factor_index])
            )
    return result


def lagrange_slope(node_list, column, position):
    total = 0.0
    for skipped in range(4):
        if skipped == column:
            continue
        term = 1.0 / (node_list[column] - node_list[skipped])
        for factor_index in range(4):
            if factor_index != column and factor_index != skipped:
                term = (
                    term
                    * (position - node_list[factor_index])
                    / (node_list[column] - node_list[factor_index])
                )
        total = total + term
    return total


def basis_tables():
    node_list = gauss_nodes()
    derivs = [
        [lagrange_slope(node_list, column, node_list[source]) for column in range(4)]
        for source in range(4)
    ]
    left_vals = [lagrange_value(node_list, column, -1.0) for column in range(4)]
    right_vals = [lagrange_value(node_list, column, 1.0) for column in range(4)]
    third_slope = [(15.0 * value * value - 3.0) / 2.0 for value in node_list]
    fourth_slope = [(35.0 * value**3 - 15.0 * value) / 2.0 for value in node_list]
    left_corr = [-0.5 * (third_slope[source] - fourth_slope[source]) for source in range(4)]
    right_corr = [0.5 * (third_slope[source] + fourth_slope[source]) for source in range(4)]
    return (derivs, left_vals, right_vals, left_corr, right_corr)


def apply_points(adj_field, matrix, point_dim):
    slab_list = [
        lax.index_in_dim(adj_field, source, point_dim, keepdims=False) for source in range(4)
    ]
    outputs = []
    for target in range(4):
        running = slab_list[0] * float(matrix[0][target])
        for source in range(1, 4):
            running = running + slab_list[source] * float(matrix[source][target])
        outputs.append(running)
    return jnp.stack(outputs, axis=point_dim)


def face_moment(adj_field, vector, point_dim):
    running = lax.index_in_dim(adj_field, 0, point_dim, keepdims=False) * float(vector[0])
    for source in range(1, 4):
        running = running + lax.index_in_dim(adj_field, source, point_dim, keepdims=False) * float(
            vector[source]
        )
    return running


def lift_face(face_vals, vector, point_dim):
    return jnp.stack([face_vals * float(vector[target]) for target in range(4)], axis=point_dim)


def conserved(primitive):
    density = primitive[0]
    velocity = primitive[1:4]
    pressure = primitive[4]
    energy = pressure / (GAMMA - 1.0) + 0.5 * density * jnp.sum(velocity * velocity, axis=0)
    return jnp.concatenate([density[None], density[None] * velocity, energy[None]], axis=0)


def euler_flux(cons_state, direction):
    density = cons_state[0]
    momentum = cons_state[1:4]
    energy = cons_state[4]
    velocity = momentum / density[None]
    pressure = (GAMMA - 1.0) * (energy - 0.5 * jnp.sum(momentum * velocity, axis=0))
    normal_speed = velocity[direction]
    columns = [momentum[direction]]
    for component in range(3):
        if component == direction:
            columns.append(momentum[component] * normal_speed + pressure)
        else:
            columns.append(momentum[component] * normal_speed)
    columns.append((energy + pressure) * normal_speed)
    return jnp.stack(columns, axis=0)


def transpose_flux(cons_state, cotangent, direction):
    unused, pullback = jax.vjp(lambda current: euler_flux(current, direction), cons_state)
    return pullback(cotangent)[0]


def section_rate(adj_field, cons_state, left_moments, right_moments, next_left, prev_right):
    derivs, left_vals, right_vals, left_corr, right_corr = basis_tables()
    rate_sum = jnp.zeros_like(adj_field)
    for direction in range(3):
        point_dim = 1 + direction
        bracket = apply_points(adj_field, derivs, point_dim)
        bracket = bracket + 0.5 * lift_face(
            next_left[direction] - right_moments[direction], right_vals, point_dim
        )
        bracket = bracket + 0.5 * lift_face(
            prev_right[direction] - left_moments[direction], left_vals, point_dim
        )
        rate_sum = rate_sum - METRIC * transpose_flux(cons_state, bracket, direction)
    return rate_sum


def all_moments(adj_field):
    derivs, left_vals, right_vals, left_corr, right_corr = basis_tables()
    left_moments = [face_moment(adj_field, left_corr, 1 + direction) for direction in range(3)]
    right_moments = [face_moment(adj_field, right_corr, 1 + direction) for direction in range(3)]
    return (left_moments, right_moments)


def faces_to_rows(face_vals):
    axial_elems = face_vals.shape[3]
    azim_elems = face_vals.shape[4]
    return face_vals.transpose(0, 3, 1, 4, 2).reshape(5, 4 * axial_elems, 4 * azim_elems)


def rows_to_face(rows_vals, axial_elems, azim_elems):
    return rows_vals.reshape(5, axial_elems, 4, azim_elems, 4).transpose(0, 2, 4, 1, 3)


def shift_sum(window, coefs, lo):
    total = None
    for offset, coef in coefs:
        term = coef[None] * window[:, :, lo + offset : lo + offset + TP]
        total = term if total is None else total + term
    return total


def lane_roll(value, shift):
    return pltpu.roll(value, shift % 128, value.ndim - 1)


def sweep(field, weights, pick):
    total = field[pick(0)] * float(weights[0])
    for source in range(1, 4):
        total = total + field[pick(source)] * float(weights[source])
    return total


def column(values, shape):
    rows = lax.broadcasted_iota(jnp.int32, shape, 2)
    out = jnp.full(shape, float(values[3]), jnp.float32)
    for index in range(3):
        out = jnp.where(rows == index, float(values[index]), out)
    return out


def rate_kernel(
    adj_ref, flow_ref, up_ax_ref, down_ax_ref, up_az_ref, down_az_ref, outer_ref, inner_ref,
    rate_ref, next_ref,
):
    derivs, left_vals, right_vals, left_corr, right_corr = basis_tables()
    shape = (4, 4, 4, 128)
    lane = lax.broadcasted_iota(jnp.int32, shape, 3)
    flat_lane = lax.broadcasted_iota(jnp.int32, (4, 4, 128), 2)
    az_flat = flat_lane // ER % ET
    radial_lane = lane % ER
    brackets = [[None] * 5 for _ in range(3)]
    for chan in range(5):
        field = adj_ref[0, chan]
        left0 = sweep(field, left_corr, lambda i: (i,))
        right0 = sweep(field, right_corr, lambda i: (i,))
        next0 = lane_roll(jnp.where(flat_lane < ET * ER, up_ax_ref[chan], left0), -ET * ER)
        prev0 = lane_roll(jnp.where(flat_lane >= (EA - 1) * ET * ER, down_ax_ref[chan], right0), ET * ER)
        jump_r = 0.5 * (next0 - right0)
        jump_l = 0.5 * (prev0 - left0)
        slabs = []
        for target in range(4):
            slab = sweep(field, [derivs[i][target] for i in range(4)], lambda i: (i,))
            slabs.append(slab + jump_r * float(right_vals[target]) + jump_l * float(left_vals[target]))
        brackets[0][chan] = jnp.stack(slabs, axis=0)
        pick1 = lambda i: (slice(None), i)
        left1 = sweep(field, left_corr, pick1)
        right1 = sweep(field, right_corr, pick1)
        next1 = lane_roll(
            jnp.where(az_flat == 0, lane_roll(up_az_ref[chan], ET * ER), left1), -ER
        )
        prev1 = lane_roll(
            jnp.where(az_flat == ET - 1, lane_roll(down_az_ref[chan], -ET * ER), right1), ER
        )
        jump_r = 0.5 * (next1 - right1)
        jump_l = 0.5 * (prev1 - left1)
        slabs = []
        for target in range(4):
            slab = sweep(field, [derivs[i][target] for i in range(4)], pick1)
            slabs.append(slab + jump_r * float(right_vals[target]) + jump_l * float(left_vals[target]))
        brackets[1][chan] = jnp.stack(slabs, axis=1)
        points = [jnp.broadcast_to(field[:, :, i : i + 1, :], shape) for i in range(4)]
        left2 = sweep(points, left_corr, lambda i: i)
        right2 = sweep(points, right_corr, lambda i: i)
        next2 = jnp.where(radial_lane == ER - 1, outer_ref[chan], lane_roll(left2, -1))
        prev2 = jnp.where(radial_lane == 0, inner_ref[chan], lane_roll(right2, 1))
        bracket = 0.5 * (next2 - right2) * column(right_vals, shape)
        bracket = bracket + 0.5 * (prev2 - left2) * column(left_vals, shape)
        for source in range(4):
            bracket = bracket + points[source] * column(derivs[source], shape)
        brackets[2][chan] = bracket
    prim = [flow_ref[0, chan].astype(jnp.float32) for chan in range(5)]
    density = prim[0]
    speed_sq = prim[1] * prim[1] + prim[2] * prim[2] + prim[3] * prim[3]
    energy = prim[4] / (GAMMA - 1.0) + 0.5 * density * speed_sq
    momentum = [density * prim[1 + k] for k in range(3)]
    velocity = [momentum[k] / density for k in range(3)]
    kinetic = momentum[0] * velocity[0] + momentum[1] * velocity[1] + momentum[2] * velocity[2]
    pressure = (GAMMA - 1.0) * (energy - 0.5 * kinetic)
    enthalpy = (energy + pressure) / density
    vel_sq = velocity[0] * velocity[0] + velocity[1] * velocity[1] + velocity[2] * velocity[2]
    grad = [None] * 5
    for direction in range(3):
        cot = brackets[direction]
        normal = velocity[direction]
        dotted = cot[1] * velocity[0] + cot[2] * velocity[1] + cot[3] * velocity[2] + cot[4] * enthalpy
        weight = cot[1 + direction] + cot[4] * normal
        terms = [
            0.5 * (GAMMA - 1.0) * vel_sq * weight - dotted * normal,
            None,
            None,
            None,
            (GAMMA - 1.0) * weight + cot[4] * normal,
        ]
        for k in range(3):
            term = cot[1 + k] * normal - (GAMMA - 1.0) * weight * velocity[k]
            if k == direction:
                term = term + (cot[0] + dotted)
            terms[1 + k] = term
        for chan in range(5):
            grad[chan] = terms[chan] if grad[chan] is None else grad[chan] + terms[chan]
    for chan in range(5):
        rate = -METRIC * grad[chan]
        rate_ref[0, chan] = rate
        next_ref[0, chan] = adj_ref[0, chan] + SECTION_STEP * rate


def local(adjoint, flow_prim, intersection_shift, weight_index, mortar_weights, sector_offset):
    n_axial = lax.axis_size("axial")
    n_azim = lax.axis_size("azim")
    adj_field = adjoint[0]
    derivs, left_vals, right_vals, left_corr, right_corr = basis_tables()
    left_ax = face_moment(adj_field, left_corr, 1)
    right_ax = face_moment(adj_field, right_corr, 1)
    left_az = face_moment(adj_field, left_corr, 2)
    right_az = face_moment(adj_field, right_corr, 2)
    is_rotor = lax.axis_index("zone") == 0
    up_ax = lax.ppermute(left_ax, "axial", [(i + 1, i) for i in range(n_axial - 1)])
    down_ax = lax.ppermute(right_ax, "axial", [(i, i + 1) for i in range(n_axial - 1)])
    face_shape = (5, 4, 4, EA, ET, ER)
    outer_moment = face_moment(adj_field, right_corr, 3).reshape(face_shape)[..., ER - 1]
    inner_moment = face_moment(adj_field, left_corr, 3).reshape(face_shape)[..., 0]
    own_rows = faces_to_rows(jnp.where(is_rotor, outer_moment, inner_moment))
    shifts_local = intersection_shift.reshape(INTERSECTIONS, AP, TP)
    table_match = weight_index[:, :, None] == jnp.arange(NW, dtype=jnp.int32)[None, None, :]
    weights_local = jnp.sum(
        jnp.where(table_match, mortar_weights[None, None, :], 0.0), axis=2
    ).reshape(INTERSECTIONS, AP, TP)
    offset = sector_offset[0]
    turn = (offset + TP // 2) // TP
    residue = offset - turn * TP
    offsets_k = residue + shifts_local
    coefs = []
    for rel in range(-TP, TP - 1):
        coef = jnp.where(offsets_k[0] == rel, weights_local[0], 0.0)
        for member in range(1, INTERSECTIONS):
            coef = coef + jnp.where(offsets_k[member] == rel, weights_local[member], 0.0)
        coefs.append((rel, coef))
    contrib = None
    for rel, coef in coefs:
        term = jnp.pad(coef[None] * own_rows, ((0, 0), (0, 0), (TP + rel, TP - rel)))
        contrib = term if contrib is None else contrib + term
    zone = lax.axis_index("zone")
    azim = lax.axis_index("azim")
    dest = jnp.arange(2 * n_azim, dtype=jnp.int32)
    dest_azim = dest % n_azim
    gap = ((dest_azim - azim) % n_azim - turn) % n_azim
    gap = gap[:, None, None, None]
    pieces = jnp.where(
        gap == n_azim - 1,
        contrib[None, :, :, :TP],
        jnp.where(gap == 0, contrib[None, :, :, TP : 2 * TP], contrib[None, :, :, 2 * TP :]),
    )
    iface_out = jnp.where(is_rotor, jnp.broadcast_to(own_rows[None], pieces.shape), pieces)
    iface_out = jnp.pad(iface_out.reshape(2 * n_azim, 5, 2, 128), ((0, 0), (0, 0), (0, 2), (0, 0)))
    split = (5, 4, 4, EA, ET, ER)
    upper_face = left_az.reshape(split)[:, :, :, :, 0, :].reshape(5, 4, 128)
    lower_face = right_az.reshape(split)[:, :, :, :, ET - 1, :].reshape(5, 4, 128)
    same_zone = dest // n_azim == zone
    to_prev = (same_zone & (dest_azim == (azim - 1) % n_azim))[:, None, None, None]
    to_next = (same_zone & (dest_azim == (azim + 1) % n_azim))[:, None, None, None]
    chunks = jnp.where(
        to_prev, upper_face[None], jnp.where(to_next, lower_face[None], jnp.where(same_zone[:, None, None, None], 0.0, iface_out))
    )
    got = lax.all_to_all(chunks, ("zone", "azim"), 0, 0)
    base = (1 - zone) * n_azim
    up_compact = lax.dynamic_index_in_dim(got, zone * n_azim + (azim + 1) % n_azim, 0, keepdims=False)
    down_compact = lax.dynamic_index_in_dim(got, zone * n_azim + (azim - 1) % n_azim, 0, keepdims=False)
    up_az = jnp.pad(
        up_compact.reshape(5, 4, 4, EA, 1, ER), ((0, 0),) * 4 + ((0, ET - 1), (0, 0))
    ).reshape(5, 4, 4, EA * ET * ER)
    down_az = jnp.pad(
        down_compact.reshape(5, 4, 4, EA, 1, ER), ((0, 0),) * 4 + ((ET - 1, 0), (0, 0))
    ).reshape(5, 4, 4, EA * ET * ER)
    direction = jnp.where(is_rotor, -1, 1)
    picked = [
        lax.dynamic_index_in_dim(
            got, base + (azim + direction * (turn + step)) % n_azim, 0, keepdims=False
        )[:, :2].reshape(5, AP, TP)
        for step in (-1, 0, 1)
    ]
    returned = picked[0] + picked[1] + picked[2]
    window = jnp.concatenate(picked, axis=2)
    incoming = shift_sum(window, coefs, TP)
    iface = rows_to_face(jnp.where(is_rotor, returned, incoming), EA, ET)
    iface = jnp.broadcast_to(
        iface[:, :, :, None, :, :, None], (5, 4, 4, 4, EA, ET, ER)
    ).reshape(5, 4, 4, 4, EA * ET * ER)
    outer = jnp.where(is_rotor, iface, 0.0)
    inner = jnp.where(is_rotor, 0.0, iface)
    field_shape = jax.ShapeDtypeStruct(adjoint.shape, jnp.float32)
    adjoint_rate, next_adjoint = pl.pallas_call(
        rate_kernel, out_shape=(field_shape, field_shape)
    )(adjoint, flow_prim, up_ax, down_ax, up_az, down_az, outer, inner)
    return (adjoint_rate, next_adjoint)


def solution(mesh):
    placed = (
        P("zone", None, None, None, None, ("axial", "azim")),
        P("zone", None, None, None, None, ("axial", "azim")),
        P(None, ("axial", "azim")),
        P(None, ("axial", "azim")),
        P(),
        P(),
    )
    return jax.shard_map(
        local,
        mesh=mesh,
        in_specs=placed,
        out_specs=(
            P("zone", None, None, None, None, ("axial", "azim")),
            P("zone", None, None, None, None, ("axial", "azim")),
        ),
        check_vma=False,
    )
```

```python
import math

import jax
import jax.numpy as jnp
from jax import lax
from jax.experimental import pallas as pl
from jax.experimental.pallas import tpu as pltpu
from jax.sharding import PartitionSpec as P

EA = 4
ET = 4
ER = 8
INTERSECTIONS = 4
NW = 128
AP = 16
TP = 16


GAMMA = 1.4
METRIC = 0.1
SECTION_STEP = 0.5


def gauss_nodes():
    root_term = math.sqrt(6.0 / 5.0)
    inner_node = math.sqrt(3.0 / 7.0 - 2.0 / 7.0 * root_term)
    outer_node = math.sqrt(3.0 / 7.0 + 2.0 / 7.0 * root_term)
    return [-outer_node, -inner_node, inner_node, outer_node]


def lagrange_value(node_list, column, position):
    result = 1.0
    for factor_index in range(4):
        if factor_index != column:
            result = (
                result
                * (position - node_list[factor_index])
                / (node_list[column] - node_list[factor_index])
            )
    return result


def lagrange_slope(node_list, column, position):
    total = 0.0
    for skipped in range(4):
        if skipped == column:
            continue
        term = 1.0 / (node_list[column] - node_list[skipped])
        for factor_index in range(4):
            if factor_index != column and factor_index != skipped:
                term = (
                    term
                    * (position - node_list[factor_index])
                    / (node_list[column] - node_list[factor_index])
                )
        total = total + term
    return total


def basis_tables():
    node_list = gauss_nodes()
    derivs = [
        [lagrange_slope(node_list, column, node_list[source]) for column in range(4)]
        for source in range(4)
    ]
    left_vals = [lagrange_value(node_list, column, -1.0) for column in range(4)]
    right_vals = [lagrange_value(node_list, column, 1.0) for column in range(4)]
    third_slope = [(15.0 * value * value - 3.0) / 2.0 for value in node_list]
    fourth_slope = [(35.0 * value**3 - 15.0 * value) / 2.0 for value in node_list]
    left_corr = [-0.5 * (third_slope[source] - fourth_slope[source]) for source in range(4)]
    right_corr = [0.5 * (third_slope[source] + fourth_slope[source]) for source in range(4)]
    return (derivs, left_vals, right_vals, left_corr, right_corr)


def apply_points(adj_field, matrix, point_dim):
    slab_list = [
        lax.index_in_dim(adj_field, source, point_dim, keepdims=False) for source in range(4)
    ]
    outputs = []
    for target in range(4):
        running = slab_list[0] * float(matrix[0][target])
        for source in range(1, 4):
            running = running + slab_list[source] * float(matrix[source][target])
        outputs.append(running)
    return jnp.stack(outputs, axis=point_dim)


def face_moment(adj_field, vector, point_dim):
    running = lax.index_in_dim(adj_field, 0, point_dim, keepdims=False) * float(vector[0])
    for source in range(1, 4):
        running = running + lax.index_in_dim(adj_field, source, point_dim, keepdims=False) * float(
            vector[source]
        )
    return running


def lift_face(face_vals, vector, point_dim):
    return jnp.stack([face_vals * float(vector[target]) for target in range(4)], axis=point_dim)


def conserved(primitive):
    density = primitive[0]
    velocity = primitive[1:4]
    pressure = primitive[4]
    energy = pressure / (GAMMA - 1.0) + 0.5 * density * jnp.sum(velocity * velocity, axis=0)
    return jnp.concatenate([density[None], density[None] * velocity, energy[None]], axis=0)


def euler_flux(cons_state, direction):
    density = cons_state[0]
    momentum = cons_state[1:4]
    energy = cons_state[4]
    velocity = momentum / density[None]
    pressure = (GAMMA - 1.0) * (energy - 0.5 * jnp.sum(momentum * velocity, axis=0))
    normal_speed = velocity[direction]
    columns = [momentum[direction]]
    for component in range(3):
        if component == direction:
            columns.append(momentum[component] * normal_speed + pressure)
        else:
            columns.append(momentum[component] * normal_speed)
    columns.append((energy + pressure) * normal_speed)
    return jnp.stack(columns, axis=0)


def transpose_flux(cons_state, cotangent, direction):
    unused, pullback = jax.vjp(lambda current: euler_flux(current, direction), cons_state)
    return pullback(cotangent)[0]


def section_rate(adj_field, cons_state, left_moments, right_moments, next_left, prev_right):
    derivs, left_vals, right_vals, left_corr, right_corr = basis_tables()
    rate_sum = jnp.zeros_like(adj_field)
    for direction in range(3):
        point_dim = 1 + direction
        bracket = apply_points(adj_field, derivs, point_dim)
        bracket = bracket + 0.5 * lift_face(
            next_left[direction] - right_moments[direction], right_vals, point_dim
        )
        bracket = bracket + 0.5 * lift_face(
            prev_right[direction] - left_moments[direction], left_vals, point_dim
        )
        rate_sum = rate_sum - METRIC * transpose_flux(cons_state, bracket, direction)
    return rate_sum


def all_moments(adj_field):
    derivs, left_vals, right_vals, left_corr, right_corr = basis_tables()
    left_moments = [face_moment(adj_field, left_corr, 1 + direction) for direction in range(3)]
    right_moments = [face_moment(adj_field, right_corr, 1 + direction) for direction in range(3)]
    return (left_moments, right_moments)


def faces_to_rows(face_vals):
    axial_elems = face_vals.shape[3]
    azim_elems = face_vals.shape[4]
    return face_vals.transpose(0, 3, 1, 4, 2).reshape(5, 4 * axial_elems, 4 * azim_elems)


def rows_to_face(rows_vals, axial_elems, azim_elems):
    return rows_vals.reshape(5, axial_elems, 4, azim_elems, 4).transpose(0, 2, 4, 1, 3)


def shift_sum(window, coefs, lo):
    total = None
    for offset, coef in coefs:
        term = coef[None] * window[:, :, lo + offset : lo + offset + TP]
        total = term if total is None else total + term
    return total


def lane_roll(value, shift):
    return pltpu.roll(value, shift % 128, value.ndim - 1)


def sweep(field, weights, pick):
    total = field[pick(0)] * float(weights[0])
    for source in range(1, 4):
        total = total + field[pick(source)] * float(weights[source])
    return total


def column(values, shape):
    rows = lax.broadcasted_iota(jnp.int32, shape, 2)
    out = jnp.full(shape, float(values[3]), jnp.float32)
    for index in range(3):
        out = jnp.where(rows == index, float(values[index]), out)
    return out


def compact_face(face, part):
    lane = lax.broadcasted_iota(jnp.int32, (4, 128), 1)
    out = jnp.zeros((4, 128), jnp.float32)
    for block in range(4):
        for group in range(EA):
            shift = block * ET * ER - group * (ET - 1) * ER - part * ER
            start = block * ET * ER + group * ER
            mask = (lane >= start) & (lane < start + ER)
            out = jnp.where(mask, lane_roll(face[block], shift), out)
    return out


def expand_face(chunk, part):
    lane = lax.broadcasted_iota(jnp.int32, (4, 128), 1)
    group_of = lane // (ET * ER)
    in_part = lane // ER % ET == part
    blocks = []
    for block in range(4):
        out = jnp.zeros((4, 128), jnp.float32)
        for group in range(EA):
            shift = block * ET * ER - group * (ET - 1) * ER - part * ER
            out = jnp.where(in_part & (group_of == group), lane_roll(chunk, -shift), out)
        blocks.append(out)
    return jnp.stack(blocks, axis=0)


def moment_kernel(adj_ref, left_ax_ref, right_ax_ref, up_ref, down_ref, outer_ref, inner_ref):
    derivs, left_vals, right_vals, left_corr, right_corr = basis_tables()
    for chan in range(5):
        field = adj_ref[0, chan]
        left_ax_ref[chan] = sweep(field, left_corr, lambda i: (i,))
        right_ax_ref[chan] = sweep(field, right_corr, lambda i: (i,))
        pick1 = lambda i: (slice(None), i)
        up_ref[chan] = compact_face(sweep(field, left_corr, pick1), 0)
        down_ref[chan] = compact_face(sweep(field, right_corr, pick1), ET - 1)
        pick2 = lambda i: (slice(None), slice(None), slice(i, i + 1))
        outer = sweep(field, right_corr, pick2)
        inner = sweep(field, left_corr, pick2)
        for axial in range(4):
            for azim in range(4):
                outer_ref[chan, axial, azim : azim + 1] = outer[axial, azim]
                inner_ref[chan, axial, azim : azim + 1] = inner[axial, azim]


def rate_kernel(
    adj_ref, flow_ref, up_ax_ref, down_ax_ref, up_az_ref, down_az_ref, iface_ref, flag_ref,
    rate_ref, next_ref,
):
    derivs, left_vals, right_vals, left_corr, right_corr = basis_tables()
    shape = (4, 4, 4, 128)
    lane = lax.broadcasted_iota(jnp.int32, shape, 3)
    flat_lane = lax.broadcasted_iota(jnp.int32, (4, 4, 128), 2)
    az_flat = flat_lane // ER % ET
    radial_lane = lane % ER
    brackets = [[None] * 5 for _ in range(3)]
    rotor = jnp.broadcast_to(flag_ref[0:1, :], shape) > 0.5
    for chan in range(5):
        field = adj_ref[0, chan]
        face = jnp.stack(
            [
                jnp.stack(
                    [jnp.broadcast_to(iface_ref[chan, axial, azim : azim + 1], (4, 128)) for azim in range(4)],
                    axis=0,
                )
                for axial in range(4)
            ],
            axis=0,
        )
        outer_face = jnp.where(rotor, face, 0.0)
        inner_face = jnp.where(rotor, 0.0, face)
        up_az = expand_face(up_az_ref[chan], 0)
        down_az = expand_face(down_az_ref[chan], ET - 1)
        left0 = sweep(field, left_corr, lambda i: (i,))
        right0 = sweep(field, right_corr, lambda i: (i,))
        next0 = lane_roll(jnp.where(flat_lane < ET * ER, up_ax_ref[chan], left0), -ET * ER)
        prev0 = lane_roll(jnp.where(flat_lane >= (EA - 1) * ET * ER, down_ax_ref[chan], right0), ET * ER)
        jump_r = 0.5 * (next0 - right0)
        jump_l = 0.5 * (prev0 - left0)
        slabs = []
        for target in range(4):
            slab = sweep(field, [derivs[i][target] for i in range(4)], lambda i: (i,))
            slabs.append(slab + jump_r * float(right_vals[target]) + jump_l * float(left_vals[target]))
        brackets[0][chan] = jnp.stack(slabs, axis=0)
        pick1 = lambda i: (slice(None), i)
        left1 = sweep(field, left_corr, pick1)
        right1 = sweep(field, right_corr, pick1)
        next1 = lane_roll(
            jnp.where(az_flat == 0, lane_roll(up_az, ET * ER), left1), -ER
        )
        prev1 = lane_roll(
            jnp.where(az_flat == ET - 1, lane_roll(down_az, -ET * ER), right1), ER
        )
        jump_r = 0.5 * (next1 - right1)
        jump_l = 0.5 * (prev1 - left1)
        slabs = []
        for target in range(4):
            slab = sweep(field, [derivs[i][target] for i in range(4)], pick1)
            slabs.append(slab + jump_r * float(right_vals[target]) + jump_l * float(left_vals[target]))
        brackets[1][chan] = jnp.stack(slabs, axis=1)
        points = [jnp.broadcast_to(field[:, :, i : i + 1, :], shape) for i in range(4)]
        left2 = sweep(points, left_corr, lambda i: i)
        right2 = sweep(points, right_corr, lambda i: i)
        next2 = jnp.where(radial_lane == ER - 1, outer_face, lane_roll(left2, -1))
        prev2 = jnp.where(radial_lane == 0, inner_face, lane_roll(right2, 1))
        bracket = 0.5 * (next2 - right2) * column(right_vals, shape)
        bracket = bracket + 0.5 * (prev2 - left2) * column(left_vals, shape)
        for source in range(4):
            bracket = bracket + points[source] * column(derivs[source], shape)
        brackets[2][chan] = bracket
    prim = [flow_ref[0, chan].astype(jnp.float32) for chan in range(5)]
    density = prim[0]
    speed_sq = prim[1] * prim[1] + prim[2] * prim[2] + prim[3] * prim[3]
    energy = prim[4] / (GAMMA - 1.0) + 0.5 * density * speed_sq
    momentum = [density * prim[1 + k] for k in range(3)]
    velocity = [momentum[k] / density for k in range(3)]
    kinetic = momentum[0] * velocity[0] + momentum[1] * velocity[1] + momentum[2] * velocity[2]
    pressure = (GAMMA - 1.0) * (energy - 0.5 * kinetic)
    enthalpy = (energy + pressure) / density
    vel_sq = velocity[0] * velocity[0] + velocity[1] * velocity[1] + velocity[2] * velocity[2]
    grad = [None] * 5
    for direction in range(3):
        cot = brackets[direction]
        normal = velocity[direction]
        dotted = cot[1] * velocity[0] + cot[2] * velocity[1] + cot[3] * velocity[2] + cot[4] * enthalpy
        weight = cot[1 + direction] + cot[4] * normal
        terms = [
            0.5 * (GAMMA - 1.0) * vel_sq * weight - dotted * normal,
            None,
            None,
            None,
            (GAMMA - 1.0) * weight + cot[4] * normal,
        ]
        for k in range(3):
            term = cot[1 + k] * normal - (GAMMA - 1.0) * weight * velocity[k]
            if k == direction:
                term = term + (cot[0] + dotted)
            terms[1 + k] = term
        for chan in range(5):
            grad[chan] = terms[chan] if grad[chan] is None else grad[chan] + terms[chan]
    for chan in range(5):
        rate = -METRIC * grad[chan]
        rate_ref[0, chan] = rate
        next_ref[0, chan] = adj_ref[0, chan] + SECTION_STEP * rate


def local(adjoint, flow_prim, intersection_shift, weight_index, mortar_weights, sector_offset):
    n_axial = lax.axis_size("axial")
    n_azim = lax.axis_size("azim")
    face4 = jax.ShapeDtypeStruct((5, 4, 4, 128), jnp.float32)
    chunk = jax.ShapeDtypeStruct((5, 4, 128), jnp.float32)
    left_ax, right_ax, upper_face, lower_face, outer_moment, inner_moment = pl.pallas_call(
        moment_kernel, out_shape=(face4, face4, chunk, chunk, face4, face4)
    )(adjoint)
    is_rotor = lax.axis_index("zone") == 0
    up_ax = lax.ppermute(left_ax, "axial", [(i + 1, i) for i in range(n_axial - 1)])
    down_ax = lax.ppermute(right_ax, "axial", [(i, i + 1) for i in range(n_axial - 1)])
    face_shape = (5, 4, 4, EA, ET, ER)
    own_face = jnp.where(
        is_rotor, outer_moment.reshape(face_shape)[..., ER - 1], inner_moment.reshape(face_shape)[..., 0]
    )
    own_rows = faces_to_rows(own_face)
    shifts_local = intersection_shift.reshape(INTERSECTIONS, AP, TP)
    table_match = weight_index[:, :, None] == jnp.arange(NW, dtype=jnp.int32)[None, None, :]
    weights_local = jnp.sum(
        jnp.where(table_match, mortar_weights[None, None, :], 0.0), axis=2
    ).reshape(INTERSECTIONS, AP, TP)
    offset = sector_offset[0]
    turn = (offset + TP // 2) // TP
    residue = offset - turn * TP
    offsets_k = residue + shifts_local
    coefs = []
    for rel in range(-TP, TP - 1):
        coef = jnp.where(offsets_k[0] == rel, weights_local[0], 0.0)
        for member in range(1, INTERSECTIONS):
            coef = coef + jnp.where(offsets_k[member] == rel, weights_local[member], 0.0)
        coefs.append((rel, coef))
    contrib = None
    for rel, coef in coefs:
        term = jnp.pad(coef[None] * own_rows, ((0, 0), (0, 0), (TP + rel, TP - rel)))
        contrib = term if contrib is None else contrib + term
    zone = lax.axis_index("zone")
    azim = lax.axis_index("azim")
    dest = jnp.arange(2 * n_azim, dtype=jnp.int32)
    dest_azim = dest % n_azim
    gap = ((dest_azim - azim) % n_azim - turn) % n_azim
    gap = gap[:, None, None, None]
    pieces = jnp.where(
        gap == n_azim - 1,
        contrib[None, :, :, :TP],
        jnp.where(gap == 0, contrib[None, :, :, TP : 2 * TP], contrib[None, :, :, 2 * TP :]),
    )
    iface_out = jnp.where(is_rotor, jnp.broadcast_to(own_rows[None], pieces.shape), pieces)
    iface_out = jnp.pad(iface_out.reshape(2 * n_azim, 5, 2, 128), ((0, 0), (0, 0), (0, 2), (0, 0)))
    same_zone = dest // n_azim == zone
    to_prev = (same_zone & (dest_azim == (azim - 1) % n_azim))[:, None, None, None]
    to_next = (same_zone & (dest_azim == (azim + 1) % n_azim))[:, None, None, None]
    chunks = jnp.where(
        to_prev, upper_face[None], jnp.where(to_next, lower_face[None], jnp.where(same_zone[:, None, None, None], 0.0, iface_out))
    )
    got = lax.all_to_all(chunks, ("zone", "azim"), 0, 0)
    base = (1 - zone) * n_azim
    up_az = lax.dynamic_index_in_dim(got, zone * n_azim + (azim + 1) % n_azim, 0, keepdims=False)
    down_az = lax.dynamic_index_in_dim(got, zone * n_azim + (azim - 1) % n_azim, 0, keepdims=False)
    direction = jnp.where(is_rotor, -1, 1)
    picked = [
        lax.dynamic_index_in_dim(
            got, base + (azim + direction * (turn + step)) % n_azim, 0, keepdims=False
        )[:, :2].reshape(5, AP, TP)
        for step in (-1, 0, 1)
    ]
    returned = picked[0] + picked[1] + picked[2]
    window = jnp.concatenate(picked, axis=2)
    incoming = shift_sum(window, coefs, TP)
    iface = rows_to_face(jnp.where(is_rotor, returned, incoming), EA, ET)
    iface = jnp.broadcast_to(iface[..., None], (5, 4, 4, EA, ET, ER)).reshape(5, 4, 4, EA * ET * ER)
    flag = jnp.broadcast_to(jnp.where(is_rotor, 1.0, 0.0), (8, 128))
    field_shape = jax.ShapeDtypeStruct(adjoint.shape, jnp.float32)
    adjoint_rate, next_adjoint = pl.pallas_call(
        rate_kernel, out_shape=(field_shape, field_shape)
    )(adjoint, flow_prim, up_ax, down_ax, up_az, down_az, iface, flag)
    return (adjoint_rate, next_adjoint)


def solution(mesh):
    placed = (
        P("zone", None, None, None, None, ("axial", "azim")),
        P("zone", None, None, None, None, ("axial", "azim")),
        P(None, ("axial", "azim")),
        P(None, ("axial", "azim")),
        P(),
        P(),
    )
    return jax.shard_map(
        local,
        mesh=mesh,
        in_specs=placed,
        out_specs=(
            P("zone", None, None, None, None, ("axial", "azim")),
            P("zone", None, None, None, None, ("axial", "azim")),
        ),
        check_vma=False,
    )
```

```python
import math

import jax
import jax.numpy as jnp
from jax import lax
from jax.experimental import pallas as pl
from jax.experimental.pallas import tpu as pltpu
from jax.sharding import PartitionSpec as P

EA = 4
ET = 4
ER = 8
INTERSECTIONS = 4
NW = 128
AP = 16
TP = 16


GAMMA = 1.4
METRIC = 0.1
SECTION_STEP = 0.5


def gauss_nodes():
    root_term = math.sqrt(6.0 / 5.0)
    inner_node = math.sqrt(3.0 / 7.0 - 2.0 / 7.0 * root_term)
    outer_node = math.sqrt(3.0 / 7.0 + 2.0 / 7.0 * root_term)
    return [-outer_node, -inner_node, inner_node, outer_node]


def lagrange_value(node_list, column, position):
    result = 1.0
    for factor_index in range(4):
        if factor_index != column:
            result = (
                result
                * (position - node_list[factor_index])
                / (node_list[column] - node_list[factor_index])
            )
    return result


def lagrange_slope(node_list, column, position):
    total = 0.0
    for skipped in range(4):
        if skipped == column:
            continue
        term = 1.0 / (node_list[column] - node_list[skipped])
        for factor_index in range(4):
            if factor_index != column and factor_index != skipped:
                term = (
                    term
                    * (position - node_list[factor_index])
                    / (node_list[column] - node_list[factor_index])
                )
        total = total + term
    return total


def basis_tables():
    node_list = gauss_nodes()
    derivs = [
        [lagrange_slope(node_list, column, node_list[source]) for column in range(4)]
        for source in range(4)
    ]
    left_vals = [lagrange_value(node_list, column, -1.0) for column in range(4)]
    right_vals = [lagrange_value(node_list, column, 1.0) for column in range(4)]
    third_slope = [(15.0 * value * value - 3.0) / 2.0 for value in node_list]
    fourth_slope = [(35.0 * value**3 - 15.0 * value) / 2.0 for value in node_list]
    left_corr = [-0.5 * (third_slope[source] - fourth_slope[source]) for source in range(4)]
    right_corr = [0.5 * (third_slope[source] + fourth_slope[source]) for source in range(4)]
    return (derivs, left_vals, right_vals, left_corr, right_corr)


def apply_points(adj_field, matrix, point_dim):
    slab_list = [
        lax.index_in_dim(adj_field, source, point_dim, keepdims=False) for source in range(4)
    ]
    outputs = []
    for target in range(4):
        running = slab_list[0] * float(matrix[0][target])
        for source in range(1, 4):
            running = running + slab_list[source] * float(matrix[source][target])
        outputs.append(running)
    return jnp.stack(outputs, axis=point_dim)


def face_moment(adj_field, vector, point_dim):
    running = lax.index_in_dim(adj_field, 0, point_dim, keepdims=False) * float(vector[0])
    for source in range(1, 4):
        running = running + lax.index_in_dim(adj_field, source, point_dim, keepdims=False) * float(
            vector[source]
        )
    return running


def lift_face(face_vals, vector, point_dim):
    return jnp.stack([face_vals * float(vector[target]) for target in range(4)], axis=point_dim)


def conserved(primitive):
    density = primitive[0]
    velocity = primitive[1:4]
    pressure = primitive[4]
    energy = pressure / (GAMMA - 1.0) + 0.5 * density * jnp.sum(velocity * velocity, axis=0)
    return jnp.concatenate([density[None], density[None] * velocity, energy[None]], axis=0)


def euler_flux(cons_state, direction):
    density = cons_state[0]
    momentum = cons_state[1:4]
    energy = cons_state[4]
    velocity = momentum / density[None]
    pressure = (GAMMA - 1.0) * (energy - 0.5 * jnp.sum(momentum * velocity, axis=0))
    normal_speed = velocity[direction]
    columns = [momentum[direction]]
    for component in range(3):
        if component == direction:
            columns.append(momentum[component] * normal_speed + pressure)
        else:
            columns.append(momentum[component] * normal_speed)
    columns.append((energy + pressure) * normal_speed)
    return jnp.stack(columns, axis=0)


def transpose_flux(cons_state, cotangent, direction):
    unused, pullback = jax.vjp(lambda current: euler_flux(current, direction), cons_state)
    return pullback(cotangent)[0]


def section_rate(adj_field, cons_state, left_moments, right_moments, next_left, prev_right):
    derivs, left_vals, right_vals, left_corr, right_corr = basis_tables()
    rate_sum = jnp.zeros_like(adj_field)
    for direction in range(3):
        point_dim = 1 + direction
        bracket = apply_points(adj_field, derivs, point_dim)
        bracket = bracket + 0.5 * lift_face(
            next_left[direction] - right_moments[direction], right_vals, point_dim
        )
        bracket = bracket + 0.5 * lift_face(
            prev_right[direction] - left_moments[direction], left_vals, point_dim
        )
        rate_sum = rate_sum - METRIC * transpose_flux(cons_state, bracket, direction)
    return rate_sum


def all_moments(adj_field):
    derivs, left_vals, right_vals, left_corr, right_corr = basis_tables()
    left_moments = [face_moment(adj_field, left_corr, 1 + direction) for direction in range(3)]
    right_moments = [face_moment(adj_field, right_corr, 1 + direction) for direction in range(3)]
    return (left_moments, right_moments)


def faces_to_rows(face_vals):
    axial_elems = face_vals.shape[3]
    azim_elems = face_vals.shape[4]
    return face_vals.transpose(0, 3, 1, 4, 2).reshape(5, 4 * axial_elems, 4 * azim_elems)


def rows_to_face(rows_vals, axial_elems, azim_elems):
    return rows_vals.reshape(5, axial_elems, 4, azim_elems, 4).transpose(0, 2, 4, 1, 3)


def shift_sum(window, coefs, lo):
    total = None
    for offset, coef in coefs:
        term = coef[None] * window[:, :, lo + offset : lo + offset + TP]
        total = term if total is None else total + term
    return total


def lane_roll(value, shift):
    return pltpu.roll(value, shift % 128, value.ndim - 1)


def sweep(field, weights, pick):
    total = field[pick(0)] * float(weights[0])
    for source in range(1, 4):
        total = total + field[pick(source)] * float(weights[source])
    return total


def column(values, shape):
    rows = lax.broadcasted_iota(jnp.int32, shape, 2)
    out = jnp.full(shape, float(values[3]), jnp.float32)
    for index in range(3):
        out = jnp.where(rows == index, float(values[index]), out)
    return out


def compact_face(face, part):
    lane = lax.broadcasted_iota(jnp.int32, (4, 128), 1)
    out = jnp.zeros((4, 128), jnp.float32)
    for block in range(4):
        for group in range(EA):
            shift = block * ET * ER - group * (ET - 1) * ER - part * ER
            start = block * ET * ER + group * ER
            mask = (lane >= start) & (lane < start + ER)
            out = jnp.where(mask, lane_roll(face[block], shift), out)
    return out


def expand_face(chunk, part):
    lane = lax.broadcasted_iota(jnp.int32, (4, 128), 1)
    group_of = lane // (ET * ER)
    in_part = lane // ER % ET == part
    blocks = []
    for block in range(4):
        out = jnp.zeros((4, 128), jnp.float32)
        for group in range(EA):
            shift = block * ET * ER - group * (ET - 1) * ER - part * ER
            out = jnp.where(in_part & (group_of == group), lane_roll(chunk, -shift), out)
        blocks.append(out)
    return jnp.stack(blocks, axis=0)


def selector(rows, cols, lane_of, use_rows):
    row = lax.broadcasted_iota(jnp.int32, (rows, cols), 0)
    col = lax.broadcasted_iota(jnp.int32, (rows, cols), 1)
    if use_rows:
        hit = (row == lane_of(col)) & (row < EA * ET)
    else:
        hit = (row == lane_of(col)) & (col < EA * ET)
    return jnp.where(hit, 1.0, 0.0)


def exact_dot(left, right):
    return jnp.dot(left, right, precision=lax.Precision.HIGHEST, preferred_element_type=jnp.float32)


def moment_kernel(adj_ref, left_ax_ref, right_ax_ref, up_ref, down_ref, outer_ref, inner_ref, scratch_ref):
    derivs, left_vals, right_vals, left_corr, right_corr = basis_tables()
    pick_outer = selector(128, 128, lambda k: k // ET * ET * ER + k % ET * ER + ER - 1, False)
    pick_inner = selector(128, 128, lambda k: k // ET * ET * ER + k % ET * ER, False)
    for chan in range(5):
        field = adj_ref[0, chan]
        left_ax_ref[chan] = sweep(field, left_corr, lambda i: (i,))
        right_ax_ref[chan] = sweep(field, right_corr, lambda i: (i,))
        pick1 = lambda i: (slice(None), i)
        up_ref[chan] = compact_face(sweep(field, left_corr, pick1), 0)
        down_ref[chan] = compact_face(sweep(field, right_corr, pick1), ET - 1)
        pick2 = lambda i: (slice(None), slice(None), slice(i, i + 1))
        outer = sweep(field, right_corr, pick2)
        inner = sweep(field, left_corr, pick2)
        for axial in range(4):
            for azim in range(4):
                row = axial * 4 + azim
                scratch_ref[0, row : row + 1] = outer[axial, azim]
                scratch_ref[1, row : row + 1] = inner[axial, azim]
        outer_ref[chan] = exact_dot(scratch_ref[0], pick_outer)
        inner_ref[chan] = exact_dot(scratch_ref[1], pick_inner)


def rate_kernel(
    adj_ref, flow_ref, up_ax_ref, down_ax_ref, up_az_ref, down_az_ref, outer_ref, inner_ref,
    rate_ref, next_ref,
):
    derivs, left_vals, right_vals, left_corr, right_corr = basis_tables()
    shape = (4, 4, 4, 128)
    lane = lax.broadcasted_iota(jnp.int32, shape, 3)
    flat_lane = lax.broadcasted_iota(jnp.int32, (4, 4, 128), 2)
    az_flat = flat_lane // ER % ET
    radial_lane = lane % ER
    brackets = [[None] * 5 for _ in range(3)]
    spread = selector(128, 128, lambda k: k // (ET * ER) * ET + k // ER % ET, True)
    for chan in range(5):
        field = adj_ref[0, chan]
        outer_lanes = exact_dot(outer_ref[chan], spread)
        inner_lanes = exact_dot(inner_ref[chan], spread)
        outer_face = jnp.stack(
            [
                jnp.stack(
                    [jnp.broadcast_to(outer_lanes[axial * 4 + azim : axial * 4 + azim + 1], (4, 128)) for azim in range(4)],
                    axis=0,
                )
                for axial in range(4)
            ],
            axis=0,
        )
        inner_face = jnp.stack(
            [
                jnp.stack(
                    [jnp.broadcast_to(inner_lanes[axial * 4 + azim : axial * 4 + azim + 1], (4, 128)) for azim in range(4)],
                    axis=0,
                )
                for axial in range(4)
            ],
            axis=0,
        )
        up_az = expand_face(up_az_ref[chan], 0)
        down_az = expand_face(down_az_ref[chan], ET - 1)
        left0 = sweep(field, left_corr, lambda i: (i,))
        right0 = sweep(field, right_corr, lambda i: (i,))
        next0 = lane_roll(jnp.where(flat_lane < ET * ER, up_ax_ref[chan], left0), -ET * ER)
        prev0 = lane_roll(jnp.where(flat_lane >= (EA - 1) * ET * ER, down_ax_ref[chan], right0), ET * ER)
        jump_r = 0.5 * (next0 - right0)
        jump_l = 0.5 * (prev0 - left0)
        slabs = []
        for target in range(4):
            slab = sweep(field, [derivs[i][target] for i in range(4)], lambda i: (i,))
            slabs.append(slab + jump_r * float(right_vals[target]) + jump_l * float(left_vals[target]))
        brackets[0][chan] = jnp.stack(slabs, axis=0)
        pick1 = lambda i: (slice(None), i)
        left1 = sweep(field, left_corr, pick1)
        right1 = sweep(field, right_corr, pick1)
        next1 = lane_roll(
            jnp.where(az_flat == 0, lane_roll(up_az, ET * ER), left1), -ER
        )
        prev1 = lane_roll(
            jnp.where(az_flat == ET - 1, lane_roll(down_az, -ET * ER), right1), ER
        )
        jump_r = 0.5 * (next1 - right1)
        jump_l = 0.5 * (prev1 - left1)
        slabs = []
        for target in range(4):
            slab = sweep(field, [derivs[i][target] for i in range(4)], pick1)
            slabs.append(slab + jump_r * float(right_vals[target]) + jump_l * float(left_vals[target]))
        brackets[1][chan] = jnp.stack(slabs, axis=1)
        points = [jnp.broadcast_to(field[:, :, i : i + 1, :], shape) for i in range(4)]
        left2 = sweep(points, left_corr, lambda i: i)
        right2 = sweep(points, right_corr, lambda i: i)
        next2 = jnp.where(radial_lane == ER - 1, outer_face, lane_roll(left2, -1))
        prev2 = jnp.where(radial_lane == 0, inner_face, lane_roll(right2, 1))
        bracket = 0.5 * (next2 - right2) * column(right_vals, shape)
        bracket = bracket + 0.5 * (prev2 - left2) * column(left_vals, shape)
        for source in range(4):
            bracket = bracket + points[source] * column(derivs[source], shape)
        brackets[2][chan] = bracket
    prim = [flow_ref[0, chan].astype(jnp.float32) for chan in range(5)]
    density = prim[0]
    speed_sq = prim[1] * prim[1] + prim[2] * prim[2] + prim[3] * prim[3]
    energy = prim[4] / (GAMMA - 1.0) + 0.5 * density * speed_sq
    momentum = [density * prim[1 + k] for k in range(3)]
    velocity = [momentum[k] / density for k in range(3)]
    kinetic = momentum[0] * velocity[0] + momentum[1] * velocity[1] + momentum[2] * velocity[2]
    pressure = (GAMMA - 1.0) * (energy - 0.5 * kinetic)
    enthalpy = (energy + pressure) / density
    vel_sq = velocity[0] * velocity[0] + velocity[1] * velocity[1] + velocity[2] * velocity[2]
    grad = [None] * 5
    for direction in range(3):
        cot = brackets[direction]
        normal = velocity[direction]
        dotted = cot[1] * velocity[0] + cot[2] * velocity[1] + cot[3] * velocity[2] + cot[4] * enthalpy
        weight = cot[1 + direction] + cot[4] * normal
        terms = [
            0.5 * (GAMMA - 1.0) * vel_sq * weight - dotted * normal,
            None,
            None,
            None,
            (GAMMA - 1.0) * weight + cot[4] * normal,
        ]
        for k in range(3):
            term = cot[1 + k] * normal - (GAMMA - 1.0) * weight * velocity[k]
            if k == direction:
                term = term + (cot[0] + dotted)
            terms[1 + k] = term
        for chan in range(5):
            grad[chan] = terms[chan] if grad[chan] is None else grad[chan] + terms[chan]
    for chan in range(5):
        rate = -METRIC * grad[chan]
        rate_ref[0, chan] = rate
        next_ref[0, chan] = adj_ref[0, chan] + SECTION_STEP * rate


def local(adjoint, flow_prim, intersection_shift, weight_index, mortar_weights, sector_offset):
    n_axial = lax.axis_size("axial")
    n_azim = lax.axis_size("azim")
    face4 = jax.ShapeDtypeStruct((5, 4, 4, 128), jnp.float32)
    chunk = jax.ShapeDtypeStruct((5, 4, 128), jnp.float32)
    rows16 = jax.ShapeDtypeStruct((5, 16, 128), jnp.float32)
    left_ax, right_ax, upper_face, lower_face, outer_moment, inner_moment = pl.pallas_call(
        moment_kernel,
        out_shape=(face4, face4, chunk, chunk, rows16, rows16),
        scratch_shapes=[pltpu.VMEM((2, 16, 128), jnp.float32)],
    )(adjoint)
    is_rotor = lax.axis_index("zone") == 0
    up_ax = lax.ppermute(left_ax, "axial", [(i + 1, i) for i in range(n_axial - 1)])
    down_ax = lax.ppermute(right_ax, "axial", [(i, i + 1) for i in range(n_axial - 1)])
    own_face = jnp.where(is_rotor, outer_moment, inner_moment)[:, :, : EA * ET]
    own_rows = own_face.reshape(5, 4, 4, EA, ET).transpose(0, 3, 1, 4, 2).reshape(5, AP, TP)
    shifts_local = intersection_shift.reshape(INTERSECTIONS, AP, TP)
    table_match = weight_index[:, :, None] == jnp.arange(NW, dtype=jnp.int32)[None, None, :]
    weights_local = jnp.sum(
        jnp.where(table_match, mortar_weights[None, None, :], 0.0), axis=2
    ).reshape(INTERSECTIONS, AP, TP)
    offset = sector_offset[0]
    turn = (offset + TP // 2) // TP
    residue = offset - turn * TP
    offsets_k = residue + shifts_local
    coefs = []
    for rel in range(-TP, TP - 1):
        coef = jnp.where(offsets_k[0] == rel, weights_local[0], 0.0)
        for member in range(1, INTERSECTIONS):
            coef = coef + jnp.where(offsets_k[member] == rel, weights_local[member], 0.0)
        coefs.append((rel, coef))
    contrib = None
    for rel, coef in coefs:
        term = jnp.pad(coef[None] * own_rows, ((0, 0), (0, 0), (TP + rel, TP - rel)))
        contrib = term if contrib is None else contrib + term
    zone = lax.axis_index("zone")
    azim = lax.axis_index("azim")
    dest = jnp.arange(2 * n_azim, dtype=jnp.int32)
    dest_azim = dest % n_azim
    gap = ((dest_azim - azim) % n_azim - turn) % n_azim
    gap = gap[:, None, None, None]
    pieces = jnp.where(
        gap == n_azim - 1,
        contrib[None, :, :, :TP],
        jnp.where(gap == 0, contrib[None, :, :, TP : 2 * TP], contrib[None, :, :, 2 * TP :]),
    )
    iface_out = jnp.where(is_rotor, jnp.broadcast_to(own_rows[None], pieces.shape), pieces)
    iface_out = jnp.pad(iface_out.reshape(2 * n_azim, 5, 2, 128), ((0, 0), (0, 0), (0, 2), (0, 0)))
    same_zone = dest // n_azim == zone
    to_prev = (same_zone & (dest_azim == (azim - 1) % n_azim))[:, None, None, None]
    to_next = (same_zone & (dest_azim == (azim + 1) % n_azim))[:, None, None, None]
    chunks = jnp.where(
        to_prev, upper_face[None], jnp.where(to_next, lower_face[None], jnp.where(same_zone[:, None, None, None], 0.0, iface_out))
    )
    got = lax.all_to_all(chunks, ("zone", "azim"), 0, 0)
    base = (1 - zone) * n_azim
    up_az = lax.dynamic_index_in_dim(got, zone * n_azim + (azim + 1) % n_azim, 0, keepdims=False)
    down_az = lax.dynamic_index_in_dim(got, zone * n_azim + (azim - 1) % n_azim, 0, keepdims=False)
    direction = jnp.where(is_rotor, -1, 1)
    picked = [
        lax.dynamic_index_in_dim(
            got, base + (azim + direction * (turn + step)) % n_azim, 0, keepdims=False
        )[:, :2].reshape(5, AP, TP)
        for step in (-1, 0, 1)
    ]
    returned = picked[0] + picked[1] + picked[2]
    window = jnp.concatenate(picked, axis=2)
    incoming = shift_sum(window, coefs, TP)
    def to_lanes(rows_vals):
        face = rows_vals.reshape(5, EA, 4, ET, 4).transpose(0, 2, 4, 1, 3).reshape(5, 16, EA * ET)
        return jnp.pad(face, ((0, 0), (0, 0), (0, 128 - EA * ET)))

    outer = to_lanes(jnp.where(is_rotor, returned, 0.0))
    inner = to_lanes(jnp.where(is_rotor, 0.0, incoming))
    field_shape = jax.ShapeDtypeStruct(adjoint.shape, jnp.float32)
    adjoint_rate, next_adjoint = pl.pallas_call(
        rate_kernel, out_shape=(field_shape, field_shape)
    )(adjoint, flow_prim, up_ax, down_ax, up_az, down_az, outer, inner)
    return (adjoint_rate, next_adjoint)


def solution(mesh):
    placed = (
        P("zone", None, None, None, None, ("axial", "azim")),
        P("zone", None, None, None, None, ("axial", "azim")),
        P(None, ("axial", "azim")),
        P(None, ("axial", "azim")),
        P(),
        P(),
    )
    return jax.shard_map(
        local,
        mesh=mesh,
        in_specs=placed,
        out_specs=(
            P("zone", None, None, None, None, ("axial", "azim")),
            P("zone", None, None, None, None, ("axial", "azim")),
        ),
        check_vma=False,
    )
```

```python
import math

import jax
import jax.numpy as jnp
from jax import lax
from jax.experimental import pallas as pl
from jax.experimental.pallas import tpu as pltpu
from jax.sharding import PartitionSpec as P

EA = 4
ET = 4
ER = 8
INTERSECTIONS = 4
NW = 128
AP = 16
TP = 16


GAMMA = 1.4
METRIC = 0.1
SECTION_STEP = 0.5


def gauss_nodes():
    root_term = math.sqrt(6.0 / 5.0)
    inner_node = math.sqrt(3.0 / 7.0 - 2.0 / 7.0 * root_term)
    outer_node = math.sqrt(3.0 / 7.0 + 2.0 / 7.0 * root_term)
    return [-outer_node, -inner_node, inner_node, outer_node]


def lagrange_value(node_list, column, position):
    result = 1.0
    for factor_index in range(4):
        if factor_index != column:
            result = (
                result
                * (position - node_list[factor_index])
                / (node_list[column] - node_list[factor_index])
            )
    return result


def lagrange_slope(node_list, column, position):
    total = 0.0
    for skipped in range(4):
        if skipped == column:
            continue
        term = 1.0 / (node_list[column] - node_list[skipped])
        for factor_index in range(4):
            if factor_index != column and factor_index != skipped:
                term = (
                    term
                    * (position - node_list[factor_index])
                    / (node_list[column] - node_list[factor_index])
                )
        total = total + term
    return total


def basis_tables():
    node_list = gauss_nodes()
    derivs = [
        [lagrange_slope(node_list, column, node_list[source]) for column in range(4)]
        for source in range(4)
    ]
    left_vals = [lagrange_value(node_list, column, -1.0) for column in range(4)]
    right_vals = [lagrange_value(node_list, column, 1.0) for column in range(4)]
    third_slope = [(15.0 * value * value - 3.0) / 2.0 for value in node_list]
    fourth_slope = [(35.0 * value**3 - 15.0 * value) / 2.0 for value in node_list]
    left_corr = [-0.5 * (third_slope[source] - fourth_slope[source]) for source in range(4)]
    right_corr = [0.5 * (third_slope[source] + fourth_slope[source]) for source in range(4)]
    return (derivs, left_vals, right_vals, left_corr, right_corr)


def apply_points(adj_field, matrix, point_dim):
    slab_list = [
        lax.index_in_dim(adj_field, source, point_dim, keepdims=False) for source in range(4)
    ]
    outputs = []
    for target in range(4):
        running = slab_list[0] * float(matrix[0][target])
        for source in range(1, 4):
            running = running + slab_list[source] * float(matrix[source][target])
        outputs.append(running)
    return jnp.stack(outputs, axis=point_dim)


def face_moment(adj_field, vector, point_dim):
    running = lax.index_in_dim(adj_field, 0, point_dim, keepdims=False) * float(vector[0])
    for source in range(1, 4):
        running = running + lax.index_in_dim(adj_field, source, point_dim, keepdims=False) * float(
            vector[source]
        )
    return running


def lift_face(face_vals, vector, point_dim):
    return jnp.stack([face_vals * float(vector[target]) for target in range(4)], axis=point_dim)


def conserved(primitive):
    density = primitive[0]
    velocity = primitive[1:4]
    pressure = primitive[4]
    energy = pressure / (GAMMA - 1.0) + 0.5 * density * jnp.sum(velocity * velocity, axis=0)
    return jnp.concatenate([density[None], density[None] * velocity, energy[None]], axis=0)


def euler_flux(cons_state, direction):
    density = cons_state[0]
    momentum = cons_state[1:4]
    energy = cons_state[4]
    velocity = momentum / density[None]
    pressure = (GAMMA - 1.0) * (energy - 0.5 * jnp.sum(momentum * velocity, axis=0))
    normal_speed = velocity[direction]
    columns = [momentum[direction]]
    for component in range(3):
        if component == direction:
            columns.append(momentum[component] * normal_speed + pressure)
        else:
            columns.append(momentum[component] * normal_speed)
    columns.append((energy + pressure) * normal_speed)
    return jnp.stack(columns, axis=0)


def transpose_flux(cons_state, cotangent, direction):
    unused, pullback = jax.vjp(lambda current: euler_flux(current, direction), cons_state)
    return pullback(cotangent)[0]


def section_rate(adj_field, cons_state, left_moments, right_moments, next_left, prev_right):
    derivs, left_vals, right_vals, left_corr, right_corr = basis_tables()
    rate_sum = jnp.zeros_like(adj_field)
    for direction in range(3):
        point_dim = 1 + direction
        bracket = apply_points(adj_field, derivs, point_dim)
        bracket = bracket + 0.5 * lift_face(
            next_left[direction] - right_moments[direction], right_vals, point_dim
        )
        bracket = bracket + 0.5 * lift_face(
            prev_right[direction] - left_moments[direction], left_vals, point_dim
        )
        rate_sum = rate_sum - METRIC * transpose_flux(cons_state, bracket, direction)
    return rate_sum


def all_moments(adj_field):
    derivs, left_vals, right_vals, left_corr, right_corr = basis_tables()
    left_moments = [face_moment(adj_field, left_corr, 1 + direction) for direction in range(3)]
    right_moments = [face_moment(adj_field, right_corr, 1 + direction) for direction in range(3)]
    return (left_moments, right_moments)


def faces_to_rows(face_vals):
    axial_elems = face_vals.shape[3]
    azim_elems = face_vals.shape[4]
    return face_vals.transpose(0, 3, 1, 4, 2).reshape(5, 4 * axial_elems, 4 * azim_elems)


def rows_to_face(rows_vals, axial_elems, azim_elems):
    return rows_vals.reshape(5, axial_elems, 4, azim_elems, 4).transpose(0, 2, 4, 1, 3)


def shift_sum(window, coefs, lo):
    total = None
    for offset, coef in coefs:
        term = coef[None] * window[:, :, lo + offset : lo + offset + TP]
        total = term if total is None else total + term
    return total


def lane_roll(value, shift):
    return pltpu.roll(value, shift % 128, value.ndim - 1)


def sweep(field, weights, pick):
    total = field[pick(0)] * float(weights[0])
    for source in range(1, 4):
        total = total + field[pick(source)] * float(weights[source])
    return total


def column(values, shape):
    rows = lax.broadcasted_iota(jnp.int32, shape, 2)
    out = jnp.full(shape, float(values[3]), jnp.float32)
    for index in range(3):
        out = jnp.where(rows == index, float(values[index]), out)
    return out


def compact_face(face, part):
    lane = lax.broadcasted_iota(jnp.int32, (4, 128), 1)
    out = jnp.zeros((4, 128), jnp.float32)
    for block in range(4):
        for group in range(EA):
            shift = block * ET * ER - group * (ET - 1) * ER - part * ER
            start = block * ET * ER + group * ER
            mask = (lane >= start) & (lane < start + ER)
            out = jnp.where(mask, lane_roll(face[block], shift), out)
    return out


def expand_face(chunk, part):
    lane = lax.broadcasted_iota(jnp.int32, (4, 128), 1)
    group_of = lane // (ET * ER)
    in_part = lane // ER % ET == part
    blocks = []
    for block in range(4):
        out = jnp.zeros((4, 128), jnp.float32)
        for group in range(EA):
            shift = block * ET * ER - group * (ET - 1) * ER - part * ER
            out = jnp.where(in_part & (group_of == group), lane_roll(chunk, -shift), out)
        blocks.append(out)
    return jnp.stack(blocks, axis=0)


def selector(rows, cols, lane_of, use_rows):
    row = lax.broadcasted_iota(jnp.int32, (rows, cols), 0)
    col = lax.broadcasted_iota(jnp.int32, (rows, cols), 1)
    if use_rows:
        hit = (row == lane_of(col)) & (row < EA * ET)
    else:
        hit = (row == lane_of(col)) & (col < EA * ET)
    return jnp.where(hit, 1.0, 0.0)


def exact_dot(left, right):
    return jnp.dot(left, right, precision=lax.Precision.HIGHEST, preferred_element_type=jnp.float32)


def moment_kernel(adj_ref, left_ax_ref, right_ax_ref, up_ref, down_ref, outer_ref, inner_ref, scratch_ref):
    derivs, left_vals, right_vals, left_corr, right_corr = basis_tables()
    pick_outer = selector(128, 128, lambda k: k // ET * ET * ER + k % ET * ER + ER - 1, False)
    pick_inner = selector(128, 128, lambda k: k // ET * ET * ER + k % ET * ER, False)
    for chan in range(5):
        field = adj_ref[0, chan]
        left_ax_ref[chan] = sweep(field, left_corr, lambda i: (i,))
        right_ax_ref[chan] = sweep(field, right_corr, lambda i: (i,))
        pick1 = lambda i: (slice(None), i)
        up_ref[chan] = compact_face(sweep(field, left_corr, pick1), 0)
        down_ref[chan] = compact_face(sweep(field, right_corr, pick1), ET - 1)
        pick2 = lambda i: (slice(None), slice(None), slice(i, i + 1))
        outer = sweep(field, right_corr, pick2)
        inner = sweep(field, left_corr, pick2)
        for axial in range(4):
            for azim in range(4):
                row = axial * 4 + azim
                scratch_ref[0, row : row + 1] = outer[axial, azim]
                scratch_ref[1, row : row + 1] = inner[axial, azim]
        outer_ref[chan] = exact_dot(scratch_ref[0], pick_outer)
        inner_ref[chan] = exact_dot(scratch_ref[1], pick_inner)


def rate_kernel(
    adj_ref, flow_ref, up_ax_ref, down_ax_ref, up_az_ref, down_az_ref, outer_ref, inner_ref,
    rate_ref, next_ref,
):
    derivs, left_vals, right_vals, left_corr, right_corr = basis_tables()
    shape = (4, 4, 4, 128)
    lane = lax.broadcasted_iota(jnp.int32, shape, 3)
    flat_lane = lax.broadcasted_iota(jnp.int32, (4, 4, 128), 2)
    az_flat = flat_lane // ER % ET
    radial_lane = lane % ER
    brackets = [[None] * 5 for _ in range(3)]
    spread = selector(128, 128, lambda k: k // (ET * ER) * ET + k // ER % ET, True)
    for chan in range(5):
        field = adj_ref[0, chan]
        outer_lanes = exact_dot(outer_ref[chan], spread)
        inner_lanes = exact_dot(inner_ref[chan], spread)
        outer_face = jnp.stack(
            [
                jnp.stack(
                    [jnp.broadcast_to(outer_lanes[axial * 4 + azim : axial * 4 + azim + 1], (4, 128)) for azim in range(4)],
                    axis=0,
                )
                for axial in range(4)
            ],
            axis=0,
        )
        inner_face = jnp.stack(
            [
                jnp.stack(
                    [jnp.broadcast_to(inner_lanes[axial * 4 + azim : axial * 4 + azim + 1], (4, 128)) for azim in range(4)],
                    axis=0,
                )
                for axial in range(4)
            ],
            axis=0,
        )
        up_az = expand_face(up_az_ref[chan], 0)
        down_az = expand_face(down_az_ref[chan], ET - 1)
        left0 = sweep(field, left_corr, lambda i: (i,))
        right0 = sweep(field, right_corr, lambda i: (i,))
        next0 = lane_roll(jnp.where(flat_lane < ET * ER, up_ax_ref[chan], left0), -ET * ER)
        prev0 = lane_roll(jnp.where(flat_lane >= (EA - 1) * ET * ER, down_ax_ref[chan], right0), ET * ER)
        jump_r = 0.5 * (next0 - right0)
        jump_l = 0.5 * (prev0 - left0)
        slabs = []
        for target in range(4):
            slab = sweep(field, [derivs[i][target] for i in range(4)], lambda i: (i,))
            slabs.append(slab + jump_r * float(right_vals[target]) + jump_l * float(left_vals[target]))
        brackets[0][chan] = jnp.stack(slabs, axis=0)
        pick1 = lambda i: (slice(None), i)
        left1 = sweep(field, left_corr, pick1)
        right1 = sweep(field, right_corr, pick1)
        next1 = lane_roll(
            jnp.where(az_flat == 0, lane_roll(up_az, ET * ER), left1), -ER
        )
        prev1 = lane_roll(
            jnp.where(az_flat == ET - 1, lane_roll(down_az, -ET * ER), right1), ER
        )
        jump_r = 0.5 * (next1 - right1)
        jump_l = 0.5 * (prev1 - left1)
        slabs = []
        for target in range(4):
            slab = sweep(field, [derivs[i][target] for i in range(4)], pick1)
            slabs.append(slab + jump_r * float(right_vals[target]) + jump_l * float(left_vals[target]))
        brackets[1][chan] = jnp.stack(slabs, axis=1)
        points = [jnp.broadcast_to(field[:, :, i : i + 1, :], shape) for i in range(4)]
        left2 = sweep(points, left_corr, lambda i: i)
        right2 = sweep(points, right_corr, lambda i: i)
        next2 = jnp.where(radial_lane == ER - 1, outer_face, lane_roll(left2, -1))
        prev2 = jnp.where(radial_lane == 0, inner_face, lane_roll(right2, 1))
        bracket = 0.5 * (next2 - right2) * column(right_vals, shape)
        bracket = bracket + 0.5 * (prev2 - left2) * column(left_vals, shape)
        for source in range(4):
            bracket = bracket + points[source] * column(derivs[source], shape)
        brackets[2][chan] = bracket
    prim = [flow_ref[0, chan].astype(jnp.float32) for chan in range(5)]
    density = prim[0]
    speed_sq = prim[1] * prim[1] + prim[2] * prim[2] + prim[3] * prim[3]
    energy = prim[4] / (GAMMA - 1.0) + 0.5 * density * speed_sq
    momentum = [density * prim[1 + k] for k in range(3)]
    velocity = [momentum[k] / density for k in range(3)]
    kinetic = momentum[0] * velocity[0] + momentum[1] * velocity[1] + momentum[2] * velocity[2]
    pressure = (GAMMA - 1.0) * (energy - 0.5 * kinetic)
    enthalpy = (energy + pressure) / density
    vel_sq = velocity[0] * velocity[0] + velocity[1] * velocity[1] + velocity[2] * velocity[2]
    grad = [None] * 5
    for direction in range(3):
        cot = brackets[direction]
        normal = velocity[direction]
        dotted = cot[1] * velocity[0] + cot[2] * velocity[1] + cot[3] * velocity[2] + cot[4] * enthalpy
        weight = cot[1 + direction] + cot[4] * normal
        terms = [
            0.5 * (GAMMA - 1.0) * vel_sq * weight - dotted * normal,
            None,
            None,
            None,
            (GAMMA - 1.0) * weight + cot[4] * normal,
        ]
        for k in range(3):
            term = cot[1 + k] * normal - (GAMMA - 1.0) * weight * velocity[k]
            if k == direction:
                term = term + (cot[0] + dotted)
            terms[1 + k] = term
        for chan in range(5):
            grad[chan] = terms[chan] if grad[chan] is None else grad[chan] + terms[chan]
    for chan in range(5):
        rate = -METRIC * grad[chan]
        rate_ref[0, chan] = rate
        next_ref[0, chan] = adj_ref[0, chan] + SECTION_STEP * rate


def local(adjoint, flow_prim, intersection_shift, weight_index, mortar_weights, sector_offset):
    n_axial = lax.axis_size("axial")
    n_azim = lax.axis_size("azim")
    face4 = jax.ShapeDtypeStruct((5, 4, 4, 128), jnp.float32)
    chunk = jax.ShapeDtypeStruct((5, 4, 128), jnp.float32)
    rows16 = jax.ShapeDtypeStruct((5, 16, 128), jnp.float32)
    left_ax, right_ax, upper_face, lower_face, outer_moment, inner_moment = pl.pallas_call(
        moment_kernel,
        out_shape=(face4, face4, chunk, chunk, rows16, rows16),
        scratch_shapes=[pltpu.VMEM((2, 16, 128), jnp.float32)],
    )(adjoint)
    is_rotor = lax.axis_index("zone") == 0
    up_ax = lax.ppermute(left_ax, "axial", [(i + 1, i) for i in range(n_axial - 1)])
    down_ax = lax.ppermute(right_ax, "axial", [(i, i + 1) for i in range(n_axial - 1)])
    own_face = jnp.where(is_rotor, outer_moment, inner_moment)[:, :, : EA * ET]
    own_rows = own_face.reshape(5, 4, 4, EA, ET).transpose(0, 3, 1, 4, 2).reshape(5, AP, TP)
    shifts_local = intersection_shift.reshape(INTERSECTIONS, AP, TP)
    table_match = weight_index[:, :, None] == jnp.arange(NW, dtype=jnp.int32)[None, None, :]
    weights_local = jnp.sum(
        jnp.where(table_match, mortar_weights[None, None, :], 0.0), axis=2
    ).reshape(INTERSECTIONS, AP, TP)
    offset = sector_offset[0]
    turn = (offset + TP // 2) // TP
    residue = offset - turn * TP
    offsets_k = residue + shifts_local
    coefs = []
    for rel in range(-TP, TP - 1):
        coef = jnp.where(offsets_k[0] == rel, weights_local[0], 0.0)
        for member in range(1, INTERSECTIONS):
            coef = coef + jnp.where(offsets_k[member] == rel, weights_local[member], 0.0)
        coefs.append((rel, coef))
    contrib = None
    for rel, coef in coefs:
        term = jnp.pad(coef[None] * own_rows, ((0, 0), (0, 0), (TP + rel, TP - rel)))
        contrib = term if contrib is None else contrib + term
    zone = lax.axis_index("zone")
    azim = lax.axis_index("azim")
    dest = jnp.arange(2 * n_azim, dtype=jnp.int32)
    dest_azim = dest % n_azim
    gap = ((dest_azim - azim) % n_azim - turn) % n_azim
    gap = gap[:, None, None, None]
    pieces = jnp.where(
        gap == n_azim - 1,
        contrib[None, :, :, :TP],
        jnp.where(gap == 0, contrib[None, :, :, TP : 2 * TP], contrib[None, :, :, 2 * TP :]),
    )
    iface_out = jnp.where(is_rotor, jnp.broadcast_to(own_rows[None], pieces.shape), pieces)
    iface_out = jnp.pad(iface_out.reshape(2 * n_azim, 5, 2, 128), ((0, 0), (0, 0), (0, 2), (0, 0)))
    same_zone = dest // n_azim == zone
    to_prev = (same_zone & (dest_azim == (azim - 1) % n_azim))[:, None, None, None]
    to_next = (same_zone & (dest_azim == (azim + 1) % n_azim))[:, None, None, None]
    chunks = jnp.where(
        to_prev, upper_face[None], jnp.where(to_next, lower_face[None], jnp.where(same_zone[:, None, None, None], 0.0, iface_out))
    )
    up_ax, down_ax, chunks = lax.optimization_barrier((up_ax, down_ax, chunks))
    got = lax.all_to_all(chunks, ("zone", "azim"), 0, 0)
    base = (1 - zone) * n_azim
    up_az = lax.dynamic_index_in_dim(got, zone * n_azim + (azim + 1) % n_azim, 0, keepdims=False)
    down_az = lax.dynamic_index_in_dim(got, zone * n_azim + (azim - 1) % n_azim, 0, keepdims=False)
    direction = jnp.where(is_rotor, -1, 1)
    picked = [
        lax.dynamic_index_in_dim(
            got, base + (azim + direction * (turn + step)) % n_azim, 0, keepdims=False
        )[:, :2].reshape(5, AP, TP)
        for step in (-1, 0, 1)
    ]
    returned = picked[0] + picked[1] + picked[2]
    window = jnp.concatenate(picked, axis=2)
    incoming = shift_sum(window, coefs, TP)
    def to_lanes(rows_vals):
        face = rows_vals.reshape(5, EA, 4, ET, 4).transpose(0, 2, 4, 1, 3).reshape(5, 16, EA * ET)
        return jnp.pad(face, ((0, 0), (0, 0), (0, 128 - EA * ET)))

    outer = to_lanes(jnp.where(is_rotor, returned, 0.0))
    inner = to_lanes(jnp.where(is_rotor, 0.0, incoming))
    field_shape = jax.ShapeDtypeStruct(adjoint.shape, jnp.float32)
    adjoint_rate, next_adjoint = pl.pallas_call(
        rate_kernel, out_shape=(field_shape, field_shape)
    )(adjoint, flow_prim, up_ax, down_ax, up_az, down_az, outer, inner)
    return (adjoint_rate, next_adjoint)


def solution(mesh):
    placed = (
        P("zone", None, None, None, None, ("axial", "azim")),
        P("zone", None, None, None, None, ("axial", "azim")),
        P(None, ("axial", "azim")),
        P(None, ("axial", "azim")),
        P(),
        P(),
    )
    return jax.shard_map(
        local,
        mesh=mesh,
        in_specs=placed,
        out_specs=(
            P("zone", None, None, None, None, ("axial", "azim")),
            P("zone", None, None, None, None, ("axial", "azim")),
        ),
        check_vma=False,
    )
```

```python
import math

import jax
import jax.numpy as jnp
from jax import lax
from jax.experimental import pallas as pl
from jax.experimental.pallas import tpu as pltpu
from jax.sharding import PartitionSpec as P

EA = 4
ET = 4
ER = 8
INTERSECTIONS = 4
NW = 128
AP = 16
TP = 16


GAMMA = 1.4
METRIC = 0.1
SECTION_STEP = 0.5


def gauss_nodes():
    root_term = math.sqrt(6.0 / 5.0)
    inner_node = math.sqrt(3.0 / 7.0 - 2.0 / 7.0 * root_term)
    outer_node = math.sqrt(3.0 / 7.0 + 2.0 / 7.0 * root_term)
    return [-outer_node, -inner_node, inner_node, outer_node]


def lagrange_value(node_list, column, position):
    result = 1.0
    for factor_index in range(4):
        if factor_index != column:
            result = (
                result
                * (position - node_list[factor_index])
                / (node_list[column] - node_list[factor_index])
            )
    return result


def lagrange_slope(node_list, column, position):
    total = 0.0
    for skipped in range(4):
        if skipped == column:
            continue
        term = 1.0 / (node_list[column] - node_list[skipped])
        for factor_index in range(4):
            if factor_index != column and factor_index != skipped:
                term = (
                    term
                    * (position - node_list[factor_index])
                    / (node_list[column] - node_list[factor_index])
                )
        total = total + term
    return total


def basis_tables():
    node_list = gauss_nodes()
    derivs = [
        [lagrange_slope(node_list, column, node_list[source]) for column in range(4)]
        for source in range(4)
    ]
    left_vals = [lagrange_value(node_list, column, -1.0) for column in range(4)]
    right_vals = [lagrange_value(node_list, column, 1.0) for column in range(4)]
    third_slope = [(15.0 * value * value - 3.0) / 2.0 for value in node_list]
    fourth_slope = [(35.0 * value**3 - 15.0 * value) / 2.0 for value in node_list]
    left_corr = [-0.5 * (third_slope[source] - fourth_slope[source]) for source in range(4)]
    right_corr = [0.5 * (third_slope[source] + fourth_slope[source]) for source in range(4)]
    return (derivs, left_vals, right_vals, left_corr, right_corr)


def apply_points(adj_field, matrix, point_dim):
    slab_list = [
        lax.index_in_dim(adj_field, source, point_dim, keepdims=False) for source in range(4)
    ]
    outputs = []
    for target in range(4):
        running = slab_list[0] * float(matrix[0][target])
        for source in range(1, 4):
            running = running + slab_list[source] * float(matrix[source][target])
        outputs.append(running)
    return jnp.stack(outputs, axis=point_dim)


def face_moment(adj_field, vector, point_dim):
    running = lax.index_in_dim(adj_field, 0, point_dim, keepdims=False) * float(vector[0])
    for source in range(1, 4):
        running = running + lax.index_in_dim(adj_field, source, point_dim, keepdims=False) * float(
            vector[source]
        )
    return running


def lift_face(face_vals, vector, point_dim):
    return jnp.stack([face_vals * float(vector[target]) for target in range(4)], axis=point_dim)


def conserved(primitive):
    density = primitive[0]
    velocity = primitive[1:4]
    pressure = primitive[4]
    energy = pressure / (GAMMA - 1.0) + 0.5 * density * jnp.sum(velocity * velocity, axis=0)
    return jnp.concatenate([density[None], density[None] * velocity, energy[None]], axis=0)


def euler_flux(cons_state, direction):
    density = cons_state[0]
    momentum = cons_state[1:4]
    energy = cons_state[4]
    velocity = momentum / density[None]
    pressure = (GAMMA - 1.0) * (energy - 0.5 * jnp.sum(momentum * velocity, axis=0))
    normal_speed = velocity[direction]
    columns = [momentum[direction]]
    for component in range(3):
        if component == direction:
            columns.append(momentum[component] * normal_speed + pressure)
        else:
            columns.append(momentum[component] * normal_speed)
    columns.append((energy + pressure) * normal_speed)
    return jnp.stack(columns, axis=0)


def transpose_flux(cons_state, cotangent, direction):
    unused, pullback = jax.vjp(lambda current: euler_flux(current, direction), cons_state)
    return pullback(cotangent)[0]


def section_rate(adj_field, cons_state, left_moments, right_moments, next_left, prev_right):
    derivs, left_vals, right_vals, left_corr, right_corr = basis_tables()
    rate_sum = jnp.zeros_like(adj_field)
    for direction in range(3):
        point_dim = 1 + direction
        bracket = apply_points(adj_field, derivs, point_dim)
        bracket = bracket + 0.5 * lift_face(
            next_left[direction] - right_moments[direction], right_vals, point_dim
        )
        bracket = bracket + 0.5 * lift_face(
            prev_right[direction] - left_moments[direction], left_vals, point_dim
        )
        rate_sum = rate_sum - METRIC * transpose_flux(cons_state, bracket, direction)
    return rate_sum


def all_moments(adj_field):
    derivs, left_vals, right_vals, left_corr, right_corr = basis_tables()
    left_moments = [face_moment(adj_field, left_corr, 1 + direction) for direction in range(3)]
    right_moments = [face_moment(adj_field, right_corr, 1 + direction) for direction in range(3)]
    return (left_moments, right_moments)


def faces_to_rows(face_vals):
    axial_elems = face_vals.shape[3]
    azim_elems = face_vals.shape[4]
    return face_vals.transpose(0, 3, 1, 4, 2).reshape(5, 4 * axial_elems, 4 * azim_elems)


def rows_to_face(rows_vals, axial_elems, azim_elems):
    return rows_vals.reshape(5, axial_elems, 4, azim_elems, 4).transpose(0, 2, 4, 1, 3)


def shift_sum(window, coefs, lo):
    total = None
    for offset, coef in coefs:
        term = coef[None] * window[:, :, lo + offset : lo + offset + TP]
        total = term if total is None else total + term
    return total


def lane_roll(value, shift):
    return pltpu.roll(value, shift % 128, value.ndim - 1)


def sweep(field, weights, pick):
    total = field[pick(0)] * float(weights[0])
    for source in range(1, 4):
        total = total + field[pick(source)] * float(weights[source])
    return total


def column(values, shape):
    rows = lax.broadcasted_iota(jnp.int32, shape, 2)
    out = jnp.full(shape, float(values[3]), jnp.float32)
    for index in range(3):
        out = jnp.where(rows == index, float(values[index]), out)
    return out


def compact_face(face, part):
    lane = lax.broadcasted_iota(jnp.int32, (4, 128), 1)
    out = jnp.zeros((4, 128), jnp.float32)
    for block in range(4):
        for group in range(EA):
            shift = block * ET * ER - group * (ET - 1) * ER - part * ER
            start = block * ET * ER + group * ER
            mask = (lane >= start) & (lane < start + ER)
            out = jnp.where(mask, lane_roll(face[block], shift), out)
    return out


def expand_face(chunk, part):
    lane = lax.broadcasted_iota(jnp.int32, (4, 128), 1)
    group_of = lane // (ET * ER)
    in_part = lane // ER % ET == part
    blocks = []
    for block in range(4):
        out = jnp.zeros((4, 128), jnp.float32)
        for group in range(EA):
            shift = block * ET * ER - group * (ET - 1) * ER - part * ER
            out = jnp.where(in_part & (group_of == group), lane_roll(chunk, -shift), out)
        blocks.append(out)
    return jnp.stack(blocks, axis=0)


def selector(rows, cols, lane_of, use_rows):
    row = lax.broadcasted_iota(jnp.int32, (rows, cols), 0)
    col = lax.broadcasted_iota(jnp.int32, (rows, cols), 1)
    if use_rows:
        hit = (row == lane_of(col)) & (row < EA * ET)
    else:
        hit = (row == lane_of(col)) & (col < EA * ET)
    return jnp.where(hit, 1.0, 0.0)


def exact_dot(left, right):
    return jnp.dot(left, right, precision=lax.Precision.HIGHEST, preferred_element_type=jnp.float32)


def compact_axial(face, part):
    lane = lax.broadcasted_iota(jnp.int32, (4, 128), 1)
    span = ET * ER
    out = jnp.zeros((4, 128), jnp.float32)
    for block in range(4):
        mask = (lane >= block * span) & (lane < block * span + span)
        out = jnp.where(mask, lane_roll(face[block], block * span - part * span), out)
    return out


def expand_axial(chunk, part):
    span = ET * ER
    return jnp.stack([lane_roll(chunk, part * span - block * span) for block in range(4)], axis=0)


def moment_kernel(adj_ref, left_ax_ref, right_ax_ref, up_ref, down_ref, outer_ref, inner_ref, scratch_ref):
    derivs, left_vals, right_vals, left_corr, right_corr = basis_tables()
    pick_outer = selector(128, 128, lambda k: k // ET * ET * ER + k % ET * ER + ER - 1, False)
    pick_inner = selector(128, 128, lambda k: k // ET * ET * ER + k % ET * ER, False)
    for chan in range(5):
        field = adj_ref[0, chan]
        left_ax_ref[chan] = compact_axial(sweep(field, left_corr, lambda i: (i,)), 0)
        right_ax_ref[chan] = compact_axial(sweep(field, right_corr, lambda i: (i,)), EA - 1)
        pick1 = lambda i: (slice(None), i)
        up_ref[chan] = compact_face(sweep(field, left_corr, pick1), 0)
        down_ref[chan] = compact_face(sweep(field, right_corr, pick1), ET - 1)
        pick2 = lambda i: (slice(None), slice(None), slice(i, i + 1))
        outer = sweep(field, right_corr, pick2)
        inner = sweep(field, left_corr, pick2)
        for axial in range(4):
            for azim in range(4):
                row = axial * 4 + azim
                scratch_ref[0, row : row + 1] = outer[axial, azim]
                scratch_ref[1, row : row + 1] = inner[axial, azim]
        outer_ref[chan] = exact_dot(scratch_ref[0], pick_outer)
        inner_ref[chan] = exact_dot(scratch_ref[1], pick_inner)


def rate_kernel(
    adj_ref, flow_ref, up_ax_ref, down_ax_ref, up_az_ref, down_az_ref, outer_ref, inner_ref,
    rate_ref, next_ref,
):
    derivs, left_vals, right_vals, left_corr, right_corr = basis_tables()
    shape = (4, 4, 4, 128)
    lane = lax.broadcasted_iota(jnp.int32, shape, 3)
    flat_lane = lax.broadcasted_iota(jnp.int32, (4, 4, 128), 2)
    az_flat = flat_lane // ER % ET
    radial_lane = lane % ER
    brackets = [[None] * 5 for _ in range(3)]
    spread = selector(128, 128, lambda k: k // (ET * ER) * ET + k // ER % ET, True)
    for chan in range(5):
        field = adj_ref[0, chan]
        outer_lanes = exact_dot(outer_ref[chan], spread)
        inner_lanes = exact_dot(inner_ref[chan], spread)
        outer_face = jnp.stack(
            [
                jnp.stack(
                    [jnp.broadcast_to(outer_lanes[axial * 4 + azim : axial * 4 + azim + 1], (4, 128)) for azim in range(4)],
                    axis=0,
                )
                for axial in range(4)
            ],
            axis=0,
        )
        inner_face = jnp.stack(
            [
                jnp.stack(
                    [jnp.broadcast_to(inner_lanes[axial * 4 + azim : axial * 4 + azim + 1], (4, 128)) for azim in range(4)],
                    axis=0,
                )
                for axial in range(4)
            ],
            axis=0,
        )
        up_az = expand_face(up_az_ref[chan], 0)
        down_az = expand_face(down_az_ref[chan], ET - 1)
        left0 = sweep(field, left_corr, lambda i: (i,))
        right0 = sweep(field, right_corr, lambda i: (i,))
        next0 = lane_roll(jnp.where(flat_lane < ET * ER, expand_axial(up_ax_ref[chan], 0), left0), -ET * ER)
        prev0 = lane_roll(jnp.where(flat_lane >= (EA - 1) * ET * ER, expand_axial(down_ax_ref[chan], EA - 1), right0), ET * ER)
        jump_r = 0.5 * (next0 - right0)
        jump_l = 0.5 * (prev0 - left0)
        slabs = []
        for target in range(4):
            slab = sweep(field, [derivs[i][target] for i in range(4)], lambda i: (i,))
            slabs.append(slab + jump_r * float(right_vals[target]) + jump_l * float(left_vals[target]))
        brackets[0][chan] = jnp.stack(slabs, axis=0)
        pick1 = lambda i: (slice(None), i)
        left1 = sweep(field, left_corr, pick1)
        right1 = sweep(field, right_corr, pick1)
        next1 = lane_roll(
            jnp.where(az_flat == 0, lane_roll(up_az, ET * ER), left1), -ER
        )
        prev1 = lane_roll(
            jnp.where(az_flat == ET - 1, lane_roll(down_az, -ET * ER), right1), ER
        )
        jump_r = 0.5 * (next1 - right1)
        jump_l = 0.5 * (prev1 - left1)
        slabs = []
        for target in range(4):
            slab = sweep(field, [derivs[i][target] for i in range(4)], pick1)
            slabs.append(slab + jump_r * float(right_vals[target]) + jump_l * float(left_vals[target]))
        brackets[1][chan] = jnp.stack(slabs, axis=1)
        points = [jnp.broadcast_to(field[:, :, i : i + 1, :], shape) for i in range(4)]
        left2 = sweep(points, left_corr, lambda i: i)
        right2 = sweep(points, right_corr, lambda i: i)
        next2 = jnp.where(radial_lane == ER - 1, outer_face, lane_roll(left2, -1))
        prev2 = jnp.where(radial_lane == 0, inner_face, lane_roll(right2, 1))
        bracket = 0.5 * (next2 - right2) * column(right_vals, shape)
        bracket = bracket + 0.5 * (prev2 - left2) * column(left_vals, shape)
        for source in range(4):
            bracket = bracket + points[source] * column(derivs[source], shape)
        brackets[2][chan] = bracket
    prim = [flow_ref[0, chan].astype(jnp.float32) for chan in range(5)]
    density = prim[0]
    speed_sq = prim[1] * prim[1] + prim[2] * prim[2] + prim[3] * prim[3]
    energy = prim[4] / (GAMMA - 1.0) + 0.5 * density * speed_sq
    momentum = [density * prim[1 + k] for k in range(3)]
    velocity = [momentum[k] / density for k in range(3)]
    kinetic = momentum[0] * velocity[0] + momentum[1] * velocity[1] + momentum[2] * velocity[2]
    pressure = (GAMMA - 1.0) * (energy - 0.5 * kinetic)
    enthalpy = (energy + pressure) / density
    vel_sq = velocity[0] * velocity[0] + velocity[1] * velocity[1] + velocity[2] * velocity[2]
    grad = [None] * 5
    for direction in range(3):
        cot = brackets[direction]
        normal = velocity[direction]
        dotted = cot[1] * velocity[0] + cot[2] * velocity[1] + cot[3] * velocity[2] + cot[4] * enthalpy
        weight = cot[1 + direction] + cot[4] * normal
        terms = [
            0.5 * (GAMMA - 1.0) * vel_sq * weight - dotted * normal,
            None,
            None,
            None,
            (GAMMA - 1.0) * weight + cot[4] * normal,
        ]
        for k in range(3):
            term = cot[1 + k] * normal - (GAMMA - 1.0) * weight * velocity[k]
            if k == direction:
                term = term + (cot[0] + dotted)
            terms[1 + k] = term
        for chan in range(5):
            grad[chan] = terms[chan] if grad[chan] is None else grad[chan] + terms[chan]
    for chan in range(5):
        rate = -METRIC * grad[chan]
        rate_ref[0, chan] = rate
        next_ref[0, chan] = adj_ref[0, chan] + SECTION_STEP * rate


def local(adjoint, flow_prim, intersection_shift, weight_index, mortar_weights, sector_offset):
    n_axial = lax.axis_size("axial")
    n_azim = lax.axis_size("azim")
    face4 = jax.ShapeDtypeStruct((5, 4, 4, 128), jnp.float32)
    chunk = jax.ShapeDtypeStruct((5, 4, 128), jnp.float32)
    rows16 = jax.ShapeDtypeStruct((5, 16, 128), jnp.float32)
    left_ax, right_ax, upper_face, lower_face, outer_moment, inner_moment = pl.pallas_call(
        moment_kernel,
        out_shape=(chunk, chunk, chunk, chunk, rows16, rows16),
        scratch_shapes=[pltpu.VMEM((2, 16, 128), jnp.float32)],
    )(adjoint)
    is_rotor = lax.axis_index("zone") == 0
    own_face = jnp.where(is_rotor, outer_moment, inner_moment)[:, :, : EA * ET]
    own_rows = own_face.reshape(5, 4, 4, EA, ET).transpose(0, 3, 1, 4, 2).reshape(5, AP, TP)
    shifts_local = intersection_shift.reshape(INTERSECTIONS, AP, TP)
    table_match = weight_index[:, :, None] == jnp.arange(NW, dtype=jnp.int32)[None, None, :]
    weights_local = jnp.sum(
        jnp.where(table_match, mortar_weights[None, None, :], 0.0), axis=2
    ).reshape(INTERSECTIONS, AP, TP)
    offset = sector_offset[0]
    turn = (offset + TP // 2) // TP
    residue = offset - turn * TP
    offsets_k = residue + shifts_local
    coefs = []
    for rel in range(-TP, TP - 1):
        coef = jnp.where(offsets_k[0] == rel, weights_local[0], 0.0)
        for member in range(1, INTERSECTIONS):
            coef = coef + jnp.where(offsets_k[member] == rel, weights_local[member], 0.0)
        coefs.append((rel, coef))
    contrib = None
    for rel, coef in coefs:
        term = jnp.pad(coef[None] * own_rows, ((0, 0), (0, 0), (TP + rel, TP - rel)))
        contrib = term if contrib is None else contrib + term
    zone = lax.axis_index("zone")
    axial = lax.axis_index("axial")
    azim = lax.axis_index("azim")
    group = n_axial * n_azim
    dest = jnp.arange(2 * group, dtype=jnp.int32)
    dest_zone = dest // group
    dest_axial = dest // n_azim % n_axial
    dest_azim = dest % n_azim
    gap = ((dest_azim - azim) % n_azim - turn) % n_azim
    gap = gap[:, None, None, None]
    pieces = jnp.where(
        gap == n_azim - 1,
        contrib[None, :, :, :TP],
        jnp.where(gap == 0, contrib[None, :, :, TP : 2 * TP], contrib[None, :, :, 2 * TP :]),
    )
    iface_out = jnp.where(is_rotor, jnp.broadcast_to(own_rows[None], pieces.shape), pieces)
    iface_out = jnp.pad(iface_out.reshape(2 * group, 5, 2, 128), ((0, 0), (0, 0), (0, 2), (0, 0)))
    same_zone = dest_zone == zone
    same_ring = same_zone & (dest_axial == axial)
    same_line = same_zone & (dest_azim == azim)
    to_prev = (same_ring & (dest_azim == (azim - 1) % n_azim))[:, None, None, None]
    to_next = (same_ring & (dest_azim == (azim + 1) % n_azim))[:, None, None, None]
    to_below = (same_line & (dest_axial == axial - 1))[:, None, None, None]
    to_above = (same_line & (dest_axial == axial + 1))[:, None, None, None]
    is_iface = ((dest_zone != zone) & (dest_axial == axial))[:, None, None, None]
    chunks = jnp.where(to_prev, upper_face[None], 0.0)
    chunks = jnp.where(to_next, lower_face[None], chunks)
    chunks = jnp.where(to_below, left_ax[None], chunks)
    chunks = jnp.where(to_above, right_ax[None], chunks)
    chunks = jnp.where(is_iface, iface_out, chunks)
    got = lax.all_to_all(chunks, ("zone", "axial", "azim"), 0, 0)
    ring = (zone * n_axial + axial) * n_azim
    base = ((1 - zone) * n_axial + axial) * n_azim
    up_az = lax.dynamic_index_in_dim(got, ring + (azim + 1) % n_azim, 0, keepdims=False)
    down_az = lax.dynamic_index_in_dim(got, ring + (azim - 1) % n_azim, 0, keepdims=False)
    above = jnp.minimum(axial + 1, n_axial - 1)
    below = jnp.maximum(axial - 1, 0)
    up_ax = lax.dynamic_index_in_dim(got, (zone * n_axial + above) * n_azim + azim, 0, keepdims=False)
    down_ax = lax.dynamic_index_in_dim(got, (zone * n_axial + below) * n_azim + azim, 0, keepdims=False)
    up_ax = jnp.where(axial + 1 < n_axial, up_ax, 0.0)
    down_ax = jnp.where(axial > 0, down_ax, 0.0)
    direction = jnp.where(is_rotor, -1, 1)
    picked = [
        lax.dynamic_index_in_dim(
            got, base + (azim + direction * (turn + step)) % n_azim, 0, keepdims=False
        )[:, :2].reshape(5, AP, TP)
        for step in (-1, 0, 1)
    ]
    returned = picked[0] + picked[1] + picked[2]
    window = jnp.concatenate(picked, axis=2)
    incoming = shift_sum(window, coefs, TP)
    def to_lanes(rows_vals):
        face = rows_vals.reshape(5, EA, 4, ET, 4).transpose(0, 2, 4, 1, 3).reshape(5, 16, EA * ET)
        return jnp.pad(face, ((0, 0), (0, 0), (0, 128 - EA * ET)))

    outer = to_lanes(jnp.where(is_rotor, returned, 0.0))
    inner = to_lanes(jnp.where(is_rotor, 0.0, incoming))
    field_shape = jax.ShapeDtypeStruct(adjoint.shape, jnp.float32)
    adjoint_rate, next_adjoint = pl.pallas_call(
        rate_kernel, out_shape=(field_shape, field_shape)
    )(adjoint, flow_prim, up_ax, down_ax, up_az, down_az, outer, inner)
    return (adjoint_rate, next_adjoint)


def solution(mesh):
    placed = (
        P("zone", None, None, None, None, ("axial", "azim")),
        P("zone", None, None, None, None, ("axial", "azim")),
        P(None, ("axial", "azim")),
        P(None, ("axial", "azim")),
        P(),
        P(),
    )
    return jax.shard_map(
        local,
        mesh=mesh,
        in_specs=placed,
        out_specs=(
            P("zone", None, None, None, None, ("axial", "azim")),
            P("zone", None, None, None, None, ("axial", "azim")),
        ),
        check_vma=False,
    )
```

```python
import math

import jax
import jax.numpy as jnp
from jax import lax
from jax.experimental import pallas as pl
from jax.experimental.pallas import tpu as pltpu
from jax.sharding import PartitionSpec as P

EA = 4
ET = 4
ER = 8
INTERSECTIONS = 4
NW = 128
AP = 16
TP = 16


GAMMA = 1.4
METRIC = 0.1
SECTION_STEP = 0.5


def gauss_nodes():
    root_term = math.sqrt(6.0 / 5.0)
    inner_node = math.sqrt(3.0 / 7.0 - 2.0 / 7.0 * root_term)
    outer_node = math.sqrt(3.0 / 7.0 + 2.0 / 7.0 * root_term)
    return [-outer_node, -inner_node, inner_node, outer_node]


def lagrange_value(node_list, column, position):
    result = 1.0
    for factor_index in range(4):
        if factor_index != column:
            result = (
                result
                * (position - node_list[factor_index])
                / (node_list[column] - node_list[factor_index])
            )
    return result


def lagrange_slope(node_list, column, position):
    total = 0.0
    for skipped in range(4):
        if skipped == column:
            continue
        term = 1.0 / (node_list[column] - node_list[skipped])
        for factor_index in range(4):
            if factor_index != column and factor_index != skipped:
                term = (
                    term
                    * (position - node_list[factor_index])
                    / (node_list[column] - node_list[factor_index])
                )
        total = total + term
    return total


def basis_tables():
    node_list = gauss_nodes()
    derivs = [
        [lagrange_slope(node_list, column, node_list[source]) for column in range(4)]
        for source in range(4)
    ]
    left_vals = [lagrange_value(node_list, column, -1.0) for column in range(4)]
    right_vals = [lagrange_value(node_list, column, 1.0) for column in range(4)]
    third_slope = [(15.0 * value * value - 3.0) / 2.0 for value in node_list]
    fourth_slope = [(35.0 * value**3 - 15.0 * value) / 2.0 for value in node_list]
    left_corr = [-0.5 * (third_slope[source] - fourth_slope[source]) for source in range(4)]
    right_corr = [0.5 * (third_slope[source] + fourth_slope[source]) for source in range(4)]
    return (derivs, left_vals, right_vals, left_corr, right_corr)


def apply_points(adj_field, matrix, point_dim):
    slab_list = [
        lax.index_in_dim(adj_field, source, point_dim, keepdims=False) for source in range(4)
    ]
    outputs = []
    for target in range(4):
        running = slab_list[0] * float(matrix[0][target])
        for source in range(1, 4):
            running = running + slab_list[source] * float(matrix[source][target])
        outputs.append(running)
    return jnp.stack(outputs, axis=point_dim)


def face_moment(adj_field, vector, point_dim):
    running = lax.index_in_dim(adj_field, 0, point_dim, keepdims=False) * float(vector[0])
    for source in range(1, 4):
        running = running + lax.index_in_dim(adj_field, source, point_dim, keepdims=False) * float(
            vector[source]
        )
    return running


def lift_face(face_vals, vector, point_dim):
    return jnp.stack([face_vals * float(vector[target]) for target in range(4)], axis=point_dim)


def conserved(primitive):
    density = primitive[0]
    velocity = primitive[1:4]
    pressure = primitive[4]
    energy = pressure / (GAMMA - 1.0) + 0.5 * density * jnp.sum(velocity * velocity, axis=0)
    return jnp.concatenate([density[None], density[None] * velocity, energy[None]], axis=0)


def euler_flux(cons_state, direction):
    density = cons_state[0]
    momentum = cons_state[1:4]
    energy = cons_state[4]
    velocity = momentum / density[None]
    pressure = (GAMMA - 1.0) * (energy - 0.5 * jnp.sum(momentum * velocity, axis=0))
    normal_speed = velocity[direction]
    columns = [momentum[direction]]
    for component in range(3):
        if component == direction:
            columns.append(momentum[component] * normal_speed + pressure)
        else:
            columns.append(momentum[component] * normal_speed)
    columns.append((energy + pressure) * normal_speed)
    return jnp.stack(columns, axis=0)


def transpose_flux(cons_state, cotangent, direction):
    unused, pullback = jax.vjp(lambda current: euler_flux(current, direction), cons_state)
    return pullback(cotangent)[0]


def section_rate(adj_field, cons_state, left_moments, right_moments, next_left, prev_right):
    derivs, left_vals, right_vals, left_corr, right_corr = basis_tables()
    rate_sum = jnp.zeros_like(adj_field)
    for direction in range(3):
        point_dim = 1 + direction
        bracket = apply_points(adj_field, derivs, point_dim)
        bracket = bracket + 0.5 * lift_face(
            next_left[direction] - right_moments[direction], right_vals, point_dim
        )
        bracket = bracket + 0.5 * lift_face(
            prev_right[direction] - left_moments[direction], left_vals, point_dim
        )
        rate_sum = rate_sum - METRIC * transpose_flux(cons_state, bracket, direction)
    return rate_sum


def all_moments(adj_field):
    derivs, left_vals, right_vals, left_corr, right_corr = basis_tables()
    left_moments = [face_moment(adj_field, left_corr, 1 + direction) for direction in range(3)]
    right_moments = [face_moment(adj_field, right_corr, 1 + direction) for direction in range(3)]
    return (left_moments, right_moments)


def faces_to_rows(face_vals):
    axial_elems = face_vals.shape[3]
    azim_elems = face_vals.shape[4]
    return face_vals.transpose(0, 3, 1, 4, 2).reshape(5, 4 * axial_elems, 4 * azim_elems)


def rows_to_face(rows_vals, axial_elems, azim_elems):
    return rows_vals.reshape(5, axial_elems, 4, azim_elems, 4).transpose(0, 2, 4, 1, 3)


def shift_sum(window, coefs, lo):
    total = None
    for offset, coef in coefs:
        term = coef[None] * window[:, :, lo + offset : lo + offset + TP]
        total = term if total is None else total + term
    return total


def lane_roll(value, shift):
    return pltpu.roll(value, shift % 128, value.ndim - 1)


def sweep(field, weights, pick):
    total = field[pick(0)] * float(weights[0])
    for source in range(1, 4):
        total = total + field[pick(source)] * float(weights[source])
    return total


def column(values, shape):
    rows = lax.broadcasted_iota(jnp.int32, shape, 2)
    out = jnp.full(shape, float(values[3]), jnp.float32)
    for index in range(3):
        out = jnp.where(rows == index, float(values[index]), out)
    return out


def compact_face(face, part):
    lane = lax.broadcasted_iota(jnp.int32, (4, 128), 1)
    out = jnp.zeros((4, 128), jnp.float32)
    for block in range(4):
        for group in range(EA):
            shift = block * ET * ER - group * (ET - 1) * ER - part * ER
            start = block * ET * ER + group * ER
            mask = (lane >= start) & (lane < start + ER)
            out = jnp.where(mask, lane_roll(face[block], shift), out)
    return out


def expand_face(chunk, part):
    lane = lax.broadcasted_iota(jnp.int32, (4, 128), 1)
    group_of = lane // (ET * ER)
    in_part = lane // ER % ET == part
    blocks = []
    for block in range(4):
        out = jnp.zeros((4, 128), jnp.float32)
        for group in range(EA):
            shift = block * ET * ER - group * (ET - 1) * ER - part * ER
            out = jnp.where(in_part & (group_of == group), lane_roll(chunk, -shift), out)
        blocks.append(out)
    return jnp.stack(blocks, axis=0)


def selector(rows, cols, lane_of, use_rows):
    row = lax.broadcasted_iota(jnp.int32, (rows, cols), 0)
    col = lax.broadcasted_iota(jnp.int32, (rows, cols), 1)
    if use_rows:
        hit = (row == lane_of(col)) & (row < EA * ET)
    else:
        hit = (row == lane_of(col)) & (col < EA * ET)
    return jnp.where(hit, 1.0, 0.0)


def exact_dot(left, right):
    return jnp.dot(left, right, precision=lax.Precision.HIGHEST, preferred_element_type=jnp.float32)


def moment_kernel(adj_ref, left_ax_ref, right_ax_ref, up_ref, down_ref, outer_ref, inner_ref, scratch_ref):
    derivs, left_vals, right_vals, left_corr, right_corr = basis_tables()
    pick_outer = selector(128, 128, lambda k: k // ET * ET * ER + k % ET * ER + ER - 1, False)
    pick_inner = selector(128, 128, lambda k: k // ET * ET * ER + k % ET * ER, False)
    for chan in range(5):
        field = adj_ref[0, chan]
        left_ax_ref[chan] = sweep(field, left_corr, lambda i: (i,))
        right_ax_ref[chan] = sweep(field, right_corr, lambda i: (i,))
        pick1 = lambda i: (slice(None), i)
        up_ref[chan] = compact_face(sweep(field, left_corr, pick1), 0)
        down_ref[chan] = compact_face(sweep(field, right_corr, pick1), ET - 1)
        pick2 = lambda i: (slice(None), slice(None), slice(i, i + 1))
        outer = sweep(field, right_corr, pick2)
        inner = sweep(field, left_corr, pick2)
        for axial in range(4):
            for azim in range(4):
                row = axial * 4 + azim
                scratch_ref[0, row : row + 1] = outer[axial, azim]
                scratch_ref[1, row : row + 1] = inner[axial, azim]
        outer_ref[chan] = exact_dot(scratch_ref[0], pick_outer)
        inner_ref[chan] = exact_dot(scratch_ref[1], pick_inner)


def rate_kernel(
    adj_ref, flow_ref, up_ax_ref, down_ax_ref, up_az_ref, down_az_ref, outer_ref, inner_ref,
    rate_ref, next_ref,
):
    derivs, left_vals, right_vals, left_corr, right_corr = basis_tables()
    shape = (4, 4, 4, 128)
    lane = lax.broadcasted_iota(jnp.int32, shape, 3)
    flat_lane = lax.broadcasted_iota(jnp.int32, (4, 4, 128), 2)
    az_flat = flat_lane // ER % ET
    radial_lane = lane % ER
    brackets = [[None] * 5 for _ in range(3)]
    spread = selector(128, 128, lambda k: k // (ET * ER) * ET + k // ER % ET, True)
    for chan in range(5):
        field = adj_ref[0, chan]
        outer_lanes = exact_dot(outer_ref[chan], spread)
        inner_lanes = exact_dot(inner_ref[chan], spread)
        outer_face = jnp.stack(
            [
                jnp.stack(
                    [jnp.broadcast_to(outer_lanes[axial * 4 + azim : axial * 4 + azim + 1], (4, 128)) for azim in range(4)],
                    axis=0,
                )
                for axial in range(4)
            ],
            axis=0,
        )
        inner_face = jnp.stack(
            [
                jnp.stack(
                    [jnp.broadcast_to(inner_lanes[axial * 4 + azim : axial * 4 + azim + 1], (4, 128)) for azim in range(4)],
                    axis=0,
                )
                for axial in range(4)
            ],
            axis=0,
        )
        up_az = expand_face(up_az_ref[chan], 0)
        down_az = expand_face(down_az_ref[chan], ET - 1)
        left0 = sweep(field, left_corr, lambda i: (i,))
        right0 = sweep(field, right_corr, lambda i: (i,))
        next0 = lane_roll(jnp.where(flat_lane < ET * ER, up_ax_ref[chan], left0), -ET * ER)
        prev0 = lane_roll(jnp.where(flat_lane >= (EA - 1) * ET * ER, down_ax_ref[chan], right0), ET * ER)
        jump_r = 0.5 * (next0 - right0)
        jump_l = 0.5 * (prev0 - left0)
        slabs = []
        for target in range(4):
            slab = sweep(field, [derivs[i][target] for i in range(4)], lambda i: (i,))
            slabs.append(slab + jump_r * float(right_vals[target]) + jump_l * float(left_vals[target]))
        brackets[0][chan] = jnp.stack(slabs, axis=0)
        pick1 = lambda i: (slice(None), i)
        left1 = sweep(field, left_corr, pick1)
        right1 = sweep(field, right_corr, pick1)
        next1 = lane_roll(
            jnp.where(az_flat == 0, lane_roll(up_az, ET * ER), left1), -ER
        )
        prev1 = lane_roll(
            jnp.where(az_flat == ET - 1, lane_roll(down_az, -ET * ER), right1), ER
        )
        jump_r = 0.5 * (next1 - right1)
        jump_l = 0.5 * (prev1 - left1)
        slabs = []
        for target in range(4):
            slab = sweep(field, [derivs[i][target] for i in range(4)], pick1)
            slabs.append(slab + jump_r * float(right_vals[target]) + jump_l * float(left_vals[target]))
        brackets[1][chan] = jnp.stack(slabs, axis=1)
        points = [jnp.broadcast_to(field[:, :, i : i + 1, :], shape) for i in range(4)]
        left2 = sweep(points, left_corr, lambda i: i)
        right2 = sweep(points, right_corr, lambda i: i)
        next2 = jnp.where(radial_lane == ER - 1, outer_face, lane_roll(left2, -1))
        prev2 = jnp.where(radial_lane == 0, inner_face, lane_roll(right2, 1))
        bracket = 0.5 * (next2 - right2) * column(right_vals, shape)
        bracket = bracket + 0.5 * (prev2 - left2) * column(left_vals, shape)
        for source in range(4):
            bracket = bracket + points[source] * column(derivs[source], shape)
        brackets[2][chan] = bracket
    prim = [flow_ref[0, chan].astype(jnp.float32) for chan in range(5)]
    density = prim[0]
    speed_sq = prim[1] * prim[1] + prim[2] * prim[2] + prim[3] * prim[3]
    energy = prim[4] / (GAMMA - 1.0) + 0.5 * density * speed_sq
    momentum = [density * prim[1 + k] for k in range(3)]
    velocity = [momentum[k] / density for k in range(3)]
    kinetic = momentum[0] * velocity[0] + momentum[1] * velocity[1] + momentum[2] * velocity[2]
    pressure = (GAMMA - 1.0) * (energy - 0.5 * kinetic)
    enthalpy = (energy + pressure) / density
    vel_sq = velocity[0] * velocity[0] + velocity[1] * velocity[1] + velocity[2] * velocity[2]
    grad = [None] * 5
    for direction in range(3):
        cot = brackets[direction]
        normal = velocity[direction]
        dotted = cot[1] * velocity[0] + cot[2] * velocity[1] + cot[3] * velocity[2] + cot[4] * enthalpy
        weight = cot[1 + direction] + cot[4] * normal
        terms = [
            0.5 * (GAMMA - 1.0) * vel_sq * weight - dotted * normal,
            None,
            None,
            None,
            (GAMMA - 1.0) * weight + cot[4] * normal,
        ]
        for k in range(3):
            term = cot[1 + k] * normal - (GAMMA - 1.0) * weight * velocity[k]
            if k == direction:
                term = term + (cot[0] + dotted)
            terms[1 + k] = term
        for chan in range(5):
            grad[chan] = terms[chan] if grad[chan] is None else grad[chan] + terms[chan]
    for chan in range(5):
        rate = -METRIC * grad[chan]
        rate_ref[0, chan] = rate
        next_ref[0, chan] = adj_ref[0, chan] + SECTION_STEP * rate


def local(adjoint, flow_prim, intersection_shift, weight_index, mortar_weights, sector_offset):
    n_axial = lax.axis_size("axial")
    n_azim = lax.axis_size("azim")
    face4 = jax.ShapeDtypeStruct((5, 4, 4, 128), jnp.float32)
    chunk = jax.ShapeDtypeStruct((5, 4, 128), jnp.float32)
    rows16 = jax.ShapeDtypeStruct((5, 16, 128), jnp.float32)
    left_ax, right_ax, upper_face, lower_face, outer_moment, inner_moment = pl.pallas_call(
        moment_kernel,
        out_shape=(face4, face4, chunk, chunk, rows16, rows16),
        scratch_shapes=[pltpu.VMEM((2, 16, 128), jnp.float32)],
    )(adjoint)
    is_rotor = lax.axis_index("zone") == 0
    up_ax = lax.ppermute(left_ax, "axial", [(i + 1, i) for i in range(n_axial - 1)])
    down_ax = lax.ppermute(right_ax, "axial", [(i, i + 1) for i in range(n_axial - 1)])
    own_face = jnp.where(is_rotor, outer_moment, inner_moment)[:, :, : EA * ET]
    own_rows = own_face.reshape(5, 4, 4, EA, ET).transpose(0, 3, 1, 4, 2).reshape(5, AP, TP)
    shifts_local = intersection_shift.reshape(INTERSECTIONS, AP, TP)
    table_match = weight_index[:, :, None] == jnp.arange(NW, dtype=jnp.int32)[None, None, :]
    weights_local = jnp.sum(
        jnp.where(table_match, mortar_weights[None, None, :], 0.0), axis=2
    ).reshape(INTERSECTIONS, AP, TP)
    offset = sector_offset[0]
    turn = (offset + TP // 2) // TP
    residue = offset - turn * TP
    offsets_k = residue + shifts_local
    rel_all = jnp.arange(-TP, TP - 1, dtype=jnp.int32)[:, None, None]
    coef_all = jnp.where(offsets_k[0][None] == rel_all, weights_local[0][None], 0.0)
    for member in range(1, INTERSECTIONS):
        coef_all = coef_all + jnp.where(offsets_k[member][None] == rel_all, weights_local[member][None], 0.0)
    coefs = [(rel, coef_all[rel + TP]) for rel in range(-TP, TP - 1)]
    contrib = None
    for rel, coef in coefs:
        term = jnp.pad(coef[None] * own_rows, ((0, 0), (0, 0), (TP + rel, TP - rel)))
        contrib = term if contrib is None else contrib + term
    zone = lax.axis_index("zone")
    azim = lax.axis_index("azim")
    dest = jnp.arange(2 * n_azim, dtype=jnp.int32)
    dest_azim = dest % n_azim
    gap = ((dest_azim - azim) % n_azim - turn) % n_azim
    gap = gap[:, None, None, None]
    pieces = jnp.where(
        gap == n_azim - 1,
        contrib[None, :, :, :TP],
        jnp.where(gap == 0, contrib[None, :, :, TP : 2 * TP], contrib[None, :, :, 2 * TP :]),
    )
    iface_out = jnp.where(is_rotor, jnp.broadcast_to(own_rows[None], pieces.shape), pieces)
    iface_out = jnp.pad(iface_out.reshape(2 * n_azim, 5, 2, 128), ((0, 0), (0, 0), (0, 2), (0, 0)))
    same_zone = dest // n_azim == zone
    to_prev = (same_zone & (dest_azim == (azim - 1) % n_azim))[:, None, None, None]
    to_next = (same_zone & (dest_azim == (azim + 1) % n_azim))[:, None, None, None]
    chunks = jnp.where(
        to_prev, upper_face[None], jnp.where(to_next, lower_face[None], jnp.where(same_zone[:, None, None, None], 0.0, iface_out))
    )
    got = lax.all_to_all(chunks, ("zone", "azim"), 0, 0)
    base = (1 - zone) * n_azim
    up_az = lax.dynamic_index_in_dim(got, zone * n_azim + (azim + 1) % n_azim, 0, keepdims=False)
    down_az = lax.dynamic_index_in_dim(got, zone * n_azim + (azim - 1) % n_azim, 0, keepdims=False)
    direction = jnp.where(is_rotor, -1, 1)
    picked = [
        lax.dynamic_index_in_dim(
            got, base + (azim + direction * (turn + step)) % n_azim, 0, keepdims=False
        )[:, :2].reshape(5, AP, TP)
        for step in (-1, 0, 1)
    ]
    returned = picked[0] + picked[1] + picked[2]
    window = jnp.concatenate(picked, axis=2)
    incoming = shift_sum(window, coefs, TP)
    def to_lanes(rows_vals):
        face = rows_vals.reshape(5, EA, 4, ET, 4).transpose(0, 2, 4, 1, 3).reshape(5, 16, EA * ET)
        return jnp.pad(face, ((0, 0), (0, 0), (0, 128 - EA * ET)))

    outer = to_lanes(jnp.where(is_rotor, returned, 0.0))
    inner = to_lanes(jnp.where(is_rotor, 0.0, incoming))
    field_shape = jax.ShapeDtypeStruct(adjoint.shape, jnp.float32)
    adjoint_rate, next_adjoint = pl.pallas_call(
        rate_kernel, out_shape=(field_shape, field_shape)
    )(adjoint, flow_prim, up_ax, down_ax, up_az, down_az, outer, inner)
    return (adjoint_rate, next_adjoint)


def solution(mesh):
    placed = (
        P("zone", None, None, None, None, ("axial", "azim")),
        P("zone", None, None, None, None, ("axial", "azim")),
        P(None, ("axial", "azim")),
        P(None, ("axial", "azim")),
        P(),
        P(),
    )
    return jax.shard_map(
        local,
        mesh=mesh,
        in_specs=placed,
        out_specs=(
            P("zone", None, None, None, None, ("axial", "azim")),
            P("zone", None, None, None, None, ("axial", "azim")),
        ),
        check_vma=False,
    )
```

```python
import math

import jax
import jax.numpy as jnp
from jax import lax
from jax.experimental import pallas as pl
from jax.experimental.pallas import tpu as pltpu
from jax.sharding import PartitionSpec as P

EA = 4
ET = 4
ER = 8
INTERSECTIONS = 4
NW = 128
AP = 16
TP = 16


GAMMA = 1.4
METRIC = 0.1
SECTION_STEP = 0.5


def gauss_nodes():
    root_term = math.sqrt(6.0 / 5.0)
    inner_node = math.sqrt(3.0 / 7.0 - 2.0 / 7.0 * root_term)
    outer_node = math.sqrt(3.0 / 7.0 + 2.0 / 7.0 * root_term)
    return [-outer_node, -inner_node, inner_node, outer_node]


def lagrange_value(node_list, column, position):
    result = 1.0
    for factor_index in range(4):
        if factor_index != column:
            result = (
                result
                * (position - node_list[factor_index])
                / (node_list[column] - node_list[factor_index])
            )
    return result


def lagrange_slope(node_list, column, position):
    total = 0.0
    for skipped in range(4):
        if skipped == column:
            continue
        term = 1.0 / (node_list[column] - node_list[skipped])
        for factor_index in range(4):
            if factor_index != column and factor_index != skipped:
                term = (
                    term
                    * (position - node_list[factor_index])
                    / (node_list[column] - node_list[factor_index])
                )
        total = total + term
    return total


def basis_tables():
    node_list = gauss_nodes()
    derivs = [
        [lagrange_slope(node_list, column, node_list[source]) for column in range(4)]
        for source in range(4)
    ]
    left_vals = [lagrange_value(node_list, column, -1.0) for column in range(4)]
    right_vals = [lagrange_value(node_list, column, 1.0) for column in range(4)]
    third_slope = [(15.0 * value * value - 3.0) / 2.0 for value in node_list]
    fourth_slope = [(35.0 * value**3 - 15.0 * value) / 2.0 for value in node_list]
    left_corr = [-0.5 * (third_slope[source] - fourth_slope[source]) for source in range(4)]
    right_corr = [0.5 * (third_slope[source] + fourth_slope[source]) for source in range(4)]
    return (derivs, left_vals, right_vals, left_corr, right_corr)


def apply_points(adj_field, matrix, point_dim):
    slab_list = [
        lax.index_in_dim(adj_field, source, point_dim, keepdims=False) for source in range(4)
    ]
    outputs = []
    for target in range(4):
        running = slab_list[0] * float(matrix[0][target])
        for source in range(1, 4):
            running = running + slab_list[source] * float(matrix[source][target])
        outputs.append(running)
    return jnp.stack(outputs, axis=point_dim)


def face_moment(adj_field, vector, point_dim):
    running = lax.index_in_dim(adj_field, 0, point_dim, keepdims=False) * float(vector[0])
    for source in range(1, 4):
        running = running + lax.index_in_dim(adj_field, source, point_dim, keepdims=False) * float(
            vector[source]
        )
    return running


def lift_face(face_vals, vector, point_dim):
    return jnp.stack([face_vals * float(vector[target]) for target in range(4)], axis=point_dim)


def conserved(primitive):
    density = primitive[0]
    velocity = primitive[1:4]
    pressure = primitive[4]
    energy = pressure / (GAMMA - 1.0) + 0.5 * density * jnp.sum(velocity * velocity, axis=0)
    return jnp.concatenate([density[None], density[None] * velocity, energy[None]], axis=0)


def euler_flux(cons_state, direction):
    density = cons_state[0]
    momentum = cons_state[1:4]
    energy = cons_state[4]
    velocity = momentum / density[None]
    pressure = (GAMMA - 1.0) * (energy - 0.5 * jnp.sum(momentum * velocity, axis=0))
    normal_speed = velocity[direction]
    columns = [momentum[direction]]
    for component in range(3):
        if component == direction:
            columns.append(momentum[component] * normal_speed + pressure)
        else:
            columns.append(momentum[component] * normal_speed)
    columns.append((energy + pressure) * normal_speed)
    return jnp.stack(columns, axis=0)


def transpose_flux(cons_state, cotangent, direction):
    unused, pullback = jax.vjp(lambda current: euler_flux(current, direction), cons_state)
    return pullback(cotangent)[0]


def section_rate(adj_field, cons_state, left_moments, right_moments, next_left, prev_right):
    derivs, left_vals, right_vals, left_corr, right_corr = basis_tables()
    rate_sum = jnp.zeros_like(adj_field)
    for direction in range(3):
        point_dim = 1 + direction
        bracket = apply_points(adj_field, derivs, point_dim)
        bracket = bracket + 0.5 * lift_face(
            next_left[direction] - right_moments[direction], right_vals, point_dim
        )
        bracket = bracket + 0.5 * lift_face(
            prev_right[direction] - left_moments[direction], left_vals, point_dim
        )
        rate_sum = rate_sum - METRIC * transpose_flux(cons_state, bracket, direction)
    return rate_sum


def all_moments(adj_field):
    derivs, left_vals, right_vals, left_corr, right_corr = basis_tables()
    left_moments = [face_moment(adj_field, left_corr, 1 + direction) for direction in range(3)]
    right_moments = [face_moment(adj_field, right_corr, 1 + direction) for direction in range(3)]
    return (left_moments, right_moments)


def faces_to_rows(face_vals):
    axial_elems = face_vals.shape[3]
    azim_elems = face_vals.shape[4]
    return face_vals.transpose(0, 3, 1, 4, 2).reshape(5, 4 * axial_elems, 4 * azim_elems)


def rows_to_face(rows_vals, axial_elems, azim_elems):
    return rows_vals.reshape(5, axial_elems, 4, azim_elems, 4).transpose(0, 2, 4, 1, 3)


def shift_sum(window, coefs, lo):
    total = None
    for offset, coef in coefs:
        term = coef[None] * window[:, :, lo + offset : lo + offset + TP]
        total = term if total is None else total + term
    return total


def lane_roll(value, shift):
    return pltpu.roll(value, shift % 128, value.ndim - 1)


def sweep(field, weights, pick):
    total = field[pick(0)] * float(weights[0])
    for source in range(1, 4):
        total = total + field[pick(source)] * float(weights[source])
    return total


def column(values, shape):
    rows = lax.broadcasted_iota(jnp.int32, shape, 2)
    out = jnp.full(shape, float(values[3]), jnp.float32)
    for index in range(3):
        out = jnp.where(rows == index, float(values[index]), out)
    return out


def compact_face(face, part):
    lane = lax.broadcasted_iota(jnp.int32, (4, 128), 1)
    out = jnp.zeros((4, 128), jnp.float32)
    for block in range(4):
        for group in range(EA):
            shift = block * ET * ER - group * (ET - 1) * ER - part * ER
            start = block * ET * ER + group * ER
            mask = (lane >= start) & (lane < start + ER)
            out = jnp.where(mask, lane_roll(face[block], shift), out)
    return out


def expand_face(chunk, part):
    lane = lax.broadcasted_iota(jnp.int32, (4, 128), 1)
    group_of = lane // (ET * ER)
    in_part = lane // ER % ET == part
    blocks = []
    for block in range(4):
        out = jnp.zeros((4, 128), jnp.float32)
        for group in range(EA):
            shift = block * ET * ER - group * (ET - 1) * ER - part * ER
            out = jnp.where(in_part & (group_of == group), lane_roll(chunk, -shift), out)
        blocks.append(out)
    return jnp.stack(blocks, axis=0)


def selector(rows, cols, lane_of, use_rows):
    row = lax.broadcasted_iota(jnp.int32, (rows, cols), 0)
    col = lax.broadcasted_iota(jnp.int32, (rows, cols), 1)
    if use_rows:
        hit = (row == lane_of(col)) & (row < EA * ET)
    else:
        hit = (row == lane_of(col)) & (col < EA * ET)
    return jnp.where(hit, 1.0, 0.0)


def exact_dot(left, right):
    return jnp.dot(left, right, precision=lax.Precision.HIGHEST, preferred_element_type=jnp.float32)


def moment_kernel(adj_ref, left_ax_ref, right_ax_ref, up_ref, down_ref, outer_ref, inner_ref, scratch_ref):
    derivs, left_vals, right_vals, left_corr, right_corr = basis_tables()
    pick_outer = selector(128, 128, lambda k: k // ET * ET * ER + k % ET * ER + ER - 1, False)
    pick_inner = selector(128, 128, lambda k: k // ET * ET * ER + k % ET * ER, False)
    for chan in range(5):
        field = adj_ref[0, chan]
        left_ax_ref[chan] = sweep(field, left_corr, lambda i: (i,))
        right_ax_ref[chan] = sweep(field, right_corr, lambda i: (i,))
        pick1 = lambda i: (slice(None), i)
        up_ref[chan] = compact_face(sweep(field, left_corr, pick1), 0)
        down_ref[chan] = compact_face(sweep(field, right_corr, pick1), ET - 1)
        pick2 = lambda i: (slice(None), slice(None), slice(i, i + 1))
        outer = sweep(field, right_corr, pick2)
        inner = sweep(field, left_corr, pick2)
        for axial in range(4):
            for azim in range(4):
                row = axial * 4 + azim
                scratch_ref[0, row : row + 1] = outer[axial, azim]
                scratch_ref[1, row : row + 1] = inner[axial, azim]
        outer_ref[chan] = exact_dot(scratch_ref[0], pick_outer)
        inner_ref[chan] = exact_dot(scratch_ref[1], pick_inner)


def rate_kernel(
    adj_ref, flow_ref, up_ax_ref, down_ax_ref, up_az_ref, down_az_ref, sides_ref,
    rate_ref, next_ref,
):
    derivs, left_vals, right_vals, left_corr, right_corr = basis_tables()
    shape = (4, 4, 4, 128)
    lane = lax.broadcasted_iota(jnp.int32, shape, 3)
    flat_lane = lax.broadcasted_iota(jnp.int32, (4, 4, 128), 2)
    az_flat = flat_lane // ER % ET
    radial_lane = lane % ER
    brackets = [[None] * 5 for _ in range(3)]
    col = lax.broadcasted_iota(jnp.int32, (16, 128), 1)
    row = lax.broadcasted_iota(jnp.int32, (16, 128), 0)
    sides = sides_ref[...]
    spread = [
        exact_dot(sides, jnp.where(row == col // ER % ET * 4 + azim, 1.0, 0.0)) for azim in range(4)
    ]
    group = lax.broadcasted_iota(jnp.int32, (1, 128), 1) // (ET * ER)

    def side_face(side, chan):
        blocks = []
        for axial in range(4):
            slabs = []
            for azim in range(4):
                base = (side * 5 + chan) * 16 + axial
                value = spread[azim][base : base + 1]
                for elem in range(1, EA):
                    pos = base + elem * 4
                    value = jnp.where(group == elem, spread[azim][pos : pos + 1], value)
                slabs.append(jnp.broadcast_to(value, (4, 128)))
            blocks.append(jnp.stack(slabs, axis=0))
        return jnp.stack(blocks, axis=0)

    for chan in range(5):
        field = adj_ref[0, chan]
        outer_face = side_face(0, chan)
        inner_face = side_face(1, chan)
        up_az = expand_face(up_az_ref[chan], 0)
        down_az = expand_face(down_az_ref[chan], ET - 1)
        left0 = sweep(field, left_corr, lambda i: (i,))
        right0 = sweep(field, right_corr, lambda i: (i,))
        next0 = lane_roll(jnp.where(flat_lane < ET * ER, up_ax_ref[chan], left0), -ET * ER)
        prev0 = lane_roll(jnp.where(flat_lane >= (EA - 1) * ET * ER, down_ax_ref[chan], right0), ET * ER)
        jump_r = 0.5 * (next0 - right0)
        jump_l = 0.5 * (prev0 - left0)
        slabs = []
        for target in range(4):
            slab = sweep(field, [derivs[i][target] for i in range(4)], lambda i: (i,))
            slabs.append(slab + jump_r * float(right_vals[target]) + jump_l * float(left_vals[target]))
        brackets[0][chan] = jnp.stack(slabs, axis=0)
        pick1 = lambda i: (slice(None), i)
        left1 = sweep(field, left_corr, pick1)
        right1 = sweep(field, right_corr, pick1)
        next1 = lane_roll(
            jnp.where(az_flat == 0, lane_roll(up_az, ET * ER), left1), -ER
        )
        prev1 = lane_roll(
            jnp.where(az_flat == ET - 1, lane_roll(down_az, -ET * ER), right1), ER
        )
        jump_r = 0.5 * (next1 - right1)
        jump_l = 0.5 * (prev1 - left1)
        slabs = []
        for target in range(4):
            slab = sweep(field, [derivs[i][target] for i in range(4)], pick1)
            slabs.append(slab + jump_r * float(right_vals[target]) + jump_l * float(left_vals[target]))
        brackets[1][chan] = jnp.stack(slabs, axis=1)
        points = [jnp.broadcast_to(field[:, :, i : i + 1, :], shape) for i in range(4)]
        left2 = sweep(points, left_corr, lambda i: i)
        right2 = sweep(points, right_corr, lambda i: i)
        next2 = jnp.where(radial_lane == ER - 1, outer_face, lane_roll(left2, -1))
        prev2 = jnp.where(radial_lane == 0, inner_face, lane_roll(right2, 1))
        bracket = 0.5 * (next2 - right2) * column(right_vals, shape)
        bracket = bracket + 0.5 * (prev2 - left2) * column(left_vals, shape)
        for source in range(4):
            bracket = bracket + points[source] * column(derivs[source], shape)
        brackets[2][chan] = bracket
    prim = [flow_ref[0, chan].astype(jnp.float32) for chan in range(5)]
    density = prim[0]
    speed_sq = prim[1] * prim[1] + prim[2] * prim[2] + prim[3] * prim[3]
    energy = prim[4] / (GAMMA - 1.0) + 0.5 * density * speed_sq
    momentum = [density * prim[1 + k] for k in range(3)]
    velocity = [momentum[k] / density for k in range(3)]
    kinetic = momentum[0] * velocity[0] + momentum[1] * velocity[1] + momentum[2] * velocity[2]
    pressure = (GAMMA - 1.0) * (energy - 0.5 * kinetic)
    enthalpy = (energy + pressure) / density
    vel_sq = velocity[0] * velocity[0] + velocity[1] * velocity[1] + velocity[2] * velocity[2]
    grad = [None] * 5
    for direction in range(3):
        cot = brackets[direction]
        normal = velocity[direction]
        dotted = cot[1] * velocity[0] + cot[2] * velocity[1] + cot[3] * velocity[2] + cot[4] * enthalpy
        weight = cot[1 + direction] + cot[4] * normal
        terms = [
            0.5 * (GAMMA - 1.0) * vel_sq * weight - dotted * normal,
            None,
            None,
            None,
            (GAMMA - 1.0) * weight + cot[4] * normal,
        ]
        for k in range(3):
            term = cot[1 + k] * normal - (GAMMA - 1.0) * weight * velocity[k]
            if k == direction:
                term = term + (cot[0] + dotted)
            terms[1 + k] = term
        for chan in range(5):
            grad[chan] = terms[chan] if grad[chan] is None else grad[chan] + terms[chan]
    for chan in range(5):
        rate = -METRIC * grad[chan]
        rate_ref[0, chan] = rate
        next_ref[0, chan] = adj_ref[0, chan] + SECTION_STEP * rate


def local(adjoint, flow_prim, intersection_shift, weight_index, mortar_weights, sector_offset):
    n_axial = lax.axis_size("axial")
    n_azim = lax.axis_size("azim")
    face4 = jax.ShapeDtypeStruct((5, 4, 4, 128), jnp.float32)
    chunk = jax.ShapeDtypeStruct((5, 4, 128), jnp.float32)
    rows16 = jax.ShapeDtypeStruct((5, 16, 128), jnp.float32)
    left_ax, right_ax, upper_face, lower_face, outer_moment, inner_moment = pl.pallas_call(
        moment_kernel,
        out_shape=(face4, face4, chunk, chunk, rows16, rows16),
        scratch_shapes=[pltpu.VMEM((2, 16, 128), jnp.float32)],
    )(adjoint)
    is_rotor = lax.axis_index("zone") == 0
    up_ax = lax.ppermute(left_ax, "axial", [(i + 1, i) for i in range(n_axial - 1)])
    down_ax = lax.ppermute(right_ax, "axial", [(i, i + 1) for i in range(n_axial - 1)])
    own_face = jnp.where(is_rotor, outer_moment, inner_moment)[:, :, : EA * ET]
    own_rows = own_face.reshape(5, 4, 4, EA, ET).transpose(0, 3, 1, 4, 2).reshape(5, AP, TP)
    shifts_local = intersection_shift.reshape(INTERSECTIONS, AP, TP)
    table_match = weight_index[:, :, None] == jnp.arange(NW, dtype=jnp.int32)[None, None, :]
    weights_local = jnp.sum(
        jnp.where(table_match, mortar_weights[None, None, :], 0.0), axis=2
    ).reshape(INTERSECTIONS, AP, TP)
    offset = sector_offset[0]
    turn = (offset + TP // 2) // TP
    residue = offset - turn * TP
    offsets_k = residue + shifts_local
    rel_all = jnp.arange(-TP, TP - 1, dtype=jnp.int32)[:, None, None]
    coef_all = jnp.where(offsets_k[0][None] == rel_all, weights_local[0][None], 0.0)
    for member in range(1, INTERSECTIONS):
        coef_all = coef_all + jnp.where(offsets_k[member][None] == rel_all, weights_local[member][None], 0.0)
    coefs = [(rel, coef_all[rel + TP]) for rel in range(-TP, TP - 1)]
    contrib = None
    for rel, coef in coefs:
        term = jnp.pad(coef[None] * own_rows, ((0, 0), (0, 0), (TP + rel, TP - rel)))
        contrib = term if contrib is None else contrib + term
    zone = lax.axis_index("zone")
    azim = lax.axis_index("azim")
    dest = jnp.arange(2 * n_azim, dtype=jnp.int32)
    dest_azim = dest % n_azim
    gap = ((dest_azim - azim) % n_azim - turn) % n_azim
    gap = gap[:, None, None, None]
    pieces = jnp.where(
        gap == n_azim - 1,
        contrib[None, :, :, :TP],
        jnp.where(gap == 0, contrib[None, :, :, TP : 2 * TP], contrib[None, :, :, 2 * TP :]),
    )
    iface_out = jnp.where(is_rotor, jnp.broadcast_to(own_rows[None], pieces.shape), pieces)
    iface_out = jnp.pad(iface_out.reshape(2 * n_azim, 5, 2, 128), ((0, 0), (0, 0), (0, 2), (0, 0)))
    same_zone = dest // n_azim == zone
    to_prev = (same_zone & (dest_azim == (azim - 1) % n_azim))[:, None, None, None]
    to_next = (same_zone & (dest_azim == (azim + 1) % n_azim))[:, None, None, None]
    chunks = jnp.where(
        to_prev, upper_face[None], jnp.where(to_next, lower_face[None], jnp.where(same_zone[:, None, None, None], 0.0, iface_out))
    )
    got = lax.all_to_all(chunks, ("zone", "azim"), 0, 0)
    base = (1 - zone) * n_azim
    up_az = lax.dynamic_index_in_dim(got, zone * n_azim + (azim + 1) % n_azim, 0, keepdims=False)
    down_az = lax.dynamic_index_in_dim(got, zone * n_azim + (azim - 1) % n_azim, 0, keepdims=False)
    direction = jnp.where(is_rotor, -1, 1)
    picked = [
        lax.dynamic_index_in_dim(
            got, base + (azim + direction * (turn + step)) % n_azim, 0, keepdims=False
        )[:, :2].reshape(5, AP, TP)
        for step in (-1, 0, 1)
    ]
    returned = picked[0] + picked[1] + picked[2]
    window = jnp.concatenate(picked, axis=2)
    incoming = shift_sum(window, coefs, TP)
    sides = jnp.concatenate(
        [jnp.where(is_rotor, returned, 0.0), jnp.where(is_rotor, 0.0, incoming)], axis=0
    ).reshape(10 * AP, TP)
    field_shape = jax.ShapeDtypeStruct(adjoint.shape, jnp.float32)
    adjoint_rate, next_adjoint = pl.pallas_call(
        rate_kernel, out_shape=(field_shape, field_shape)
    )(adjoint, flow_prim, up_ax, down_ax, up_az, down_az, sides)
    return (adjoint_rate, next_adjoint)


def solution(mesh):
    placed = (
        P("zone", None, None, None, None, ("axial", "azim")),
        P("zone", None, None, None, None, ("axial", "azim")),
        P(None, ("axial", "azim")),
        P(None, ("axial", "azim")),
        P(),
        P(),
    )
    return jax.shard_map(
        local,
        mesh=mesh,
        in_specs=placed,
        out_specs=(
            P("zone", None, None, None, None, ("axial", "azim")),
            P("zone", None, None, None, None, ("axial", "azim")),
        ),
        check_vma=False,
    )
```

```python
import math

import jax
import jax.numpy as jnp
from jax import lax
from jax.experimental import pallas as pl
from jax.experimental.pallas import tpu as pltpu
from jax.sharding import PartitionSpec as P

EA = 4
ET = 4
ER = 8
INTERSECTIONS = 4
NW = 128
AP = 16
TP = 16


GAMMA = 1.4
METRIC = 0.1
SECTION_STEP = 0.5


def gauss_nodes():
    root_term = math.sqrt(6.0 / 5.0)
    inner_node = math.sqrt(3.0 / 7.0 - 2.0 / 7.0 * root_term)
    outer_node = math.sqrt(3.0 / 7.0 + 2.0 / 7.0 * root_term)
    return [-outer_node, -inner_node, inner_node, outer_node]


def lagrange_value(node_list, column, position):
    result = 1.0
    for factor_index in range(4):
        if factor_index != column:
            result = (
                result
                * (position - node_list[factor_index])
                / (node_list[column] - node_list[factor_index])
            )
    return result


def lagrange_slope(node_list, column, position):
    total = 0.0
    for skipped in range(4):
        if skipped == column:
            continue
        term = 1.0 / (node_list[column] - node_list[skipped])
        for factor_index in range(4):
            if factor_index != column and factor_index != skipped:
                term = (
                    term
                    * (position - node_list[factor_index])
                    / (node_list[column] - node_list[factor_index])
                )
        total = total + term
    return total


def basis_tables():
    node_list = gauss_nodes()
    derivs = [
        [lagrange_slope(node_list, column, node_list[source]) for column in range(4)]
        for source in range(4)
    ]
    left_vals = [lagrange_value(node_list, column, -1.0) for column in range(4)]
    right_vals = [lagrange_value(node_list, column, 1.0) for column in range(4)]
    third_slope = [(15.0 * value * value - 3.0) / 2.0 for value in node_list]
    fourth_slope = [(35.0 * value**3 - 15.0 * value) / 2.0 for value in node_list]
    left_corr = [-0.5 * (third_slope[source] - fourth_slope[source]) for source in range(4)]
    right_corr = [0.5 * (third_slope[source] + fourth_slope[source]) for source in range(4)]
    return (derivs, left_vals, right_vals, left_corr, right_corr)


def apply_points(adj_field, matrix, point_dim):
    slab_list = [
        lax.index_in_dim(adj_field, source, point_dim, keepdims=False) for source in range(4)
    ]
    outputs = []
    for target in range(4):
        running = slab_list[0] * float(matrix[0][target])
        for source in range(1, 4):
            running = running + slab_list[source] * float(matrix[source][target])
        outputs.append(running)
    return jnp.stack(outputs, axis=point_dim)


def face_moment(adj_field, vector, point_dim):
    running = lax.index_in_dim(adj_field, 0, point_dim, keepdims=False) * float(vector[0])
    for source in range(1, 4):
        running = running + lax.index_in_dim(adj_field, source, point_dim, keepdims=False) * float(
            vector[source]
        )
    return running


def lift_face(face_vals, vector, point_dim):
    return jnp.stack([face_vals * float(vector[target]) for target in range(4)], axis=point_dim)


def conserved(primitive):
    density = primitive[0]
    velocity = primitive[1:4]
    pressure = primitive[4]
    energy = pressure / (GAMMA - 1.0) + 0.5 * density * jnp.sum(velocity * velocity, axis=0)
    return jnp.concatenate([density[None], density[None] * velocity, energy[None]], axis=0)


def euler_flux(cons_state, direction):
    density = cons_state[0]
    momentum = cons_state[1:4]
    energy = cons_state[4]
    velocity = momentum / density[None]
    pressure = (GAMMA - 1.0) * (energy - 0.5 * jnp.sum(momentum * velocity, axis=0))
    normal_speed = velocity[direction]
    columns = [momentum[direction]]
    for component in range(3):
        if component == direction:
            columns.append(momentum[component] * normal_speed + pressure)
        else:
            columns.append(momentum[component] * normal_speed)
    columns.append((energy + pressure) * normal_speed)
    return jnp.stack(columns, axis=0)


def transpose_flux(cons_state, cotangent, direction):
    unused, pullback = jax.vjp(lambda current: euler_flux(current, direction), cons_state)
    return pullback(cotangent)[0]


def section_rate(adj_field, cons_state, left_moments, right_moments, next_left, prev_right):
    derivs, left_vals, right_vals, left_corr, right_corr = basis_tables()
    rate_sum = jnp.zeros_like(adj_field)
    for direction in range(3):
        point_dim = 1 + direction
        bracket = apply_points(adj_field, derivs, point_dim)
        bracket = bracket + 0.5 * lift_face(
            next_left[direction] - right_moments[direction], right_vals, point_dim
        )
        bracket = bracket + 0.5 * lift_face(
            prev_right[direction] - left_moments[direction], left_vals, point_dim
        )
        rate_sum = rate_sum - METRIC * transpose_flux(cons_state, bracket, direction)
    return rate_sum


def all_moments(adj_field):
    derivs, left_vals, right_vals, left_corr, right_corr = basis_tables()
    left_moments = [face_moment(adj_field, left_corr, 1 + direction) for direction in range(3)]
    right_moments = [face_moment(adj_field, right_corr, 1 + direction) for direction in range(3)]
    return (left_moments, right_moments)


def faces_to_rows(face_vals):
    axial_elems = face_vals.shape[3]
    azim_elems = face_vals.shape[4]
    return face_vals.transpose(0, 3, 1, 4, 2).reshape(5, 4 * axial_elems, 4 * azim_elems)


def rows_to_face(rows_vals, axial_elems, azim_elems):
    return rows_vals.reshape(5, axial_elems, 4, azim_elems, 4).transpose(0, 2, 4, 1, 3)


def shift_sum(window, coefs, lo):
    total = None
    for offset, coef in coefs:
        term = coef[None] * window[:, :, lo + offset : lo + offset + TP]
        total = term if total is None else total + term
    return total


def lane_roll(value, shift):
    return pltpu.roll(value, shift % 128, value.ndim - 1)


def sweep(field, weights, pick):
    total = field[pick(0)] * float(weights[0])
    for source in range(1, 4):
        total = total + field[pick(source)] * float(weights[source])
    return total


def column(values, shape):
    rows = lax.broadcasted_iota(jnp.int32, shape, 2)
    out = jnp.full(shape, float(values[3]), jnp.float32)
    for index in range(3):
        out = jnp.where(rows == index, float(values[index]), out)
    return out


def compact_face(face, part):
    lane = lax.broadcasted_iota(jnp.int32, (4, 128), 1)
    out = jnp.zeros((4, 128), jnp.float32)
    for block in range(4):
        for group in range(EA):
            shift = block * ET * ER - group * (ET - 1) * ER - part * ER
            start = block * ET * ER + group * ER
            mask = (lane >= start) & (lane < start + ER)
            out = jnp.where(mask, lane_roll(face[block], shift), out)
    return out


def expand_face(chunk, part):
    lane = lax.broadcasted_iota(jnp.int32, (4, 128), 1)
    group_of = lane // (ET * ER)
    in_part = lane // ER % ET == part
    blocks = []
    for block in range(4):
        out = jnp.zeros((4, 128), jnp.float32)
        for group in range(EA):
            shift = block * ET * ER - group * (ET - 1) * ER - part * ER
            out = jnp.where(in_part & (group_of == group), lane_roll(chunk, -shift), out)
        blocks.append(out)
    return jnp.stack(blocks, axis=0)


def selector(rows, cols, lane_of, use_rows):
    row = lax.broadcasted_iota(jnp.int32, (rows, cols), 0)
    col = lax.broadcasted_iota(jnp.int32, (rows, cols), 1)
    if use_rows:
        hit = (row == lane_of(col)) & (row < EA * ET)
    else:
        hit = (row == lane_of(col)) & (col < EA * ET)
    return jnp.where(hit, 1.0, 0.0)


def exact_dot(left, right):
    return jnp.dot(left, right, precision=lax.Precision.HIGHEST, preferred_element_type=jnp.float32)


def moment_kernel(adj_ref, left_ax_ref, right_ax_ref, up_ref, down_ref, outer_ref, inner_ref, scratch_ref):
    derivs, left_vals, right_vals, left_corr, right_corr = basis_tables()
    pick_outer = selector(128, 128, lambda k: k // ET * ET * ER + k % ET * ER + ER - 1, False)
    pick_inner = selector(128, 128, lambda k: k // ET * ET * ER + k % ET * ER, False)
    for chan in range(5):
        field = adj_ref[0, chan]
        left_ax_ref[chan] = sweep(field, left_corr, lambda i: (i,))
        right_ax_ref[chan] = sweep(field, right_corr, lambda i: (i,))
        pick1 = lambda i: (slice(None), i)
        up_ref[chan] = compact_face(sweep(field, left_corr, pick1), 0)
        down_ref[chan] = compact_face(sweep(field, right_corr, pick1), ET - 1)
        pick2 = lambda i: (slice(None), slice(None), slice(i, i + 1))
        outer = sweep(field, right_corr, pick2)
        inner = sweep(field, left_corr, pick2)
        for axial in range(4):
            for azim in range(4):
                row = axial * 4 + azim
                scratch_ref[0, row : row + 1] = outer[axial, azim]
                scratch_ref[1, row : row + 1] = inner[axial, azim]
        outer_ref[chan] = exact_dot(scratch_ref[0], pick_outer)
        inner_ref[chan] = exact_dot(scratch_ref[1], pick_inner)


def rate_kernel(
    adj_ref, flow_ref, up_ax_ref, down_ax_ref, up_az_ref, down_az_ref, sides_ref,
    rate_ref, next_ref,
):
    derivs, left_vals, right_vals, left_corr, right_corr = basis_tables()
    shape = (4, 4, 4, 128)
    lane = lax.broadcasted_iota(jnp.int32, shape, 3)
    flat_lane = lax.broadcasted_iota(jnp.int32, (4, 4, 128), 2)
    az_flat = flat_lane // ER % ET
    radial_lane = lane % ER
    brackets = [[None] * 5 for _ in range(3)]
    col = lax.broadcasted_iota(jnp.int32, (16, 128), 1)
    row = lax.broadcasted_iota(jnp.int32, (16, 128), 0)
    sides = sides_ref[...]
    spread = [
        exact_dot(sides, jnp.where(row == col // ER % ET * 4 + azim, 1.0, 0.0)) for azim in range(4)
    ]
    group = lax.broadcasted_iota(jnp.int32, (1, 128), 1) // (ET * ER)

    def side_face(side, chan):
        blocks = []
        for axial in range(4):
            slabs = []
            for azim in range(4):
                base = (side * 5 + chan) * 16 + axial
                value = spread[azim][base : base + 1]
                for elem in range(1, EA):
                    pos = base + elem * 4
                    value = jnp.where(group == elem, spread[azim][pos : pos + 1], value)
                slabs.append(jnp.broadcast_to(value, (4, 128)))
            blocks.append(jnp.stack(slabs, axis=0))
        return jnp.stack(blocks, axis=0)

    for chan in range(5):
        field = adj_ref[0, chan]
        outer_face = side_face(0, chan)
        inner_face = side_face(1, chan)
        up_az = expand_face(up_az_ref[chan], 0)
        down_az = expand_face(down_az_ref[chan], ET - 1)
        left0 = sweep(field, left_corr, lambda i: (i,))
        right0 = sweep(field, right_corr, lambda i: (i,))
        next0 = lane_roll(jnp.where(flat_lane < ET * ER, up_ax_ref[chan], left0), -ET * ER)
        prev0 = lane_roll(jnp.where(flat_lane >= (EA - 1) * ET * ER, down_ax_ref[chan], right0), ET * ER)
        jump_r = 0.5 * (next0 - right0)
        jump_l = 0.5 * (prev0 - left0)
        slabs = []
        for target in range(4):
            slab = sweep(field, [derivs[i][target] for i in range(4)], lambda i: (i,))
            slabs.append(slab + jump_r * float(right_vals[target]) + jump_l * float(left_vals[target]))
        brackets[0][chan] = jnp.stack(slabs, axis=0)
        pick1 = lambda i: (slice(None), i)
        left1 = sweep(field, left_corr, pick1)
        right1 = sweep(field, right_corr, pick1)
        next1 = lane_roll(
            jnp.where(az_flat == 0, lane_roll(up_az, ET * ER), left1), -ER
        )
        prev1 = lane_roll(
            jnp.where(az_flat == ET - 1, lane_roll(down_az, -ET * ER), right1), ER
        )
        jump_r = 0.5 * (next1 - right1)
        jump_l = 0.5 * (prev1 - left1)
        slabs = []
        for target in range(4):
            slab = sweep(field, [derivs[i][target] for i in range(4)], pick1)
            slabs.append(slab + jump_r * float(right_vals[target]) + jump_l * float(left_vals[target]))
        brackets[1][chan] = jnp.stack(slabs, axis=1)
        points = [jnp.broadcast_to(field[:, :, i : i + 1, :], shape) for i in range(4)]
        left2 = sweep(points, left_corr, lambda i: i)
        right2 = sweep(points, right_corr, lambda i: i)
        next2 = jnp.where(radial_lane == ER - 1, outer_face, lane_roll(left2, -1))
        prev2 = jnp.where(radial_lane == 0, inner_face, lane_roll(right2, 1))
        bracket = 0.5 * (next2 - right2) * column(right_vals, shape)
        bracket = bracket + 0.5 * (prev2 - left2) * column(left_vals, shape)
        for source in range(4):
            bracket = bracket + points[source] * column(derivs[source], shape)
        brackets[2][chan] = bracket
    prim = [flow_ref[0, chan].astype(jnp.float32) for chan in range(5)]
    density = prim[0]
    speed_sq = prim[1] * prim[1] + prim[2] * prim[2] + prim[3] * prim[3]
    energy = prim[4] / (GAMMA - 1.0) + 0.5 * density * speed_sq
    momentum = [density * prim[1 + k] for k in range(3)]
    velocity = [momentum[k] / density for k in range(3)]
    kinetic = momentum[0] * velocity[0] + momentum[1] * velocity[1] + momentum[2] * velocity[2]
    pressure = (GAMMA - 1.0) * (energy - 0.5 * kinetic)
    enthalpy = (energy + pressure) / density
    vel_sq = velocity[0] * velocity[0] + velocity[1] * velocity[1] + velocity[2] * velocity[2]
    grad = [None] * 5
    for direction in range(3):
        cot = brackets[direction]
        normal = velocity[direction]
        dotted = cot[1] * velocity[0] + cot[2] * velocity[1] + cot[3] * velocity[2] + cot[4] * enthalpy
        weight = cot[1 + direction] + cot[4] * normal
        terms = [
            0.5 * (GAMMA - 1.0) * vel_sq * weight - dotted * normal,
            None,
            None,
            None,
            (GAMMA - 1.0) * weight + cot[4] * normal,
        ]
        for k in range(3):
            term = cot[1 + k] * normal - (GAMMA - 1.0) * weight * velocity[k]
            if k == direction:
                term = term + (cot[0] + dotted)
            terms[1 + k] = term
        for chan in range(5):
            grad[chan] = terms[chan] if grad[chan] is None else grad[chan] + terms[chan]
    for chan in range(5):
        rate = -METRIC * grad[chan]
        rate_ref[0, chan] = rate
        next_ref[0, chan] = adj_ref[0, chan] + SECTION_STEP * rate


def local(adjoint, flow_prim, intersection_shift, weight_index, mortar_weights, sector_offset):
    n_axial = lax.axis_size("axial")
    n_azim = lax.axis_size("azim")
    face4 = jax.ShapeDtypeStruct((5, 4, 4, 128), jnp.float32)
    chunk = jax.ShapeDtypeStruct((5, 4, 128), jnp.float32)
    rows16 = jax.ShapeDtypeStruct((5, 16, 128), jnp.float32)
    left_ax, right_ax, upper_face, lower_face, outer_moment, inner_moment = pl.pallas_call(
        moment_kernel,
        out_shape=(face4, face4, chunk, chunk, rows16, rows16),
        scratch_shapes=[pltpu.VMEM((2, 16, 128), jnp.float32)],
    )(adjoint)
    is_rotor = lax.axis_index("zone") == 0
    even = lax.axis_index("axial") % 2 == 0
    first = [(i, i + 1) for i in range(0, n_axial - 1, 2)] + [(i, i - 1) for i in range(1, n_axial, 2)]
    second = [(i, i + 1) for i in range(1, n_axial - 1, 2)] + [(i, i - 1) for i in range(2, n_axial, 2)]
    got_first = lax.ppermute(jnp.where(even, right_ax, left_ax), "axial", first)
    if second:
        got_second = lax.ppermute(jnp.where(even, left_ax, right_ax), "axial", second)
    else:
        got_second = jnp.zeros_like(got_first)
    up_ax = jnp.where(even, got_first, got_second)
    down_ax = jnp.where(even, got_second, got_first)
    own_face = jnp.where(is_rotor, outer_moment, inner_moment)[:, :, : EA * ET]
    own_rows = own_face.reshape(5, 4, 4, EA, ET).transpose(0, 3, 1, 4, 2).reshape(5, AP, TP)
    shifts_local = intersection_shift.reshape(INTERSECTIONS, AP, TP)
    table_match = weight_index[:, :, None] == jnp.arange(NW, dtype=jnp.int32)[None, None, :]
    weights_local = jnp.sum(
        jnp.where(table_match, mortar_weights[None, None, :], 0.0), axis=2
    ).reshape(INTERSECTIONS, AP, TP)
    offset = sector_offset[0]
    turn = (offset + TP // 2) // TP
    residue = offset - turn * TP
    offsets_k = residue + shifts_local
    rel_all = jnp.arange(-TP, TP - 1, dtype=jnp.int32)[:, None, None]
    coef_all = jnp.where(offsets_k[0][None] == rel_all, weights_local[0][None], 0.0)
    for member in range(1, INTERSECTIONS):
        coef_all = coef_all + jnp.where(offsets_k[member][None] == rel_all, weights_local[member][None], 0.0)
    coefs = [(rel, coef_all[rel + TP]) for rel in range(-TP, TP - 1)]
    contrib = None
    for rel, coef in coefs:
        term = jnp.pad(coef[None] * own_rows, ((0, 0), (0, 0), (TP + rel, TP - rel)))
        contrib = term if contrib is None else contrib + term
    zone = lax.axis_index("zone")
    azim = lax.axis_index("azim")
    dest = jnp.arange(2 * n_azim, dtype=jnp.int32)
    dest_azim = dest % n_azim
    gap = ((dest_azim - azim) % n_azim - turn) % n_azim
    gap = gap[:, None, None, None]
    pieces = jnp.where(
        gap == n_azim - 1,
        contrib[None, :, :, :TP],
        jnp.where(gap == 0, contrib[None, :, :, TP : 2 * TP], contrib[None, :, :, 2 * TP :]),
    )
    iface_out = jnp.where(is_rotor, jnp.broadcast_to(own_rows[None], pieces.shape), pieces)
    iface_out = jnp.pad(iface_out.reshape(2 * n_azim, 5, 2, 128), ((0, 0), (0, 0), (0, 2), (0, 0)))
    same_zone = dest // n_azim == zone
    to_prev = (same_zone & (dest_azim == (azim - 1) % n_azim))[:, None, None, None]
    to_next = (same_zone & (dest_azim == (azim + 1) % n_azim))[:, None, None, None]
    chunks = jnp.where(
        to_prev, upper_face[None], jnp.where(to_next, lower_face[None], jnp.where(same_zone[:, None, None, None], 0.0, iface_out))
    )
    got = lax.all_to_all(chunks, ("zone", "azim"), 0, 0)
    base = (1 - zone) * n_azim
    up_az = lax.dynamic_index_in_dim(got, zone * n_azim + (azim + 1) % n_azim, 0, keepdims=False)
    down_az = lax.dynamic_index_in_dim(got, zone * n_azim + (azim - 1) % n_azim, 0, keepdims=False)
    direction = jnp.where(is_rotor, -1, 1)
    picked = [
        lax.dynamic_index_in_dim(
            got, base + (azim + direction * (turn + step)) % n_azim, 0, keepdims=False
        )[:, :2].reshape(5, AP, TP)
        for step in (-1, 0, 1)
    ]
    returned = picked[0] + picked[1] + picked[2]
    window = jnp.concatenate(picked, axis=2)
    incoming = shift_sum(window, coefs, TP)
    sides = jnp.concatenate(
        [jnp.where(is_rotor, returned, 0.0), jnp.where(is_rotor, 0.0, incoming)], axis=0
    ).reshape(10 * AP, TP)
    field_shape = jax.ShapeDtypeStruct(adjoint.shape, jnp.float32)
    adjoint_rate, next_adjoint = pl.pallas_call(
        rate_kernel, out_shape=(field_shape, field_shape)
    )(adjoint, flow_prim, up_ax, down_ax, up_az, down_az, sides)
    return (adjoint_rate, next_adjoint)


def solution(mesh):
    placed = (
        P("zone", None, None, None, None, ("axial", "azim")),
        P("zone", None, None, None, None, ("axial", "azim")),
        P(None, ("axial", "azim")),
        P(None, ("axial", "azim")),
        P(),
        P(),
    )
    return jax.shard_map(
        local,
        mesh=mesh,
        in_specs=placed,
        out_specs=(
            P("zone", None, None, None, None, ("axial", "azim")),
            P("zone", None, None, None, None, ("axial", "azim")),
        ),
        check_vma=False,
    )
```

```python
import math

import jax
import jax.numpy as jnp
from jax import lax
from jax.experimental import pallas as pl
from jax.experimental.pallas import tpu as pltpu
from jax.sharding import PartitionSpec as P

EA = 4
ET = 4
ER = 8
INTERSECTIONS = 4
NW = 128
AP = 16
TP = 16


GAMMA = 1.4
METRIC = 0.1
SECTION_STEP = 0.5


def gauss_nodes():
    root_term = math.sqrt(6.0 / 5.0)
    inner_node = math.sqrt(3.0 / 7.0 - 2.0 / 7.0 * root_term)
    outer_node = math.sqrt(3.0 / 7.0 + 2.0 / 7.0 * root_term)
    return [-outer_node, -inner_node, inner_node, outer_node]


def lagrange_value(node_list, column, position):
    result = 1.0
    for factor_index in range(4):
        if factor_index != column:
            result = (
                result
                * (position - node_list[factor_index])
                / (node_list[column] - node_list[factor_index])
            )
    return result


def lagrange_slope(node_list, column, position):
    total = 0.0
    for skipped in range(4):
        if skipped == column:
            continue
        term = 1.0 / (node_list[column] - node_list[skipped])
        for factor_index in range(4):
            if factor_index != column and factor_index != skipped:
                term = (
                    term
                    * (position - node_list[factor_index])
                    / (node_list[column] - node_list[factor_index])
                )
        total = total + term
    return total


def basis_tables():
    node_list = gauss_nodes()
    derivs = [
        [lagrange_slope(node_list, column, node_list[source]) for column in range(4)]
        for source in range(4)
    ]
    left_vals = [lagrange_value(node_list, column, -1.0) for column in range(4)]
    right_vals = [lagrange_value(node_list, column, 1.0) for column in range(4)]
    third_slope = [(15.0 * value * value - 3.0) / 2.0 for value in node_list]
    fourth_slope = [(35.0 * value**3 - 15.0 * value) / 2.0 for value in node_list]
    left_corr = [-0.5 * (third_slope[source] - fourth_slope[source]) for source in range(4)]
    right_corr = [0.5 * (third_slope[source] + fourth_slope[source]) for source in range(4)]
    return (derivs, left_vals, right_vals, left_corr, right_corr)


def apply_points(adj_field, matrix, point_dim):
    slab_list = [
        lax.index_in_dim(adj_field, source, point_dim, keepdims=False) for source in range(4)
    ]
    outputs = []
    for target in range(4):
        running = slab_list[0] * float(matrix[0][target])
        for source in range(1, 4):
            running = running + slab_list[source] * float(matrix[source][target])
        outputs.append(running)
    return jnp.stack(outputs, axis=point_dim)


def face_moment(adj_field, vector, point_dim):
    running = lax.index_in_dim(adj_field, 0, point_dim, keepdims=False) * float(vector[0])
    for source in range(1, 4):
        running = running + lax.index_in_dim(adj_field, source, point_dim, keepdims=False) * float(
            vector[source]
        )
    return running


def lift_face(face_vals, vector, point_dim):
    return jnp.stack([face_vals * float(vector[target]) for target in range(4)], axis=point_dim)


def conserved(primitive):
    density = primitive[0]
    velocity = primitive[1:4]
    pressure = primitive[4]
    energy = pressure / (GAMMA - 1.0) + 0.5 * density * jnp.sum(velocity * velocity, axis=0)
    return jnp.concatenate([density[None], density[None] * velocity, energy[None]], axis=0)


def euler_flux(cons_state, direction):
    density = cons_state[0]
    momentum = cons_state[1:4]
    energy = cons_state[4]
    velocity = momentum / density[None]
    pressure = (GAMMA - 1.0) * (energy - 0.5 * jnp.sum(momentum * velocity, axis=0))
    normal_speed = velocity[direction]
    columns = [momentum[direction]]
    for component in range(3):
        if component == direction:
            columns.append(momentum[component] * normal_speed + pressure)
        else:
            columns.append(momentum[component] * normal_speed)
    columns.append((energy + pressure) * normal_speed)
    return jnp.stack(columns, axis=0)


def transpose_flux(cons_state, cotangent, direction):
    unused, pullback = jax.vjp(lambda current: euler_flux(current, direction), cons_state)
    return pullback(cotangent)[0]


def section_rate(adj_field, cons_state, left_moments, right_moments, next_left, prev_right):
    derivs, left_vals, right_vals, left_corr, right_corr = basis_tables()
    rate_sum = jnp.zeros_like(adj_field)
    for direction in range(3):
        point_dim = 1 + direction
        bracket = apply_points(adj_field, derivs, point_dim)
        bracket = bracket + 0.5 * lift_face(
            next_left[direction] - right_moments[direction], right_vals, point_dim
        )
        bracket = bracket + 0.5 * lift_face(
            prev_right[direction] - left_moments[direction], left_vals, point_dim
        )
        rate_sum = rate_sum - METRIC * transpose_flux(cons_state, bracket, direction)
    return rate_sum


def all_moments(adj_field):
    derivs, left_vals, right_vals, left_corr, right_corr = basis_tables()
    left_moments = [face_moment(adj_field, left_corr, 1 + direction) for direction in range(3)]
    right_moments = [face_moment(adj_field, right_corr, 1 + direction) for direction in range(3)]
    return (left_moments, right_moments)


def faces_to_rows(face_vals):
    axial_elems = face_vals.shape[3]
    azim_elems = face_vals.shape[4]
    return face_vals.transpose(0, 3, 1, 4, 2).reshape(5, 4 * axial_elems, 4 * azim_elems)


def rows_to_face(rows_vals, axial_elems, azim_elems):
    return rows_vals.reshape(5, axial_elems, 4, azim_elems, 4).transpose(0, 2, 4, 1, 3)


def shift_sum(window, coefs, lo):
    total = None
    for offset, coef in coefs:
        term = coef[None] * window[:, :, lo + offset : lo + offset + TP]
        total = term if total is None else total + term
    return total


def lane_roll(value, shift):
    return pltpu.roll(value, shift % 128, value.ndim - 1)


def sweep(field, weights, pick):
    total = field[pick(0)] * float(weights[0])
    for source in range(1, 4):
        total = total + field[pick(source)] * float(weights[source])
    return total


def column(values, shape):
    rows = lax.broadcasted_iota(jnp.int32, shape, 2)
    out = jnp.full(shape, float(values[3]), jnp.float32)
    for index in range(3):
        out = jnp.where(rows == index, float(values[index]), out)
    return out


def compact_face(face, part):
    lane = lax.broadcasted_iota(jnp.int32, (4, 128), 1)
    out = jnp.zeros((4, 128), jnp.float32)
    for block in range(4):
        for group in range(EA):
            shift = block * ET * ER - group * (ET - 1) * ER - part * ER
            start = block * ET * ER + group * ER
            mask = (lane >= start) & (lane < start + ER)
            out = jnp.where(mask, lane_roll(face[block], shift), out)
    return out


def expand_face(chunk, part):
    lane = lax.broadcasted_iota(jnp.int32, (4, 128), 1)
    group_of = lane // (ET * ER)
    in_part = lane // ER % ET == part
    blocks = []
    for block in range(4):
        out = jnp.zeros((4, 128), jnp.float32)
        for group in range(EA):
            shift = block * ET * ER - group * (ET - 1) * ER - part * ER
            out = jnp.where(in_part & (group_of == group), lane_roll(chunk, -shift), out)
        blocks.append(out)
    return jnp.stack(blocks, axis=0)


def selector(rows, cols, lane_of, use_rows):
    row = lax.broadcasted_iota(jnp.int32, (rows, cols), 0)
    col = lax.broadcasted_iota(jnp.int32, (rows, cols), 1)
    if use_rows:
        hit = (row == lane_of(col)) & (row < EA * ET)
    else:
        hit = (row == lane_of(col)) & (col < EA * ET)
    return jnp.where(hit, 1.0, 0.0)


def exact_dot(left, right):
    return jnp.dot(left, right, precision=lax.Precision.HIGHEST, preferred_element_type=jnp.float32)


def moment_kernel(adj_ref, left_ax_ref, right_ax_ref, up_ref, down_ref, own_ref, scratch_ref):
    derivs, left_vals, right_vals, left_corr, right_corr = basis_tables()
    pick_outer = selector(128, 128, lambda k: k // ET * ET * ER + k % ET * ER + ER - 1, False)
    pick_inner = selector(128, 128, lambda k: k // ET * ET * ER + k % ET * ER, False)
    rotor = lax.axis_index("zone") == 0
    pick = jnp.where(rotor, pick_outer, pick_inner)
    for chan in range(5):
        field = adj_ref[0, chan]
        left_ax_ref[chan] = sweep(field, left_corr, lambda i: (i,))
        right_ax_ref[chan] = sweep(field, right_corr, lambda i: (i,))
        pick1 = lambda i: (slice(None), i)
        up_ref[chan] = compact_face(sweep(field, left_corr, pick1), 0)
        down_ref[chan] = compact_face(sweep(field, right_corr, pick1), ET - 1)
        pick2 = lambda i: (slice(None), slice(None), slice(i, i + 1))
        outer = sweep(field, right_corr, pick2)
        inner = sweep(field, left_corr, pick2)
        for axial in range(4):
            for azim in range(4):
                row = axial * 4 + azim
                scratch_ref[0, row : row + 1] = outer[axial, azim]
                scratch_ref[1, row : row + 1] = inner[axial, azim]
        rows = jnp.where(rotor, scratch_ref[0], scratch_ref[1])
        own_ref[chan] = exact_dot(rows, pick)[:, : EA * ET]


def rate_kernel(
    adj_ref, flow_ref, up_ax_ref, down_ax_ref, up_az_ref, down_az_ref, sides_ref,
    rate_ref, next_ref,
):
    derivs, left_vals, right_vals, left_corr, right_corr = basis_tables()
    shape = (4, 4, 4, 128)
    lane = lax.broadcasted_iota(jnp.int32, shape, 3)
    flat_lane = lax.broadcasted_iota(jnp.int32, (4, 4, 128), 2)
    az_flat = flat_lane // ER % ET
    radial_lane = lane % ER
    brackets = [[None] * 5 for _ in range(3)]
    col = lax.broadcasted_iota(jnp.int32, (16, 128), 1)
    row = lax.broadcasted_iota(jnp.int32, (16, 128), 0)
    sides = sides_ref[...]
    spread = [
        exact_dot(sides, jnp.where(row == col // ER % ET * 4 + azim, 1.0, 0.0)) for azim in range(4)
    ]
    group = lax.broadcasted_iota(jnp.int32, (1, 128), 1) // (ET * ER)

    def side_face(side, chan):
        blocks = []
        for axial in range(4):
            slabs = []
            for azim in range(4):
                base = (side * 5 + chan) * 16 + axial
                value = spread[azim][base : base + 1]
                for elem in range(1, EA):
                    pos = base + elem * 4
                    value = jnp.where(group == elem, spread[azim][pos : pos + 1], value)
                slabs.append(jnp.broadcast_to(value, (4, 128)))
            blocks.append(jnp.stack(slabs, axis=0))
        return jnp.stack(blocks, axis=0)

    for chan in range(5):
        field = adj_ref[0, chan]
        outer_face = side_face(0, chan)
        inner_face = side_face(1, chan)
        up_az = expand_face(up_az_ref[chan], 0)
        down_az = expand_face(down_az_ref[chan], ET - 1)
        left0 = sweep(field, left_corr, lambda i: (i,))
        right0 = sweep(field, right_corr, lambda i: (i,))
        next0 = lane_roll(jnp.where(flat_lane < ET * ER, up_ax_ref[chan], left0), -ET * ER)
        prev0 = lane_roll(jnp.where(flat_lane >= (EA - 1) * ET * ER, down_ax_ref[chan], right0), ET * ER)
        jump_r = 0.5 * (next0 - right0)
        jump_l = 0.5 * (prev0 - left0)
        slabs = []
        for target in range(4):
            slab = sweep(field, [derivs[i][target] for i in range(4)], lambda i: (i,))
            slabs.append(slab + jump_r * float(right_vals[target]) + jump_l * float(left_vals[target]))
        brackets[0][chan] = jnp.stack(slabs, axis=0)
        pick1 = lambda i: (slice(None), i)
        left1 = sweep(field, left_corr, pick1)
        right1 = sweep(field, right_corr, pick1)
        next1 = lane_roll(
            jnp.where(az_flat == 0, lane_roll(up_az, ET * ER), left1), -ER
        )
        prev1 = lane_roll(
            jnp.where(az_flat == ET - 1, lane_roll(down_az, -ET * ER), right1), ER
        )
        jump_r = 0.5 * (next1 - right1)
        jump_l = 0.5 * (prev1 - left1)
        slabs = []
        for target in range(4):
            slab = sweep(field, [derivs[i][target] for i in range(4)], pick1)
            slabs.append(slab + jump_r * float(right_vals[target]) + jump_l * float(left_vals[target]))
        brackets[1][chan] = jnp.stack(slabs, axis=1)
        points = [jnp.broadcast_to(field[:, :, i : i + 1, :], shape) for i in range(4)]
        left2 = sweep(points, left_corr, lambda i: i)
        right2 = sweep(points, right_corr, lambda i: i)
        next2 = jnp.where(radial_lane == ER - 1, outer_face, lane_roll(left2, -1))
        prev2 = jnp.where(radial_lane == 0, inner_face, lane_roll(right2, 1))
        bracket = 0.5 * (next2 - right2) * column(right_vals, shape)
        bracket = bracket + 0.5 * (prev2 - left2) * column(left_vals, shape)
        for source in range(4):
            bracket = bracket + points[source] * column(derivs[source], shape)
        brackets[2][chan] = bracket
    prim = [flow_ref[0, chan].astype(jnp.float32) for chan in range(5)]
    density = prim[0]
    speed_sq = prim[1] * prim[1] + prim[2] * prim[2] + prim[3] * prim[3]
    energy = prim[4] / (GAMMA - 1.0) + 0.5 * density * speed_sq
    momentum = [density * prim[1 + k] for k in range(3)]
    velocity = [momentum[k] / density for k in range(3)]
    kinetic = momentum[0] * velocity[0] + momentum[1] * velocity[1] + momentum[2] * velocity[2]
    pressure = (GAMMA - 1.0) * (energy - 0.5 * kinetic)
    enthalpy = (energy + pressure) / density
    vel_sq = velocity[0] * velocity[0] + velocity[1] * velocity[1] + velocity[2] * velocity[2]
    grad = [None] * 5
    for direction in range(3):
        cot = brackets[direction]
        normal = velocity[direction]
        dotted = cot[1] * velocity[0] + cot[2] * velocity[1] + cot[3] * velocity[2] + cot[4] * enthalpy
        weight = cot[1 + direction] + cot[4] * normal
        terms = [
            0.5 * (GAMMA - 1.0) * vel_sq * weight - dotted * normal,
            None,
            None,
            None,
            (GAMMA - 1.0) * weight + cot[4] * normal,
        ]
        for k in range(3):
            term = cot[1 + k] * normal - (GAMMA - 1.0) * weight * velocity[k]
            if k == direction:
                term = term + (cot[0] + dotted)
            terms[1 + k] = term
        for chan in range(5):
            grad[chan] = terms[chan] if grad[chan] is None else grad[chan] + terms[chan]
    for chan in range(5):
        rate = -METRIC * grad[chan]
        rate_ref[0, chan] = rate
        next_ref[0, chan] = adj_ref[0, chan] + SECTION_STEP * rate


def local(adjoint, flow_prim, intersection_shift, weight_index, mortar_weights, sector_offset):
    n_axial = lax.axis_size("axial")
    n_azim = lax.axis_size("azim")
    face4 = jax.ShapeDtypeStruct((5, 4, 4, 128), jnp.float32)
    chunk = jax.ShapeDtypeStruct((5, 4, 128), jnp.float32)
    rows16 = jax.ShapeDtypeStruct((5, 16, 128), jnp.float32)
    left_ax, right_ax, upper_face, lower_face, own_face = pl.pallas_call(
        moment_kernel,
        out_shape=(face4, face4, chunk, chunk, jax.ShapeDtypeStruct((5, 16, EA * ET), jnp.float32)),
        scratch_shapes=[pltpu.VMEM((2, 16, 128), jnp.float32)],
    )(adjoint)
    is_rotor = lax.axis_index("zone") == 0
    even = lax.axis_index("axial") % 2 == 0
    first = [(i, i + 1) for i in range(0, n_axial - 1, 2)] + [(i, i - 1) for i in range(1, n_axial, 2)]
    second = [(i, i + 1) for i in range(1, n_axial - 1, 2)] + [(i, i - 1) for i in range(2, n_axial, 2)]
    got_first = lax.ppermute(jnp.where(even, right_ax, left_ax), "axial", first)
    if second:
        got_second = lax.ppermute(jnp.where(even, left_ax, right_ax), "axial", second)
    else:
        got_second = jnp.zeros_like(got_first)
    up_ax = jnp.where(even, got_first, got_second)
    down_ax = jnp.where(even, got_second, got_first)
    own_rows = own_face.reshape(5, 4, 4, EA, ET).transpose(0, 3, 1, 4, 2).reshape(5, AP, TP)
    shifts_local = intersection_shift.reshape(INTERSECTIONS, AP, TP)
    table_match = weight_index[:, :, None] == jnp.arange(NW, dtype=jnp.int32)[None, None, :]
    weights_local = jnp.sum(
        jnp.where(table_match, mortar_weights[None, None, :], 0.0), axis=2
    ).reshape(INTERSECTIONS, AP, TP)
    offset = sector_offset[0]
    turn = (offset + TP // 2) // TP
    residue = offset - turn * TP
    offsets_k = residue + shifts_local
    rel_all = jnp.arange(-TP, TP - 1, dtype=jnp.int32)[:, None, None]
    coef_all = jnp.where(offsets_k[0][None] == rel_all, weights_local[0][None], 0.0)
    for member in range(1, INTERSECTIONS):
        coef_all = coef_all + jnp.where(offsets_k[member][None] == rel_all, weights_local[member][None], 0.0)
    coefs = [(rel, coef_all[rel + TP]) for rel in range(-TP, TP - 1)]
    contrib = None
    for rel, coef in coefs:
        term = jnp.pad(coef[None] * own_rows, ((0, 0), (0, 0), (TP + rel, TP - rel)))
        contrib = term if contrib is None else contrib + term
    zone = lax.axis_index("zone")
    azim = lax.axis_index("azim")
    dest = jnp.arange(2 * n_azim, dtype=jnp.int32)
    dest_azim = dest % n_azim
    gap = ((dest_azim - azim) % n_azim - turn) % n_azim
    gap = gap[:, None, None, None]
    pieces = jnp.where(
        gap == n_azim - 1,
        contrib[None, :, :, :TP],
        jnp.where(gap == 0, contrib[None, :, :, TP : 2 * TP], contrib[None, :, :, 2 * TP :]),
    )
    iface_out = jnp.where(is_rotor, jnp.broadcast_to(own_rows[None], pieces.shape), pieces)
    iface_out = jnp.pad(iface_out.reshape(2 * n_azim, 5, 2, 128), ((0, 0), (0, 0), (0, 2), (0, 0)))
    same_zone = dest // n_azim == zone
    to_prev = (same_zone & (dest_azim == (azim - 1) % n_azim))[:, None, None, None]
    to_next = (same_zone & (dest_azim == (azim + 1) % n_azim))[:, None, None, None]
    chunks = jnp.where(
        to_prev, upper_face[None], jnp.where(to_next, lower_face[None], jnp.where(same_zone[:, None, None, None], 0.0, iface_out))
    )
    got = lax.all_to_all(chunks, ("zone", "azim"), 0, 0)
    base = (1 - zone) * n_azim
    up_az = lax.dynamic_index_in_dim(got, zone * n_azim + (azim + 1) % n_azim, 0, keepdims=False)
    down_az = lax.dynamic_index_in_dim(got, zone * n_azim + (azim - 1) % n_azim, 0, keepdims=False)
    direction = jnp.where(is_rotor, -1, 1)
    picked = [
        lax.dynamic_index_in_dim(
            got, base + (azim + direction * (turn + step)) % n_azim, 0, keepdims=False
        )[:, :2].reshape(5, AP, TP)
        for step in (-1, 0, 1)
    ]
    returned = picked[0] + picked[1] + picked[2]
    window = jnp.concatenate(picked, axis=2)
    incoming = shift_sum(window, coefs, TP)
    sides = jnp.concatenate(
        [jnp.where(is_rotor, returned, 0.0), jnp.where(is_rotor, 0.0, incoming)], axis=0
    ).reshape(10 * AP, TP)
    field_shape = jax.ShapeDtypeStruct(adjoint.shape, jnp.float32)
    adjoint_rate, next_adjoint = pl.pallas_call(
        rate_kernel, out_shape=(field_shape, field_shape)
    )(adjoint, flow_prim, up_ax, down_ax, up_az, down_az, sides)
    return (adjoint_rate, next_adjoint)


def solution(mesh):
    placed = (
        P("zone", None, None, None, None, ("axial", "azim")),
        P("zone", None, None, None, None, ("axial", "azim")),
        P(None, ("axial", "azim")),
        P(None, ("axial", "azim")),
        P(),
        P(),
    )
    return jax.shard_map(
        local,
        mesh=mesh,
        in_specs=placed,
        out_specs=(
            P("zone", None, None, None, None, ("axial", "azim")),
            P("zone", None, None, None, None, ("axial", "azim")),
        ),
        check_vma=False,
    )
```

```python
import functools
import math

import jax
import jax.numpy as jnp
from jax import lax
from jax.experimental import pallas as pl
from jax.experimental.pallas import tpu as pltpu
from jax.sharding import PartitionSpec as P

EA = 4
ET = 4
ER = 8
INTERSECTIONS = 4
NW = 128
AP = 16
TP = 16


GAMMA = 1.4
METRIC = 0.1
SECTION_STEP = 0.5


def gauss_nodes():
    root_term = math.sqrt(6.0 / 5.0)
    inner_node = math.sqrt(3.0 / 7.0 - 2.0 / 7.0 * root_term)
    outer_node = math.sqrt(3.0 / 7.0 + 2.0 / 7.0 * root_term)
    return [-outer_node, -inner_node, inner_node, outer_node]


def lagrange_value(node_list, column, position):
    result = 1.0
    for factor_index in range(4):
        if factor_index != column:
            result = (
                result
                * (position - node_list[factor_index])
                / (node_list[column] - node_list[factor_index])
            )
    return result


def lagrange_slope(node_list, column, position):
    total = 0.0
    for skipped in range(4):
        if skipped == column:
            continue
        term = 1.0 / (node_list[column] - node_list[skipped])
        for factor_index in range(4):
            if factor_index != column and factor_index != skipped:
                term = (
                    term
                    * (position - node_list[factor_index])
                    / (node_list[column] - node_list[factor_index])
                )
        total = total + term
    return total


def basis_tables():
    node_list = gauss_nodes()
    derivs = [
        [lagrange_slope(node_list, column, node_list[source]) for column in range(4)]
        for source in range(4)
    ]
    left_vals = [lagrange_value(node_list, column, -1.0) for column in range(4)]
    right_vals = [lagrange_value(node_list, column, 1.0) for column in range(4)]
    third_slope = [(15.0 * value * value - 3.0) / 2.0 for value in node_list]
    fourth_slope = [(35.0 * value**3 - 15.0 * value) / 2.0 for value in node_list]
    left_corr = [-0.5 * (third_slope[source] - fourth_slope[source]) for source in range(4)]
    right_corr = [0.5 * (third_slope[source] + fourth_slope[source]) for source in range(4)]
    return (derivs, left_vals, right_vals, left_corr, right_corr)


def apply_points(adj_field, matrix, point_dim):
    slab_list = [
        lax.index_in_dim(adj_field, source, point_dim, keepdims=False) for source in range(4)
    ]
    outputs = []
    for target in range(4):
        running = slab_list[0] * float(matrix[0][target])
        for source in range(1, 4):
            running = running + slab_list[source] * float(matrix[source][target])
        outputs.append(running)
    return jnp.stack(outputs, axis=point_dim)


def face_moment(adj_field, vector, point_dim):
    running = lax.index_in_dim(adj_field, 0, point_dim, keepdims=False) * float(vector[0])
    for source in range(1, 4):
        running = running + lax.index_in_dim(adj_field, source, point_dim, keepdims=False) * float(
            vector[source]
        )
    return running


def lift_face(face_vals, vector, point_dim):
    return jnp.stack([face_vals * float(vector[target]) for target in range(4)], axis=point_dim)


def conserved(primitive):
    density = primitive[0]
    velocity = primitive[1:4]
    pressure = primitive[4]
    energy = pressure / (GAMMA - 1.0) + 0.5 * density * jnp.sum(velocity * velocity, axis=0)
    return jnp.concatenate([density[None], density[None] * velocity, energy[None]], axis=0)


def euler_flux(cons_state, direction):
    density = cons_state[0]
    momentum = cons_state[1:4]
    energy = cons_state[4]
    velocity = momentum / density[None]
    pressure = (GAMMA - 1.0) * (energy - 0.5 * jnp.sum(momentum * velocity, axis=0))
    normal_speed = velocity[direction]
    columns = [momentum[direction]]
    for component in range(3):
        if component == direction:
            columns.append(momentum[component] * normal_speed + pressure)
        else:
            columns.append(momentum[component] * normal_speed)
    columns.append((energy + pressure) * normal_speed)
    return jnp.stack(columns, axis=0)


def transpose_flux(cons_state, cotangent, direction):
    unused, pullback = jax.vjp(lambda current: euler_flux(current, direction), cons_state)
    return pullback(cotangent)[0]


def section_rate(adj_field, cons_state, left_moments, right_moments, next_left, prev_right):
    derivs, left_vals, right_vals, left_corr, right_corr = basis_tables()
    rate_sum = jnp.zeros_like(adj_field)
    for direction in range(3):
        point_dim = 1 + direction
        bracket = apply_points(adj_field, derivs, point_dim)
        bracket = bracket + 0.5 * lift_face(
            next_left[direction] - right_moments[direction], right_vals, point_dim
        )
        bracket = bracket + 0.5 * lift_face(
            prev_right[direction] - left_moments[direction], left_vals, point_dim
        )
        rate_sum = rate_sum - METRIC * transpose_flux(cons_state, bracket, direction)
    return rate_sum


def all_moments(adj_field):
    derivs, left_vals, right_vals, left_corr, right_corr = basis_tables()
    left_moments = [face_moment(adj_field, left_corr, 1 + direction) for direction in range(3)]
    right_moments = [face_moment(adj_field, right_corr, 1 + direction) for direction in range(3)]
    return (left_moments, right_moments)


def faces_to_rows(face_vals):
    axial_elems = face_vals.shape[3]
    azim_elems = face_vals.shape[4]
    return face_vals.transpose(0, 3, 1, 4, 2).reshape(5, 4 * axial_elems, 4 * azim_elems)


def rows_to_face(rows_vals, axial_elems, azim_elems):
    return rows_vals.reshape(5, axial_elems, 4, azim_elems, 4).transpose(0, 2, 4, 1, 3)


def shift_sum(window, coefs, lo):
    total = None
    for offset, coef in coefs:
        term = coef[None] * window[:, :, lo + offset : lo + offset + TP]
        total = term if total is None else total + term
    return total


def lane_roll(value, shift):
    return pltpu.roll(value, shift % 128, value.ndim - 1)


def sweep(field, weights, pick):
    total = field[pick(0)] * float(weights[0])
    for source in range(1, 4):
        total = total + field[pick(source)] * float(weights[source])
    return total


def column(values, shape):
    rows = lax.broadcasted_iota(jnp.int32, shape, 2)
    out = jnp.full(shape, float(values[3]), jnp.float32)
    for index in range(3):
        out = jnp.where(rows == index, float(values[index]), out)
    return out


def compact_face(face, part):
    lane = lax.broadcasted_iota(jnp.int32, (4, 128), 1)
    out = jnp.zeros((4, 128), jnp.float32)
    for block in range(4):
        for group in range(EA):
            shift = block * ET * ER - group * (ET - 1) * ER - part * ER
            start = block * ET * ER + group * ER
            mask = (lane >= start) & (lane < start + ER)
            out = jnp.where(mask, lane_roll(face[block], shift), out)
    return out


def expand_face(chunk, part):
    lane = lax.broadcasted_iota(jnp.int32, (4, 128), 1)
    group_of = lane // (ET * ER)
    in_part = lane // ER % ET == part
    blocks = []
    for block in range(4):
        out = jnp.zeros((4, 128), jnp.float32)
        for group in range(EA):
            shift = block * ET * ER - group * (ET - 1) * ER - part * ER
            out = jnp.where(in_part & (group_of == group), lane_roll(chunk, -shift), out)
        blocks.append(out)
    return jnp.stack(blocks, axis=0)


def selector(rows, cols, lane_of, use_rows):
    row = lax.broadcasted_iota(jnp.int32, (rows, cols), 0)
    col = lax.broadcasted_iota(jnp.int32, (rows, cols), 1)
    if use_rows:
        hit = (row == lane_of(col)) & (row < EA * ET)
    else:
        hit = (row == lane_of(col)) & (col < EA * ET)
    return jnp.where(hit, 1.0, 0.0)


def exact_dot(left, right):
    return jnp.dot(left, right, precision=lax.Precision.HIGHEST, preferred_element_type=jnp.float32)


def moment_kernel(adj_ref, left_ax_ref, right_ax_ref, up_ref, down_ref, own_ref, scratch_ref):
    derivs, left_vals, right_vals, left_corr, right_corr = basis_tables()
    pick_outer = selector(128, 128, lambda k: k // ET * ET * ER + k % ET * ER + ER - 1, False)
    pick_inner = selector(128, 128, lambda k: k // ET * ET * ER + k % ET * ER, False)
    rotor = lax.axis_index("zone") == 0
    pick = jnp.where(rotor, pick_outer, pick_inner)
    for chan in range(5):
        field = adj_ref[0, chan]
        left_ax_ref[chan] = sweep(field, left_corr, lambda i: (i,))
        right_ax_ref[chan] = sweep(field, right_corr, lambda i: (i,))
        pick1 = lambda i: (slice(None), i)
        up_ref[chan] = compact_face(sweep(field, left_corr, pick1), 0)
        down_ref[chan] = compact_face(sweep(field, right_corr, pick1), ET - 1)
        pick2 = lambda i: (slice(None), slice(None), slice(i, i + 1))
        outer = sweep(field, right_corr, pick2)
        inner = sweep(field, left_corr, pick2)
        for axial in range(4):
            for azim in range(4):
                row = axial * 4 + azim
                scratch_ref[0, row : row + 1] = outer[axial, azim]
                scratch_ref[1, row : row + 1] = inner[axial, azim]
        rows = jnp.where(rotor, scratch_ref[0], scratch_ref[1])
        own_ref[chan] = exact_dot(rows, pick)[:, : EA * ET]


def rate_kernel_single(body, adj_ref, flow_ref, first_ref, *rest):
    return body(adj_ref, flow_ref, first_ref, None, *rest)


def rate_kernel(
    adj_ref, flow_ref, first_ref, second_ref, up_az_ref, down_az_ref, sides_ref,
    rate_ref, next_ref,
):
    derivs, left_vals, right_vals, left_corr, right_corr = basis_tables()
    shape = (4, 4, 4, 128)
    lane = lax.broadcasted_iota(jnp.int32, shape, 3)
    flat_lane = lax.broadcasted_iota(jnp.int32, (4, 4, 128), 2)
    az_flat = flat_lane // ER % ET
    radial_lane = lane % ER
    brackets = [[None] * 5 for _ in range(3)]
    col = lax.broadcasted_iota(jnp.int32, (16, 128), 1)
    row = lax.broadcasted_iota(jnp.int32, (16, 128), 0)
    sides = sides_ref[...]
    even = lax.axis_index("axial") % 2 == 0
    rotor = lax.axis_index("zone") == 0
    spread = [
        exact_dot(sides, jnp.where(row == col // ER % ET * 4 + azim, 1.0, 0.0)) for azim in range(4)
    ]
    group = lax.broadcasted_iota(jnp.int32, (1, 128), 1) // (ET * ER)

    def side_face(side, chan):
        blocks = []
        for axial in range(4):
            slabs = []
            for azim in range(4):
                base = chan * 16 + axial
                value = spread[azim][base : base + 1]
                for elem in range(1, EA):
                    pos = base + elem * 4
                    value = jnp.where(group == elem, spread[azim][pos : pos + 1], value)
                slabs.append(jnp.broadcast_to(value, (4, 128)))
            blocks.append(jnp.stack(slabs, axis=0))
        return jnp.stack(blocks, axis=0)

    for chan in range(5):
        field = adj_ref[0, chan]
        own_face = side_face(0, chan)
        outer_face = jnp.where(rotor, own_face, 0.0)
        inner_face = jnp.where(rotor, 0.0, own_face)
        first = first_ref[chan]
        second = first * 0.0 if second_ref is None else second_ref[chan]
        up_ax = jnp.where(even, first, second)
        down_ax = jnp.where(even, second, first)
        up_az = expand_face(up_az_ref[chan], 0)
        down_az = expand_face(down_az_ref[chan], ET - 1)
        left0 = sweep(field, left_corr, lambda i: (i,))
        right0 = sweep(field, right_corr, lambda i: (i,))
        next0 = lane_roll(jnp.where(flat_lane < ET * ER, up_ax, left0), -ET * ER)
        prev0 = lane_roll(jnp.where(flat_lane >= (EA - 1) * ET * ER, down_ax, right0), ET * ER)
        jump_r = 0.5 * (next0 - right0)
        jump_l = 0.5 * (prev0 - left0)
        slabs = []
        for target in range(4):
            slab = sweep(field, [derivs[i][target] for i in range(4)], lambda i: (i,))
            slabs.append(slab + jump_r * float(right_vals[target]) + jump_l * float(left_vals[target]))
        brackets[0][chan] = jnp.stack(slabs, axis=0)
        pick1 = lambda i: (slice(None), i)
        left1 = sweep(field, left_corr, pick1)
        right1 = sweep(field, right_corr, pick1)
        next1 = lane_roll(
            jnp.where(az_flat == 0, lane_roll(up_az, ET * ER), left1), -ER
        )
        prev1 = lane_roll(
            jnp.where(az_flat == ET - 1, lane_roll(down_az, -ET * ER), right1), ER
        )
        jump_r = 0.5 * (next1 - right1)
        jump_l = 0.5 * (prev1 - left1)
        slabs = []
        for target in range(4):
            slab = sweep(field, [derivs[i][target] for i in range(4)], pick1)
            slabs.append(slab + jump_r * float(right_vals[target]) + jump_l * float(left_vals[target]))
        brackets[1][chan] = jnp.stack(slabs, axis=1)
        points = [jnp.broadcast_to(field[:, :, i : i + 1, :], shape) for i in range(4)]
        left2 = sweep(points, left_corr, lambda i: i)
        right2 = sweep(points, right_corr, lambda i: i)
        next2 = jnp.where(radial_lane == ER - 1, outer_face, lane_roll(left2, -1))
        prev2 = jnp.where(radial_lane == 0, inner_face, lane_roll(right2, 1))
        bracket = 0.5 * (next2 - right2) * column(right_vals, shape)
        bracket = bracket + 0.5 * (prev2 - left2) * column(left_vals, shape)
        for source in range(4):
            bracket = bracket + points[source] * column(derivs[source], shape)
        brackets[2][chan] = bracket
    prim = [flow_ref[0, chan].astype(jnp.float32) for chan in range(5)]
    density = prim[0]
    speed_sq = prim[1] * prim[1] + prim[2] * prim[2] + prim[3] * prim[3]
    energy = prim[4] / (GAMMA - 1.0) + 0.5 * density * speed_sq
    momentum = [density * prim[1 + k] for k in range(3)]
    velocity = [momentum[k] / density for k in range(3)]
    kinetic = momentum[0] * velocity[0] + momentum[1] * velocity[1] + momentum[2] * velocity[2]
    pressure = (GAMMA - 1.0) * (energy - 0.5 * kinetic)
    enthalpy = (energy + pressure) / density
    vel_sq = velocity[0] * velocity[0] + velocity[1] * velocity[1] + velocity[2] * velocity[2]
    grad = [None] * 5
    for direction in range(3):
        cot = brackets[direction]
        normal = velocity[direction]
        dotted = cot[1] * velocity[0] + cot[2] * velocity[1] + cot[3] * velocity[2] + cot[4] * enthalpy
        weight = cot[1 + direction] + cot[4] * normal
        terms = [
            0.5 * (GAMMA - 1.0) * vel_sq * weight - dotted * normal,
            None,
            None,
            None,
            (GAMMA - 1.0) * weight + cot[4] * normal,
        ]
        for k in range(3):
            term = cot[1 + k] * normal - (GAMMA - 1.0) * weight * velocity[k]
            if k == direction:
                term = term + (cot[0] + dotted)
            terms[1 + k] = term
        for chan in range(5):
            grad[chan] = terms[chan] if grad[chan] is None else grad[chan] + terms[chan]
    for chan in range(5):
        rate = -METRIC * grad[chan]
        rate_ref[0, chan] = rate
        next_ref[0, chan] = adj_ref[0, chan] + SECTION_STEP * rate


def local(adjoint, flow_prim, intersection_shift, weight_index, mortar_weights, sector_offset):
    n_axial = lax.axis_size("axial")
    n_azim = lax.axis_size("azim")
    face4 = jax.ShapeDtypeStruct((5, 4, 4, 128), jnp.float32)
    chunk = jax.ShapeDtypeStruct((5, 4, 128), jnp.float32)
    rows16 = jax.ShapeDtypeStruct((5, 16, 128), jnp.float32)
    left_ax, right_ax, upper_face, lower_face, own_face = pl.pallas_call(
        moment_kernel,
        out_shape=(face4, face4, chunk, chunk, jax.ShapeDtypeStruct((5, 16, EA * ET), jnp.float32)),
        scratch_shapes=[pltpu.VMEM((2, 16, 128), jnp.float32)],
    )(adjoint)
    is_rotor = lax.axis_index("zone") == 0
    even = lax.axis_index("axial") % 2 == 0
    first = [(i, i + 1) for i in range(0, n_axial - 1, 2)] + [(i, i - 1) for i in range(1, n_axial, 2)]
    second = [(i, i + 1) for i in range(1, n_axial - 1, 2)] + [(i, i - 1) for i in range(2, n_axial, 2)]
    got_first = lax.ppermute(jnp.where(even, right_ax, left_ax), "axial", first)
    if second:
        got_second = lax.ppermute(jnp.where(even, left_ax, right_ax), "axial", second)
    else:
        got_second = None
    own_rows = own_face.reshape(5, 4, 4, EA, ET).transpose(0, 3, 1, 4, 2).reshape(5, AP, TP)
    shifts_local = intersection_shift.reshape(INTERSECTIONS, AP, TP)
    table_match = weight_index[:, :, None] == jnp.arange(NW, dtype=jnp.int32)[None, None, :]
    weights_local = jnp.sum(
        jnp.where(table_match, mortar_weights[None, None, :], 0.0), axis=2
    ).reshape(INTERSECTIONS, AP, TP)
    offset = sector_offset[0]
    turn = (offset + TP // 2) // TP
    residue = offset - turn * TP
    offsets_k = residue + shifts_local
    rel_all = jnp.arange(-TP, TP - 1, dtype=jnp.int32)[:, None, None]
    coef_all = jnp.where(offsets_k[0][None] == rel_all, weights_local[0][None], 0.0)
    for member in range(1, INTERSECTIONS):
        coef_all = coef_all + jnp.where(offsets_k[member][None] == rel_all, weights_local[member][None], 0.0)
    coefs = [(rel, coef_all[rel + TP]) for rel in range(-TP, TP - 1)]
    contrib = None
    for rel, coef in coefs:
        term = jnp.pad(coef[None] * own_rows, ((0, 0), (0, 0), (TP + rel, TP - rel)))
        contrib = term if contrib is None else contrib + term
    zone = lax.axis_index("zone")
    azim = lax.axis_index("azim")
    dest = jnp.arange(2 * n_azim, dtype=jnp.int32)
    dest_azim = dest % n_azim
    gap = ((dest_azim - azim) % n_azim - turn) % n_azim
    gap = gap[:, None, None, None]
    pieces = jnp.where(
        gap == n_azim - 1,
        contrib[None, :, :, :TP],
        jnp.where(gap == 0, contrib[None, :, :, TP : 2 * TP], contrib[None, :, :, 2 * TP :]),
    )
    iface_out = jnp.where(is_rotor, jnp.broadcast_to(own_rows[None], pieces.shape), pieces)
    iface_out = jnp.pad(iface_out.reshape(2 * n_azim, 5, 2, 128), ((0, 0), (0, 0), (0, 2), (0, 0)))
    same_zone = dest // n_azim == zone
    to_prev = (same_zone & (dest_azim == (azim - 1) % n_azim))[:, None, None, None]
    to_next = (same_zone & (dest_azim == (azim + 1) % n_azim))[:, None, None, None]
    chunks = jnp.where(
        to_prev, upper_face[None], jnp.where(to_next, lower_face[None], jnp.where(same_zone[:, None, None, None], 0.0, iface_out))
    )
    got = lax.all_to_all(chunks, ("zone", "azim"), 0, 0)
    base = (1 - zone) * n_azim
    up_az = lax.dynamic_index_in_dim(got, zone * n_azim + (azim + 1) % n_azim, 0, keepdims=False)
    down_az = lax.dynamic_index_in_dim(got, zone * n_azim + (azim - 1) % n_azim, 0, keepdims=False)
    direction = jnp.where(is_rotor, -1, 1)
    picked = [
        lax.dynamic_index_in_dim(
            got, base + (azim + direction * (turn + step)) % n_azim, 0, keepdims=False
        )[:, :2].reshape(5, AP, TP)
        for step in (-1, 0, 1)
    ]
    returned = picked[0] + picked[1] + picked[2]
    window = jnp.concatenate(picked, axis=2)
    incoming = shift_sum(window, coefs, TP)
    sides = jnp.where(is_rotor, returned, incoming).reshape(5 * AP, TP)
    field_shape = jax.ShapeDtypeStruct(adjoint.shape, jnp.float32)
    operands = (adjoint, flow_prim, got_first, got_second, up_az, down_az, sides)
    kernel = rate_kernel
    if got_second is None:
        operands = (adjoint, flow_prim, got_first, up_az, down_az, sides)
        kernel = functools.partial(rate_kernel_single, rate_kernel)
    adjoint_rate, next_adjoint = pl.pallas_call(
        kernel, out_shape=(field_shape, field_shape)
    )(*operands)
    return (adjoint_rate, next_adjoint)


def solution(mesh):
    placed = (
        P("zone", None, None, None, None, ("axial", "azim")),
        P("zone", None, None, None, None, ("axial", "azim")),
        P(None, ("axial", "azim")),
        P(None, ("axial", "azim")),
        P(),
        P(),
    )
    return jax.shard_map(
        local,
        mesh=mesh,
        in_specs=placed,
        out_specs=(
            P("zone", None, None, None, None, ("axial", "azim")),
            P("zone", None, None, None, None, ("axial", "azim")),
        ),
        check_vma=False,
    )
```

```python
import functools
import math

import jax
import jax.numpy as jnp
from jax import lax
from jax.experimental import pallas as pl
from jax.experimental.pallas import tpu as pltpu
from jax.sharding import PartitionSpec as P

EA = 4
ET = 4
ER = 8
INTERSECTIONS = 4
NW = 128
AP = 16
TP = 16


GAMMA = 1.4
METRIC = 0.1
SECTION_STEP = 0.5


def gauss_nodes():
    root_term = math.sqrt(6.0 / 5.0)
    inner_node = math.sqrt(3.0 / 7.0 - 2.0 / 7.0 * root_term)
    outer_node = math.sqrt(3.0 / 7.0 + 2.0 / 7.0 * root_term)
    return [-outer_node, -inner_node, inner_node, outer_node]


def lagrange_value(node_list, column, position):
    result = 1.0
    for factor_index in range(4):
        if factor_index != column:
            result = (
                result
                * (position - node_list[factor_index])
                / (node_list[column] - node_list[factor_index])
            )
    return result


def lagrange_slope(node_list, column, position):
    total = 0.0
    for skipped in range(4):
        if skipped == column:
            continue
        term = 1.0 / (node_list[column] - node_list[skipped])
        for factor_index in range(4):
            if factor_index != column and factor_index != skipped:
                term = (
                    term
                    * (position - node_list[factor_index])
                    / (node_list[column] - node_list[factor_index])
                )
        total = total + term
    return total


def basis_tables():
    node_list = gauss_nodes()
    derivs = [
        [lagrange_slope(node_list, column, node_list[source]) for column in range(4)]
        for source in range(4)
    ]
    left_vals = [lagrange_value(node_list, column, -1.0) for column in range(4)]
    right_vals = [lagrange_value(node_list, column, 1.0) for column in range(4)]
    third_slope = [(15.0 * value * value - 3.0) / 2.0 for value in node_list]
    fourth_slope = [(35.0 * value**3 - 15.0 * value) / 2.0 for value in node_list]
    left_corr = [-0.5 * (third_slope[source] - fourth_slope[source]) for source in range(4)]
    right_corr = [0.5 * (third_slope[source] + fourth_slope[source]) for source in range(4)]
    return (derivs, left_vals, right_vals, left_corr, right_corr)


def apply_points(adj_field, matrix, point_dim):
    slab_list = [
        lax.index_in_dim(adj_field, source, point_dim, keepdims=False) for source in range(4)
    ]
    outputs = []
    for target in range(4):
        running = slab_list[0] * float(matrix[0][target])
        for source in range(1, 4):
            running = running + slab_list[source] * float(matrix[source][target])
        outputs.append(running)
    return jnp.stack(outputs, axis=point_dim)


def face_moment(adj_field, vector, point_dim):
    running = lax.index_in_dim(adj_field, 0, point_dim, keepdims=False) * float(vector[0])
    for source in range(1, 4):
        running = running + lax.index_in_dim(adj_field, source, point_dim, keepdims=False) * float(
            vector[source]
        )
    return running


def lift_face(face_vals, vector, point_dim):
    return jnp.stack([face_vals * float(vector[target]) for target in range(4)], axis=point_dim)


def conserved(primitive):
    density = primitive[0]
    velocity = primitive[1:4]
    pressure = primitive[4]
    energy = pressure / (GAMMA - 1.0) + 0.5 * density * jnp.sum(velocity * velocity, axis=0)
    return jnp.concatenate([density[None], density[None] * velocity, energy[None]], axis=0)


def euler_flux(cons_state, direction):
    density = cons_state[0]
    momentum = cons_state[1:4]
    energy = cons_state[4]
    velocity = momentum / density[None]
    pressure = (GAMMA - 1.0) * (energy - 0.5 * jnp.sum(momentum * velocity, axis=0))
    normal_speed = velocity[direction]
    columns = [momentum[direction]]
    for component in range(3):
        if component == direction:
            columns.append(momentum[component] * normal_speed + pressure)
        else:
            columns.append(momentum[component] * normal_speed)
    columns.append((energy + pressure) * normal_speed)
    return jnp.stack(columns, axis=0)


def transpose_flux(cons_state, cotangent, direction):
    unused, pullback = jax.vjp(lambda current: euler_flux(current, direction), cons_state)
    return pullback(cotangent)[0]


def section_rate(adj_field, cons_state, left_moments, right_moments, next_left, prev_right):
    derivs, left_vals, right_vals, left_corr, right_corr = basis_tables()
    rate_sum = jnp.zeros_like(adj_field)
    for direction in range(3):
        point_dim = 1 + direction
        bracket = apply_points(adj_field, derivs, point_dim)
        bracket = bracket + 0.5 * lift_face(
            next_left[direction] - right_moments[direction], right_vals, point_dim
        )
        bracket = bracket + 0.5 * lift_face(
            prev_right[direction] - left_moments[direction], left_vals, point_dim
        )
        rate_sum = rate_sum - METRIC * transpose_flux(cons_state, bracket, direction)
    return rate_sum


def all_moments(adj_field):
    derivs, left_vals, right_vals, left_corr, right_corr = basis_tables()
    left_moments = [face_moment(adj_field, left_corr, 1 + direction) for direction in range(3)]
    right_moments = [face_moment(adj_field, right_corr, 1 + direction) for direction in range(3)]
    return (left_moments, right_moments)


def faces_to_rows(face_vals):
    axial_elems = face_vals.shape[3]
    azim_elems = face_vals.shape[4]
    return face_vals.transpose(0, 3, 1, 4, 2).reshape(5, 4 * axial_elems, 4 * azim_elems)


def rows_to_face(rows_vals, axial_elems, azim_elems):
    return rows_vals.reshape(5, axial_elems, 4, azim_elems, 4).transpose(0, 2, 4, 1, 3)


def shift_sum(window, coefs, lo):
    total = None
    for offset, coef in coefs:
        term = coef[None] * window[:, :, lo + offset : lo + offset + TP]
        total = term if total is None else total + term
    return total


def lane_roll(value, shift):
    return pltpu.roll(value, shift % 128, value.ndim - 1)


def sweep(field, weights, pick):
    total = field[pick(0)] * float(weights[0])
    for source in range(1, 4):
        total = total + field[pick(source)] * float(weights[source])
    return total


def column(values, shape):
    rows = lax.broadcasted_iota(jnp.int32, shape, 2)
    out = jnp.full(shape, float(values[3]), jnp.float32)
    for index in range(3):
        out = jnp.where(rows == index, float(values[index]), out)
    return out


def compact_face(face, part):
    lane = lax.broadcasted_iota(jnp.int32, (4, 128), 1)
    out = jnp.zeros((4, 128), jnp.float32)
    for block in range(4):
        for group in range(EA):
            shift = block * ET * ER - group * (ET - 1) * ER - part * ER
            start = block * ET * ER + group * ER
            mask = (lane >= start) & (lane < start + ER)
            out = jnp.where(mask, lane_roll(face[block], shift), out)
    return out


def expand_face(chunk, part):
    lane = lax.broadcasted_iota(jnp.int32, (4, 128), 1)
    group_of = lane // (ET * ER)
    in_part = lane // ER % ET == part
    blocks = []
    for block in range(4):
        out = jnp.zeros((4, 128), jnp.float32)
        for group in range(EA):
            shift = block * ET * ER - group * (ET - 1) * ER - part * ER
            out = jnp.where(in_part & (group_of == group), lane_roll(chunk, -shift), out)
        blocks.append(out)
    return jnp.stack(blocks, axis=0)


def selector(rows, cols, lane_of, use_rows):
    row = lax.broadcasted_iota(jnp.int32, (rows, cols), 0)
    col = lax.broadcasted_iota(jnp.int32, (rows, cols), 1)
    if use_rows:
        hit = (row == lane_of(col)) & (row < EA * ET)
    else:
        hit = (row == lane_of(col)) & (col < EA * ET)
    return jnp.where(hit, 1.0, 0.0)


def exact_dot(left, right):
    return jnp.dot(left, right, precision=lax.Precision.HIGHEST, preferred_element_type=jnp.float32)


def moment_kernel(adj_ref, left_ax_ref, right_ax_ref, up_ref, down_ref, own_ref, scratch_ref):
    derivs, left_vals, right_vals, left_corr, right_corr = basis_tables()
    pick_outer = selector(128, 128, lambda k: k // ET * ET * ER + k % ET * ER + ER - 1, False)
    pick_inner = selector(128, 128, lambda k: k // ET * ET * ER + k % ET * ER, False)
    rotor = lax.axis_index("zone") == 0
    pick = jnp.where(rotor, pick_outer, pick_inner)
    for chan in range(5):
        field = adj_ref[0, chan]
        left_ax_ref[chan] = sweep(field, left_corr, lambda i: (i,))
        right_ax_ref[chan] = sweep(field, right_corr, lambda i: (i,))
        pick1 = lambda i: (slice(None), i)
        up_ref[chan] = compact_face(sweep(field, left_corr, pick1), 0)
        down_ref[chan] = compact_face(sweep(field, right_corr, pick1), ET - 1)
        pick2 = lambda i: (slice(None), slice(None), slice(i, i + 1))
        outer = sweep(field, right_corr, pick2)
        inner = sweep(field, left_corr, pick2)
        for axial in range(4):
            for azim in range(4):
                row = axial * 4 + azim
                scratch_ref[0, row : row + 1] = outer[axial, azim]
                scratch_ref[1, row : row + 1] = inner[axial, azim]
        rows = jnp.where(rotor, scratch_ref[0], scratch_ref[1])
        own_ref[chan] = exact_dot(rows, pick)[:, : EA * ET]


def flow_terms(flow_ref):
    prim = [flow_ref[0, chan].astype(jnp.float32) for chan in range(5)]
    density = prim[0]
    speed_sq = prim[1] * prim[1] + prim[2] * prim[2] + prim[3] * prim[3]
    energy = prim[4] / (GAMMA - 1.0) + 0.5 * density * speed_sq
    momentum = [density * prim[1 + k] for k in range(3)]
    velocity = [momentum[k] / density for k in range(3)]
    kinetic = momentum[0] * velocity[0] + momentum[1] * velocity[1] + momentum[2] * velocity[2]
    pressure = (GAMMA - 1.0) * (energy - 0.5 * kinetic)
    enthalpy = (energy + pressure) / density
    vel_sq = velocity[0] * velocity[0] + velocity[1] * velocity[1] + velocity[2] * velocity[2]
    return velocity, enthalpy, vel_sq


def flux_transpose(grad, cot, direction, velocity, enthalpy, vel_sq):
    normal = velocity[direction]
    dotted = cot[1] * velocity[0] + cot[2] * velocity[1] + cot[3] * velocity[2] + cot[4] * enthalpy
    weight = cot[1 + direction] + cot[4] * normal
    terms = [
        0.5 * (GAMMA - 1.0) * vel_sq * weight - dotted * normal,
        None,
        None,
        None,
        (GAMMA - 1.0) * weight + cot[4] * normal,
    ]
    for k in range(3):
        term = cot[1 + k] * normal - (GAMMA - 1.0) * weight * velocity[k]
        if k == direction:
            term = term + (cot[0] + dotted)
        terms[1 + k] = term
    return [terms[c] if grad[c] is None else grad[c] + terms[c] for c in range(5)]


def early_kernel(adj_ref, flow_ref, first_ref, *rest):
    if len(rest) == 2:
        second_ref, grad_ref = rest
    else:
        second_ref, grad_ref = None, rest[0]
    derivs, left_vals, right_vals, left_corr, right_corr = basis_tables()
    shape = (4, 4, 4, 128)
    lane = lax.broadcasted_iota(jnp.int32, shape, 3)
    flat_lane = lax.broadcasted_iota(jnp.int32, (4, 4, 128), 2)
    radial_lane = lane % ER
    even = lax.axis_index("axial") % 2 == 0
    brackets = [[None] * 5 for _ in range(3)]
    for chan in range(5):
        field = adj_ref[0, chan]
        first = first_ref[chan]
        second = first * 0.0 if second_ref is None else second_ref[chan]
        up_ax = jnp.where(even, first, second)
        down_ax = jnp.where(even, second, first)
        left0 = sweep(field, left_corr, lambda i: (i,))
        right0 = sweep(field, right_corr, lambda i: (i,))
        next0 = lane_roll(jnp.where(flat_lane < ET * ER, up_ax, left0), -ET * ER)
        prev0 = lane_roll(jnp.where(flat_lane >= (EA - 1) * ET * ER, down_ax, right0), ET * ER)
        jump_r = 0.5 * (next0 - right0)
        jump_l = 0.5 * (prev0 - left0)
        slabs = []
        for target in range(4):
            slab = sweep(field, [derivs[i][target] for i in range(4)], lambda i: (i,))
            slabs.append(slab + jump_r * float(right_vals[target]) + jump_l * float(left_vals[target]))
        brackets[0][chan] = jnp.stack(slabs, axis=0)
        points = [jnp.broadcast_to(field[:, :, i : i + 1, :], shape) for i in range(4)]
        left2 = sweep(points, left_corr, lambda i: i)
        right2 = sweep(points, right_corr, lambda i: i)
        next2 = jnp.where(radial_lane == ER - 1, 0.0, lane_roll(left2, -1))
        prev2 = jnp.where(radial_lane == 0, 0.0, lane_roll(right2, 1))
        bracket = 0.5 * (next2 - right2) * column(right_vals, shape)
        bracket = bracket + 0.5 * (prev2 - left2) * column(left_vals, shape)
        for source in range(4):
            bracket = bracket + points[source] * column(derivs[source], shape)
        brackets[2][chan] = bracket
    velocity, enthalpy, vel_sq = flow_terms(flow_ref)
    grad = [None] * 5
    for direction in (0, 2):
        grad = flux_transpose(grad, brackets[direction], direction, velocity, enthalpy, vel_sq)
    for chan in range(5):
        grad_ref[0, chan] = grad[chan]


def late_kernel(adj_ref, flow_ref, grad_ref, up_az_ref, down_az_ref, sides_ref, rate_ref, next_ref):
    derivs, left_vals, right_vals, left_corr, right_corr = basis_tables()
    shape = (4, 4, 4, 128)
    lane = lax.broadcasted_iota(jnp.int32, shape, 3)
    flat_lane = lax.broadcasted_iota(jnp.int32, (4, 4, 128), 2)
    az_flat = flat_lane // ER % ET
    radial_lane = lane % ER
    col = lax.broadcasted_iota(jnp.int32, (16, 128), 1)
    row = lax.broadcasted_iota(jnp.int32, (16, 128), 0)
    sides = sides_ref[...]
    rotor = lax.axis_index("zone") == 0
    spread = [
        exact_dot(sides, jnp.where(row == col // ER % ET * 4 + azim, 1.0, 0.0)) for azim in range(4)
    ]
    group = lax.broadcasted_iota(jnp.int32, (1, 128), 1) // (ET * ER)

    def side_face(chan):
        blocks = []
        for axial in range(4):
            slabs = []
            for azim in range(4):
                base = chan * 16 + axial
                value = spread[azim][base : base + 1]
                for elem in range(1, EA):
                    pos = base + elem * 4
                    value = jnp.where(group == elem, spread[azim][pos : pos + 1], value)
                slabs.append(jnp.broadcast_to(value, (4, 128)))
            blocks.append(jnp.stack(slabs, axis=0))
        return jnp.stack(blocks, axis=0)

    azim_b = [None] * 5
    radial_b = [None] * 5
    for chan in range(5):
        field = adj_ref[0, chan]
        own_face = side_face(chan)
        outer_face = jnp.where(rotor & (radial_lane == ER - 1), own_face, 0.0)
        inner_face = jnp.where(rotor | (radial_lane != 0), 0.0, own_face)
        radial_b[chan] = 0.5 * outer_face * column(right_vals, shape) + 0.5 * inner_face * column(
            left_vals, shape
        )
        up_az = expand_face(up_az_ref[chan], 0)
        down_az = expand_face(down_az_ref[chan], ET - 1)
        pick1 = lambda i: (slice(None), i)
        left1 = sweep(field, left_corr, pick1)
        right1 = sweep(field, right_corr, pick1)
        next1 = lane_roll(jnp.where(az_flat == 0, lane_roll(up_az, ET * ER), left1), -ER)
        prev1 = lane_roll(jnp.where(az_flat == ET - 1, lane_roll(down_az, -ET * ER), right1), ER)
        jump_r = 0.5 * (next1 - right1)
        jump_l = 0.5 * (prev1 - left1)
        slabs = []
        for target in range(4):
            slab = sweep(field, [derivs[i][target] for i in range(4)], pick1)
            slabs.append(slab + jump_r * float(right_vals[target]) + jump_l * float(left_vals[target]))
        azim_b[chan] = jnp.stack(slabs, axis=1)
    velocity, enthalpy, vel_sq = flow_terms(flow_ref)
    grad = [grad_ref[0, chan] for chan in range(5)]
    grad = flux_transpose(grad, azim_b, 1, velocity, enthalpy, vel_sq)
    grad = flux_transpose(grad, radial_b, 2, velocity, enthalpy, vel_sq)
    for chan in range(5):
        rate = -METRIC * grad[chan]
        rate_ref[0, chan] = rate
        next_ref[0, chan] = adj_ref[0, chan] + SECTION_STEP * rate


def local(adjoint, flow_prim, intersection_shift, weight_index, mortar_weights, sector_offset):
    n_axial = lax.axis_size("axial")
    n_azim = lax.axis_size("azim")
    face4 = jax.ShapeDtypeStruct((5, 4, 4, 128), jnp.float32)
    chunk = jax.ShapeDtypeStruct((5, 4, 128), jnp.float32)
    rows16 = jax.ShapeDtypeStruct((5, 16, 128), jnp.float32)
    left_ax, right_ax, upper_face, lower_face, own_face = pl.pallas_call(
        moment_kernel,
        out_shape=(face4, face4, chunk, chunk, jax.ShapeDtypeStruct((5, 16, EA * ET), jnp.float32)),
        scratch_shapes=[pltpu.VMEM((2, 16, 128), jnp.float32)],
    )(adjoint)
    is_rotor = lax.axis_index("zone") == 0
    even = lax.axis_index("axial") % 2 == 0
    first = [(i, i + 1) for i in range(0, n_axial - 1, 2)] + [(i, i - 1) for i in range(1, n_axial, 2)]
    second = [(i, i + 1) for i in range(1, n_axial - 1, 2)] + [(i, i - 1) for i in range(2, n_axial, 2)]
    got_first = lax.ppermute(jnp.where(even, right_ax, left_ax), "axial", first)
    if second:
        got_second = lax.ppermute(jnp.where(even, left_ax, right_ax), "axial", second)
    else:
        got_second = None
    own_rows = own_face.reshape(5, 4, 4, EA, ET).transpose(0, 3, 1, 4, 2).reshape(5, AP, TP)
    shifts_local = intersection_shift.reshape(INTERSECTIONS, AP, TP)
    table_match = weight_index[:, :, None] == jnp.arange(NW, dtype=jnp.int32)[None, None, :]
    weights_local = jnp.sum(
        jnp.where(table_match, mortar_weights[None, None, :], 0.0), axis=2
    ).reshape(INTERSECTIONS, AP, TP)
    offset = sector_offset[0]
    turn = (offset + TP // 2) // TP
    residue = offset - turn * TP
    offsets_k = residue + shifts_local
    rel_all = jnp.arange(-TP, TP - 1, dtype=jnp.int32)[:, None, None]
    coef_all = jnp.where(offsets_k[0][None] == rel_all, weights_local[0][None], 0.0)
    for member in range(1, INTERSECTIONS):
        coef_all = coef_all + jnp.where(offsets_k[member][None] == rel_all, weights_local[member][None], 0.0)
    coefs = [(rel, coef_all[rel + TP]) for rel in range(-TP, TP - 1)]
    contrib = None
    for rel, coef in coefs:
        term = jnp.pad(coef[None] * own_rows, ((0, 0), (0, 0), (TP + rel, TP - rel)))
        contrib = term if contrib is None else contrib + term
    zone = lax.axis_index("zone")
    azim = lax.axis_index("azim")
    dest = jnp.arange(2 * n_azim, dtype=jnp.int32)
    dest_azim = dest % n_azim
    gap = ((dest_azim - azim) % n_azim - turn) % n_azim
    gap = gap[:, None, None, None]
    pieces = jnp.where(
        gap == n_azim - 1,
        contrib[None, :, :, :TP],
        jnp.where(gap == 0, contrib[None, :, :, TP : 2 * TP], contrib[None, :, :, 2 * TP :]),
    )
    iface_out = jnp.where(is_rotor, jnp.broadcast_to(own_rows[None], pieces.shape), pieces)
    iface_out = jnp.pad(iface_out.reshape(2 * n_azim, 5, 2, 128), ((0, 0), (0, 0), (0, 2), (0, 0)))
    same_zone = dest // n_azim == zone
    to_prev = (same_zone & (dest_azim == (azim - 1) % n_azim))[:, None, None, None]
    to_next = (same_zone & (dest_azim == (azim + 1) % n_azim))[:, None, None, None]
    chunks = jnp.where(
        to_prev, upper_face[None], jnp.where(to_next, lower_face[None], jnp.where(same_zone[:, None, None, None], 0.0, iface_out))
    )
    got = lax.all_to_all(chunks, ("zone", "azim"), 0, 0)
    base = (1 - zone) * n_azim
    up_az = lax.dynamic_index_in_dim(got, zone * n_azim + (azim + 1) % n_azim, 0, keepdims=False)
    down_az = lax.dynamic_index_in_dim(got, zone * n_azim + (azim - 1) % n_azim, 0, keepdims=False)
    direction = jnp.where(is_rotor, -1, 1)
    picked = [
        lax.dynamic_index_in_dim(
            got, base + (azim + direction * (turn + step)) % n_azim, 0, keepdims=False
        )[:, :2].reshape(5, AP, TP)
        for step in (-1, 0, 1)
    ]
    returned = picked[0] + picked[1] + picked[2]
    window = jnp.concatenate(picked, axis=2)
    incoming = shift_sum(window, coefs, TP)
    sides = jnp.where(is_rotor, returned, incoming).reshape(5 * AP, TP)
    field_shape = jax.ShapeDtypeStruct(adjoint.shape, jnp.float32)
    early_in = (adjoint, flow_prim, got_first) + (() if got_second is None else (got_second,))
    partial = pl.pallas_call(early_kernel, out_shape=field_shape)(*early_in)
    adjoint_rate, next_adjoint = pl.pallas_call(late_kernel, out_shape=(field_shape, field_shape))(
        adjoint, flow_prim, partial, up_az, down_az, sides
    )
    return (adjoint_rate, next_adjoint)


def solution(mesh):
    placed = (
        P("zone", None, None, None, None, ("axial", "azim")),
        P("zone", None, None, None, None, ("axial", "azim")),
        P(None, ("axial", "azim")),
        P(None, ("axial", "azim")),
        P(),
        P(),
    )
    return jax.shard_map(
        local,
        mesh=mesh,
        in_specs=placed,
        out_specs=(
            P("zone", None, None, None, None, ("axial", "azim")),
            P("zone", None, None, None, None, ("axial", "azim")),
        ),
        check_vma=False,
    )
```

```python
import functools
import math

import jax
import jax.numpy as jnp
from jax import lax
from jax.experimental import pallas as pl
from jax.experimental.pallas import tpu as pltpu
from jax.sharding import PartitionSpec as P

EA = 4
ET = 4
ER = 8
INTERSECTIONS = 4
NW = 128
AP = 16
TP = 16


GAMMA = 1.4
METRIC = 0.1
SECTION_STEP = 0.5


def gauss_nodes():
    root_term = math.sqrt(6.0 / 5.0)
    inner_node = math.sqrt(3.0 / 7.0 - 2.0 / 7.0 * root_term)
    outer_node = math.sqrt(3.0 / 7.0 + 2.0 / 7.0 * root_term)
    return [-outer_node, -inner_node, inner_node, outer_node]


def lagrange_value(node_list, column, position):
    result = 1.0
    for factor_index in range(4):
        if factor_index != column:
            result = (
                result
                * (position - node_list[factor_index])
                / (node_list[column] - node_list[factor_index])
            )
    return result


def lagrange_slope(node_list, column, position):
    total = 0.0
    for skipped in range(4):
        if skipped == column:
            continue
        term = 1.0 / (node_list[column] - node_list[skipped])
        for factor_index in range(4):
            if factor_index != column and factor_index != skipped:
                term = (
                    term
                    * (position - node_list[factor_index])
                    / (node_list[column] - node_list[factor_index])
                )
        total = total + term
    return total


def basis_tables():
    node_list = gauss_nodes()
    derivs = [
        [lagrange_slope(node_list, column, node_list[source]) for column in range(4)]
        for source in range(4)
    ]
    left_vals = [lagrange_value(node_list, column, -1.0) for column in range(4)]
    right_vals = [lagrange_value(node_list, column, 1.0) for column in range(4)]
    third_slope = [(15.0 * value * value - 3.0) / 2.0 for value in node_list]
    fourth_slope = [(35.0 * value**3 - 15.0 * value) / 2.0 for value in node_list]
    left_corr = [-0.5 * (third_slope[source] - fourth_slope[source]) for source in range(4)]
    right_corr = [0.5 * (third_slope[source] + fourth_slope[source]) for source in range(4)]
    return (derivs, left_vals, right_vals, left_corr, right_corr)


def apply_points(adj_field, matrix, point_dim):
    slab_list = [
        lax.index_in_dim(adj_field, source, point_dim, keepdims=False) for source in range(4)
    ]
    outputs = []
    for target in range(4):
        running = slab_list[0] * float(matrix[0][target])
        for source in range(1, 4):
            running = running + slab_list[source] * float(matrix[source][target])
        outputs.append(running)
    return jnp.stack(outputs, axis=point_dim)


def face_moment(adj_field, vector, point_dim):
    running = lax.index_in_dim(adj_field, 0, point_dim, keepdims=False) * float(vector[0])
    for source in range(1, 4):
        running = running + lax.index_in_dim(adj_field, source, point_dim, keepdims=False) * float(
            vector[source]
        )
    return running


def lift_face(face_vals, vector, point_dim):
    return jnp.stack([face_vals * float(vector[target]) for target in range(4)], axis=point_dim)


def conserved(primitive):
    density = primitive[0]
    velocity = primitive[1:4]
    pressure = primitive[4]
    energy = pressure / (GAMMA - 1.0) + 0.5 * density * jnp.sum(velocity * velocity, axis=0)
    return jnp.concatenate([density[None], density[None] * velocity, energy[None]], axis=0)


def euler_flux(cons_state, direction):
    density = cons_state[0]
    momentum = cons_state[1:4]
    energy = cons_state[4]
    velocity = momentum / density[None]
    pressure = (GAMMA - 1.0) * (energy - 0.5 * jnp.sum(momentum * velocity, axis=0))
    normal_speed = velocity[direction]
    columns = [momentum[direction]]
    for component in range(3):
        if component == direction:
            columns.append(momentum[component] * normal_speed + pressure)
        else:
            columns.append(momentum[component] * normal_speed)
    columns.append((energy + pressure) * normal_speed)
    return jnp.stack(columns, axis=0)


def transpose_flux(cons_state, cotangent, direction):
    unused, pullback = jax.vjp(lambda current: euler_flux(current, direction), cons_state)
    return pullback(cotangent)[0]


def section_rate(adj_field, cons_state, left_moments, right_moments, next_left, prev_right):
    derivs, left_vals, right_vals, left_corr, right_corr = basis_tables()
    rate_sum = jnp.zeros_like(adj_field)
    for direction in range(3):
        point_dim = 1 + direction
        bracket = apply_points(adj_field, derivs, point_dim)
        bracket = bracket + 0.5 * lift_face(
            next_left[direction] - right_moments[direction], right_vals, point_dim
        )
        bracket = bracket + 0.5 * lift_face(
            prev_right[direction] - left_moments[direction], left_vals, point_dim
        )
        rate_sum = rate_sum - METRIC * transpose_flux(cons_state, bracket, direction)
    return rate_sum


def all_moments(adj_field):
    derivs, left_vals, right_vals, left_corr, right_corr = basis_tables()
    left_moments = [face_moment(adj_field, left_corr, 1 + direction) for direction in range(3)]
    right_moments = [face_moment(adj_field, right_corr, 1 + direction) for direction in range(3)]
    return (left_moments, right_moments)


def faces_to_rows(face_vals):
    axial_elems = face_vals.shape[3]
    azim_elems = face_vals.shape[4]
    return face_vals.transpose(0, 3, 1, 4, 2).reshape(5, 4 * axial_elems, 4 * azim_elems)


def rows_to_face(rows_vals, axial_elems, azim_elems):
    return rows_vals.reshape(5, axial_elems, 4, azim_elems, 4).transpose(0, 2, 4, 1, 3)


def shift_sum(window, coefs, lo):
    total = None
    for offset, coef in coefs:
        term = coef[None] * window[:, :, lo + offset : lo + offset + TP]
        total = term if total is None else total + term
    return total


def lane_roll(value, shift):
    return pltpu.roll(value, shift % 128, value.ndim - 1)


def sweep(field, weights, pick):
    total = field[pick(0)] * float(weights[0])
    for source in range(1, 4):
        total = total + field[pick(source)] * float(weights[source])
    return total


def column(values, shape):
    rows = lax.broadcasted_iota(jnp.int32, shape, 2)
    out = jnp.full(shape, float(values[3]), jnp.float32)
    for index in range(3):
        out = jnp.where(rows == index, float(values[index]), out)
    return out


def compact_face(face, part):
    lane = lax.broadcasted_iota(jnp.int32, (4, 128), 1)
    out = jnp.zeros((4, 128), jnp.float32)
    for block in range(4):
        for group in range(EA):
            shift = block * ET * ER - group * (ET - 1) * ER - part * ER
            start = block * ET * ER + group * ER
            mask = (lane >= start) & (lane < start + ER)
            out = jnp.where(mask, lane_roll(face[block], shift), out)
    return out


def expand_face(chunk, part):
    lane = lax.broadcasted_iota(jnp.int32, (4, 128), 1)
    group_of = lane // (ET * ER)
    in_part = lane // ER % ET == part
    blocks = []
    for block in range(4):
        out = jnp.zeros((4, 128), jnp.float32)
        for group in range(EA):
            shift = block * ET * ER - group * (ET - 1) * ER - part * ER
            out = jnp.where(in_part & (group_of == group), lane_roll(chunk, -shift), out)
        blocks.append(out)
    return jnp.stack(blocks, axis=0)


def selector(rows, cols, lane_of, use_rows):
    row = lax.broadcasted_iota(jnp.int32, (rows, cols), 0)
    col = lax.broadcasted_iota(jnp.int32, (rows, cols), 1)
    if use_rows:
        hit = (row == lane_of(col)) & (row < EA * ET)
    else:
        hit = (row == lane_of(col)) & (col < EA * ET)
    return jnp.where(hit, 1.0, 0.0)


def exact_dot(left, right):
    return jnp.dot(left, right, precision=lax.Precision.HIGHEST, preferred_element_type=jnp.float32)


def moment_kernel(adj_ref, left_ax_ref, right_ax_ref, up_ref, down_ref, own_ref, scratch_ref):
    derivs, left_vals, right_vals, left_corr, right_corr = basis_tables()
    pick_outer = selector(128, 128, lambda k: k // ET * ET * ER + k % ET * ER + ER - 1, False)
    pick_inner = selector(128, 128, lambda k: k // ET * ET * ER + k % ET * ER, False)
    rotor = lax.axis_index("zone") == 0
    pick = jnp.where(rotor, pick_outer, pick_inner)
    for chan in range(5):
        field = adj_ref[0, chan]
        left_ax_ref[chan] = sweep(field, left_corr, lambda i: (i,))
        right_ax_ref[chan] = sweep(field, right_corr, lambda i: (i,))
        pick1 = lambda i: (slice(None), i)
        up_ref[chan] = compact_face(sweep(field, left_corr, pick1), 0)
        down_ref[chan] = compact_face(sweep(field, right_corr, pick1), ET - 1)
        pick2 = lambda i: (slice(None), slice(None), slice(i, i + 1))
        outer = sweep(field, right_corr, pick2)
        inner = sweep(field, left_corr, pick2)
        for axial in range(4):
            for azim in range(4):
                row = axial * 4 + azim
                scratch_ref[0, row : row + 1] = outer[axial, azim]
                scratch_ref[1, row : row + 1] = inner[axial, azim]
        rows = jnp.where(rotor, scratch_ref[0], scratch_ref[1])
        own_ref[chan] = exact_dot(rows, pick)[:, : EA * ET]


def flow_terms(flow_ref):
    prim = [flow_ref[0, chan].astype(jnp.float32) for chan in range(5)]
    density = prim[0]
    speed_sq = prim[1] * prim[1] + prim[2] * prim[2] + prim[3] * prim[3]
    energy = prim[4] / (GAMMA - 1.0) + 0.5 * density * speed_sq
    momentum = [density * prim[1 + k] for k in range(3)]
    velocity = [momentum[k] / density for k in range(3)]
    kinetic = momentum[0] * velocity[0] + momentum[1] * velocity[1] + momentum[2] * velocity[2]
    pressure = (GAMMA - 1.0) * (energy - 0.5 * kinetic)
    enthalpy = (energy + pressure) / density
    vel_sq = velocity[0] * velocity[0] + velocity[1] * velocity[1] + velocity[2] * velocity[2]
    return velocity, enthalpy, vel_sq


def flux_transpose(grad, cot, direction, velocity, enthalpy, vel_sq):
    normal = velocity[direction]
    dotted = cot[1] * velocity[0] + cot[2] * velocity[1] + cot[3] * velocity[2] + cot[4] * enthalpy
    weight = cot[1 + direction] + cot[4] * normal
    terms = [
        0.5 * (GAMMA - 1.0) * vel_sq * weight - dotted * normal,
        None,
        None,
        None,
        (GAMMA - 1.0) * weight + cot[4] * normal,
    ]
    for k in range(3):
        term = cot[1 + k] * normal - (GAMMA - 1.0) * weight * velocity[k]
        if k == direction:
            term = term + (cot[0] + dotted)
        terms[1 + k] = term
    return [terms[c] if grad[c] is None else grad[c] + terms[c] for c in range(5)]


def early_kernel(adj_ref, flow_ref, first_ref, *rest):
    if len(rest) == 2:
        second_ref, grad_ref = rest
    else:
        second_ref, grad_ref = None, rest[0]
    derivs, left_vals, right_vals, left_corr, right_corr = basis_tables()
    shape = (4, 4, 4, 128)
    lane = lax.broadcasted_iota(jnp.int32, shape, 3)
    flat_lane = lax.broadcasted_iota(jnp.int32, (4, 4, 128), 2)
    radial_lane = lane % ER
    even = lax.axis_index("axial") % 2 == 0
    brackets = [[None] * 5 for _ in range(3)]
    for chan in range(5):
        field = adj_ref[0, chan]
        first = first_ref[chan]
        second = first * 0.0 if second_ref is None else second_ref[chan]
        up_ax = jnp.where(even, first, second)
        down_ax = jnp.where(even, second, first)
        left0 = sweep(field, left_corr, lambda i: (i,))
        right0 = sweep(field, right_corr, lambda i: (i,))
        next0 = lane_roll(jnp.where(flat_lane < ET * ER, up_ax, left0), -ET * ER)
        prev0 = lane_roll(jnp.where(flat_lane >= (EA - 1) * ET * ER, down_ax, right0), ET * ER)
        jump_r = 0.5 * (next0 - right0)
        jump_l = 0.5 * (prev0 - left0)
        slabs = []
        for target in range(4):
            slab = sweep(field, [derivs[i][target] for i in range(4)], lambda i: (i,))
            slabs.append(slab + jump_r * float(right_vals[target]) + jump_l * float(left_vals[target]))
        brackets[0][chan] = jnp.stack(slabs, axis=0)
        points = [jnp.broadcast_to(field[:, :, i : i + 1, :], shape) for i in range(4)]
        left2 = sweep(points, left_corr, lambda i: i)
        right2 = sweep(points, right_corr, lambda i: i)
        next2 = jnp.where(radial_lane == ER - 1, 0.0, lane_roll(left2, -1))
        prev2 = jnp.where(radial_lane == 0, 0.0, lane_roll(right2, 1))
        bracket = 0.5 * (next2 - right2) * column(right_vals, shape)
        bracket = bracket + 0.5 * (prev2 - left2) * column(left_vals, shape)
        for source in range(4):
            bracket = bracket + points[source] * column(derivs[source], shape)
        brackets[2][chan] = bracket
    velocity, enthalpy, vel_sq = flow_terms(flow_ref)
    grad = [None] * 5
    for direction in (0, 2):
        grad = flux_transpose(grad, brackets[direction], direction, velocity, enthalpy, vel_sq)
    for chan in range(5):
        grad_ref[0, chan] = grad[chan]


def late_kernel(adj_ref, flow_ref, grad_ref, up_az_ref, down_az_ref, returned_ref, incoming_ref, rate_ref, next_ref):
    derivs, left_vals, right_vals, left_corr, right_corr = basis_tables()
    shape = (4, 4, 4, 128)
    lane = lax.broadcasted_iota(jnp.int32, shape, 3)
    flat_lane = lax.broadcasted_iota(jnp.int32, (4, 4, 128), 2)
    az_flat = flat_lane // ER % ET
    radial_lane = lane % ER
    col = lax.broadcasted_iota(jnp.int32, (16, 128), 1)
    row = lax.broadcasted_iota(jnp.int32, (16, 128), 0)
    rotor = lax.axis_index("zone") == 0
    sides = jnp.where(rotor, returned_ref[...], incoming_ref[...])
    spread = [
        exact_dot(sides, jnp.where(row == col // ER % ET * 4 + azim, 1.0, 0.0)) for azim in range(4)
    ]
    group = lax.broadcasted_iota(jnp.int32, (1, 128), 1) // (ET * ER)

    def side_face(chan):
        blocks = []
        for axial in range(4):
            slabs = []
            for azim in range(4):
                base = chan * 16 + axial
                value = spread[azim][base : base + 1]
                for elem in range(1, EA):
                    pos = base + elem * 4
                    value = jnp.where(group == elem, spread[azim][pos : pos + 1], value)
                slabs.append(jnp.broadcast_to(value, (4, 128)))
            blocks.append(jnp.stack(slabs, axis=0))
        return jnp.stack(blocks, axis=0)

    azim_b = [None] * 5
    radial_b = [None] * 5
    for chan in range(5):
        field = adj_ref[0, chan]
        own_face = side_face(chan)
        outer_face = jnp.where(rotor & (radial_lane == ER - 1), own_face, 0.0)
        inner_face = jnp.where(rotor | (radial_lane != 0), 0.0, own_face)
        radial_b[chan] = 0.5 * outer_face * column(right_vals, shape) + 0.5 * inner_face * column(
            left_vals, shape
        )
        up_az = expand_face(up_az_ref[chan], 0)
        down_az = expand_face(down_az_ref[chan], ET - 1)
        pick1 = lambda i: (slice(None), i)
        left1 = sweep(field, left_corr, pick1)
        right1 = sweep(field, right_corr, pick1)
        next1 = lane_roll(jnp.where(az_flat == 0, lane_roll(up_az, ET * ER), left1), -ER)
        prev1 = lane_roll(jnp.where(az_flat == ET - 1, lane_roll(down_az, -ET * ER), right1), ER)
        jump_r = 0.5 * (next1 - right1)
        jump_l = 0.5 * (prev1 - left1)
        slabs = []
        for target in range(4):
            slab = sweep(field, [derivs[i][target] for i in range(4)], pick1)
            slabs.append(slab + jump_r * float(right_vals[target]) + jump_l * float(left_vals[target]))
        azim_b[chan] = jnp.stack(slabs, axis=1)
    velocity, enthalpy, vel_sq = flow_terms(flow_ref)
    grad = [grad_ref[0, chan] for chan in range(5)]
    grad = flux_transpose(grad, azim_b, 1, velocity, enthalpy, vel_sq)
    grad = flux_transpose(grad, radial_b, 2, velocity, enthalpy, vel_sq)
    for chan in range(5):
        rate = -METRIC * grad[chan]
        rate_ref[0, chan] = rate
        next_ref[0, chan] = adj_ref[0, chan] + SECTION_STEP * rate


def local(adjoint, flow_prim, intersection_shift, weight_index, mortar_weights, sector_offset):
    n_axial = lax.axis_size("axial")
    n_azim = lax.axis_size("azim")
    face4 = jax.ShapeDtypeStruct((5, 4, 4, 128), jnp.float32)
    chunk = jax.ShapeDtypeStruct((5, 4, 128), jnp.float32)
    rows16 = jax.ShapeDtypeStruct((5, 16, 128), jnp.float32)
    left_ax, right_ax, upper_face, lower_face, own_face = pl.pallas_call(
        moment_kernel,
        out_shape=(face4, face4, chunk, chunk, jax.ShapeDtypeStruct((5, 16, EA * ET), jnp.float32)),
        scratch_shapes=[pltpu.VMEM((2, 16, 128), jnp.float32)],
    )(adjoint)
    is_rotor = lax.axis_index("zone") == 0
    even = lax.axis_index("axial") % 2 == 0
    first = [(i, i + 1) for i in range(0, n_axial - 1, 2)] + [(i, i - 1) for i in range(1, n_axial, 2)]
    second = [(i, i + 1) for i in range(1, n_axial - 1, 2)] + [(i, i - 1) for i in range(2, n_axial, 2)]
    got_first = lax.ppermute(jnp.where(even, right_ax, left_ax), "axial", first)
    if second:
        got_second = lax.ppermute(jnp.where(even, left_ax, right_ax), "axial", second)
    else:
        got_second = None
    own_rows = own_face.reshape(5, 4, 4, EA, ET).transpose(0, 3, 1, 4, 2).reshape(5, AP, TP)
    shifts_local = intersection_shift.reshape(INTERSECTIONS, AP, TP)
    table_match = weight_index[:, :, None] == jnp.arange(NW, dtype=jnp.int32)[None, None, :]
    weights_local = jnp.sum(
        jnp.where(table_match, mortar_weights[None, None, :], 0.0), axis=2
    ).reshape(INTERSECTIONS, AP, TP)
    offset = sector_offset[0]
    turn = (offset + TP // 2) // TP
    residue = offset - turn * TP
    offsets_k = residue + shifts_local
    rel_all = jnp.arange(-TP, TP - 1, dtype=jnp.int32)[:, None, None]
    coef_all = jnp.where(offsets_k[0][None] == rel_all, weights_local[0][None], 0.0)
    for member in range(1, INTERSECTIONS):
        coef_all = coef_all + jnp.where(offsets_k[member][None] == rel_all, weights_local[member][None], 0.0)
    coefs = [(rel, coef_all[rel + TP]) for rel in range(-TP, TP - 1)]
    contrib = None
    for rel, coef in coefs:
        term = jnp.pad(coef[None] * own_rows, ((0, 0), (0, 0), (TP + rel, TP - rel)))
        contrib = term if contrib is None else contrib + term
    zone = lax.axis_index("zone")
    azim = lax.axis_index("azim")
    dest = jnp.arange(2 * n_azim, dtype=jnp.int32)
    dest_azim = dest % n_azim
    gap = ((dest_azim - azim) % n_azim - turn) % n_azim
    gap = gap[:, None, None, None]
    pieces = jnp.where(
        gap == n_azim - 1,
        contrib[None, :, :, :TP],
        jnp.where(gap == 0, contrib[None, :, :, TP : 2 * TP], contrib[None, :, :, 2 * TP :]),
    )
    iface_out = jnp.where(is_rotor, jnp.broadcast_to(own_rows[None], pieces.shape), pieces)
    iface_out = jnp.pad(iface_out.reshape(2 * n_azim, 5, 2, 128), ((0, 0), (0, 0), (0, 2), (0, 0)))
    same_zone = dest // n_azim == zone
    to_prev = (same_zone & (dest_azim == (azim - 1) % n_azim))[:, None, None, None]
    to_next = (same_zone & (dest_azim == (azim + 1) % n_azim))[:, None, None, None]
    chunks = jnp.where(
        to_prev, upper_face[None], jnp.where(to_next, lower_face[None], jnp.where(same_zone[:, None, None, None], 0.0, iface_out))
    )
    got = lax.all_to_all(chunks, ("zone", "azim"), 0, 0)
    base = (1 - zone) * n_azim
    up_az = lax.dynamic_index_in_dim(got, zone * n_azim + (azim + 1) % n_azim, 0, keepdims=False)
    down_az = lax.dynamic_index_in_dim(got, zone * n_azim + (azim - 1) % n_azim, 0, keepdims=False)
    direction = jnp.where(is_rotor, -1, 1)
    picked = [
        lax.dynamic_index_in_dim(
            got, base + (azim + direction * (turn + step)) % n_azim, 0, keepdims=False
        )[:, :2].reshape(5, AP, TP)
        for step in (-1, 0, 1)
    ]
    returned = picked[0] + picked[1] + picked[2]
    window = jnp.concatenate(picked, axis=2)
    incoming = shift_sum(window, coefs, TP)
    field_shape = jax.ShapeDtypeStruct(adjoint.shape, jnp.float32)
    early_in = (adjoint, flow_prim, got_first) + (() if got_second is None else (got_second,))
    partial = pl.pallas_call(early_kernel, out_shape=field_shape)(*early_in)
    adjoint_rate, next_adjoint = pl.pallas_call(late_kernel, out_shape=(field_shape, field_shape))(
        adjoint, flow_prim, partial, up_az, down_az, returned.reshape(5 * AP, TP), incoming.reshape(5 * AP, TP)
    )
    return (adjoint_rate, next_adjoint)


def solution(mesh):
    placed = (
        P("zone", None, None, None, None, ("axial", "azim")),
        P("zone", None, None, None, None, ("axial", "azim")),
        P(None, ("axial", "azim")),
        P(None, ("axial", "azim")),
        P(),
        P(),
    )
    return jax.shard_map(
        local,
        mesh=mesh,
        in_specs=placed,
        out_specs=(
            P("zone", None, None, None, None, ("axial", "azim")),
            P("zone", None, None, None, None, ("axial", "azim")),
        ),
        check_vma=False,
    )
```

```python
import functools
import math

import jax
import jax.numpy as jnp
from jax import lax
from jax.experimental import pallas as pl
from jax.experimental.pallas import tpu as pltpu
from jax.sharding import PartitionSpec as P

EA = 4
ET = 4
ER = 8
INTERSECTIONS = 4
NW = 128
AP = 16
TP = 16


GAMMA = 1.4
METRIC = 0.1
SECTION_STEP = 0.5


def gauss_nodes():
    root_term = math.sqrt(6.0 / 5.0)
    inner_node = math.sqrt(3.0 / 7.0 - 2.0 / 7.0 * root_term)
    outer_node = math.sqrt(3.0 / 7.0 + 2.0 / 7.0 * root_term)
    return [-outer_node, -inner_node, inner_node, outer_node]


def lagrange_value(node_list, column, position):
    result = 1.0
    for factor_index in range(4):
        if factor_index != column:
            result = (
                result
                * (position - node_list[factor_index])
                / (node_list[column] - node_list[factor_index])
            )
    return result


def lagrange_slope(node_list, column, position):
    total = 0.0
    for skipped in range(4):
        if skipped == column:
            continue
        term = 1.0 / (node_list[column] - node_list[skipped])
        for factor_index in range(4):
            if factor_index != column and factor_index != skipped:
                term = (
                    term
                    * (position - node_list[factor_index])
                    / (node_list[column] - node_list[factor_index])
                )
        total = total + term
    return total


def basis_tables():
    node_list = gauss_nodes()
    derivs = [
        [lagrange_slope(node_list, column, node_list[source]) for column in range(4)]
        for source in range(4)
    ]
    left_vals = [lagrange_value(node_list, column, -1.0) for column in range(4)]
    right_vals = [lagrange_value(node_list, column, 1.0) for column in range(4)]
    third_slope = [(15.0 * value * value - 3.0) / 2.0 for value in node_list]
    fourth_slope = [(35.0 * value**3 - 15.0 * value) / 2.0 for value in node_list]
    left_corr = [-0.5 * (third_slope[source] - fourth_slope[source]) for source in range(4)]
    right_corr = [0.5 * (third_slope[source] + fourth_slope[source]) for source in range(4)]
    return (derivs, left_vals, right_vals, left_corr, right_corr)


def apply_points(adj_field, matrix, point_dim):
    slab_list = [
        lax.index_in_dim(adj_field, source, point_dim, keepdims=False) for source in range(4)
    ]
    outputs = []
    for target in range(4):
        running = slab_list[0] * float(matrix[0][target])
        for source in range(1, 4):
            running = running + slab_list[source] * float(matrix[source][target])
        outputs.append(running)
    return jnp.stack(outputs, axis=point_dim)


def face_moment(adj_field, vector, point_dim):
    running = lax.index_in_dim(adj_field, 0, point_dim, keepdims=False) * float(vector[0])
    for source in range(1, 4):
        running = running + lax.index_in_dim(adj_field, source, point_dim, keepdims=False) * float(
            vector[source]
        )
    return running


def lift_face(face_vals, vector, point_dim):
    return jnp.stack([face_vals * float(vector[target]) for target in range(4)], axis=point_dim)


def conserved(primitive):
    density = primitive[0]
    velocity = primitive[1:4]
    pressure = primitive[4]
    energy = pressure / (GAMMA - 1.0) + 0.5 * density * jnp.sum(velocity * velocity, axis=0)
    return jnp.concatenate([density[None], density[None] * velocity, energy[None]], axis=0)


def euler_flux(cons_state, direction):
    density = cons_state[0]
    momentum = cons_state[1:4]
    energy = cons_state[4]
    velocity = momentum / density[None]
    pressure = (GAMMA - 1.0) * (energy - 0.5 * jnp.sum(momentum * velocity, axis=0))
    normal_speed = velocity[direction]
    columns = [momentum[direction]]
    for component in range(3):
        if component == direction:
            columns.append(momentum[component] * normal_speed + pressure)
        else:
            columns.append(momentum[component] * normal_speed)
    columns.append((energy + pressure) * normal_speed)
    return jnp.stack(columns, axis=0)


def transpose_flux(cons_state, cotangent, direction):
    unused, pullback = jax.vjp(lambda current: euler_flux(current, direction), cons_state)
    return pullback(cotangent)[0]


def section_rate(adj_field, cons_state, left_moments, right_moments, next_left, prev_right):
    derivs, left_vals, right_vals, left_corr, right_corr = basis_tables()
    rate_sum = jnp.zeros_like(adj_field)
    for direction in range(3):
        point_dim = 1 + direction
        bracket = apply_points(adj_field, derivs, point_dim)
        bracket = bracket + 0.5 * lift_face(
            next_left[direction] - right_moments[direction], right_vals, point_dim
        )
        bracket = bracket + 0.5 * lift_face(
            prev_right[direction] - left_moments[direction], left_vals, point_dim
        )
        rate_sum = rate_sum - METRIC * transpose_flux(cons_state, bracket, direction)
    return rate_sum


def all_moments(adj_field):
    derivs, left_vals, right_vals, left_corr, right_corr = basis_tables()
    left_moments = [face_moment(adj_field, left_corr, 1 + direction) for direction in range(3)]
    right_moments = [face_moment(adj_field, right_corr, 1 + direction) for direction in range(3)]
    return (left_moments, right_moments)


def faces_to_rows(face_vals):
    axial_elems = face_vals.shape[3]
    azim_elems = face_vals.shape[4]
    return face_vals.transpose(0, 3, 1, 4, 2).reshape(5, 4 * axial_elems, 4 * azim_elems)


def rows_to_face(rows_vals, axial_elems, azim_elems):
    return rows_vals.reshape(5, axial_elems, 4, azim_elems, 4).transpose(0, 2, 4, 1, 3)


def shift_sum(window, coefs, lo):
    total = None
    for offset, coef in coefs:
        term = coef[None] * window[:, :, lo + offset : lo + offset + TP]
        total = term if total is None else total + term
    return total


def lane_roll(value, shift):
    return pltpu.roll(value, shift % 128, value.ndim - 1)


def sweep(field, weights, pick):
    total = field[pick(0)] * float(weights[0])
    for source in range(1, 4):
        total = total + field[pick(source)] * float(weights[source])
    return total


def column(values, shape):
    rows = lax.broadcasted_iota(jnp.int32, shape, 2)
    out = jnp.full(shape, float(values[3]), jnp.float32)
    for index in range(3):
        out = jnp.where(rows == index, float(values[index]), out)
    return out


def compact_face(face, part):
    lane = lax.broadcasted_iota(jnp.int32, (4, 128), 1)
    out = jnp.zeros((4, 128), jnp.float32)
    for block in range(4):
        for group in range(EA):
            shift = block * ET * ER - group * (ET - 1) * ER - part * ER
            start = block * ET * ER + group * ER
            mask = (lane >= start) & (lane < start + ER)
            out = jnp.where(mask, lane_roll(face[block], shift), out)
    return out


def expand_face(chunk, part):
    lane = lax.broadcasted_iota(jnp.int32, (4, 128), 1)
    group_of = lane // (ET * ER)
    in_part = lane // ER % ET == part
    blocks = []
    for block in range(4):
        out = jnp.zeros((4, 128), jnp.float32)
        for group in range(EA):
            shift = block * ET * ER - group * (ET - 1) * ER - part * ER
            out = jnp.where(in_part & (group_of == group), lane_roll(chunk, -shift), out)
        blocks.append(out)
    return jnp.stack(blocks, axis=0)


def selector(rows, cols, lane_of, use_rows):
    row = lax.broadcasted_iota(jnp.int32, (rows, cols), 0)
    col = lax.broadcasted_iota(jnp.int32, (rows, cols), 1)
    if use_rows:
        hit = (row == lane_of(col)) & (row < EA * ET)
    else:
        hit = (row == lane_of(col)) & (col < EA * ET)
    return jnp.where(hit, 1.0, 0.0)


def exact_dot(left, right):
    return jnp.dot(left, right, precision=lax.Precision.HIGHEST, preferred_element_type=jnp.float32)


def moment_kernel(
    adj_ref, shift_ref, index_ref, table_ref, offset_ref,
    left_ax_ref, right_ax_ref, up_ref, down_ref, own_ref, weight_ref, place_ref, scratch_ref,
):
    index = index_ref[...]
    weight = jnp.zeros(index.shape, jnp.float32)
    for entry in range(table_ref.shape[0]):
        weight = jnp.where(index == entry, table_ref[entry], weight)
    weight_ref[...] = weight
    offset = offset_ref[0]
    turn = (offset + TP // 2) // TP
    place_ref[...] = shift_ref[...] + (offset - turn * TP)
    derivs, left_vals, right_vals, left_corr, right_corr = basis_tables()
    pick_outer = selector(128, 128, lambda k: k // ET * ET * ER + k % ET * ER + ER - 1, False)
    pick_inner = selector(128, 128, lambda k: k // ET * ET * ER + k % ET * ER, False)
    rotor = lax.axis_index("zone") == 0
    pick = jnp.where(rotor, pick_outer, pick_inner)
    for chan in range(5):
        field = adj_ref[0, chan]
        left_ax_ref[chan] = sweep(field, left_corr, lambda i: (i,))
        right_ax_ref[chan] = sweep(field, right_corr, lambda i: (i,))
        pick1 = lambda i: (slice(None), i)
        up_ref[chan] = compact_face(sweep(field, left_corr, pick1), 0)
        down_ref[chan] = compact_face(sweep(field, right_corr, pick1), ET - 1)
        pick2 = lambda i: (slice(None), slice(None), slice(i, i + 1))
        outer = sweep(field, right_corr, pick2)
        inner = sweep(field, left_corr, pick2)
        for axial in range(4):
            for azim in range(4):
                row = axial * 4 + azim
                scratch_ref[0, row : row + 1] = outer[axial, azim]
                scratch_ref[1, row : row + 1] = inner[axial, azim]
        rows = jnp.where(rotor, scratch_ref[0], scratch_ref[1])
        own_ref[chan] = exact_dot(rows, pick)[:, : EA * ET]


def flow_terms(flow_ref):
    prim = [flow_ref[0, chan].astype(jnp.float32) for chan in range(5)]
    density = prim[0]
    speed_sq = prim[1] * prim[1] + prim[2] * prim[2] + prim[3] * prim[3]
    energy = prim[4] / (GAMMA - 1.0) + 0.5 * density * speed_sq
    momentum = [density * prim[1 + k] for k in range(3)]
    velocity = [momentum[k] / density for k in range(3)]
    kinetic = momentum[0] * velocity[0] + momentum[1] * velocity[1] + momentum[2] * velocity[2]
    pressure = (GAMMA - 1.0) * (energy - 0.5 * kinetic)
    enthalpy = (energy + pressure) / density
    vel_sq = velocity[0] * velocity[0] + velocity[1] * velocity[1] + velocity[2] * velocity[2]
    return velocity, enthalpy, vel_sq


def flux_transpose(grad, cot, direction, velocity, enthalpy, vel_sq):
    normal = velocity[direction]
    dotted = cot[1] * velocity[0] + cot[2] * velocity[1] + cot[3] * velocity[2] + cot[4] * enthalpy
    weight = cot[1 + direction] + cot[4] * normal
    terms = [
        0.5 * (GAMMA - 1.0) * vel_sq * weight - dotted * normal,
        None,
        None,
        None,
        (GAMMA - 1.0) * weight + cot[4] * normal,
    ]
    for k in range(3):
        term = cot[1 + k] * normal - (GAMMA - 1.0) * weight * velocity[k]
        if k == direction:
            term = term + (cot[0] + dotted)
        terms[1 + k] = term
    return [terms[c] if grad[c] is None else grad[c] + terms[c] for c in range(5)]


def early_kernel(adj_ref, flow_ref, first_ref, *rest):
    if len(rest) == 2:
        second_ref, grad_ref = rest
    else:
        second_ref, grad_ref = None, rest[0]
    derivs, left_vals, right_vals, left_corr, right_corr = basis_tables()
    shape = (4, 4, 4, 128)
    lane = lax.broadcasted_iota(jnp.int32, shape, 3)
    flat_lane = lax.broadcasted_iota(jnp.int32, (4, 4, 128), 2)
    radial_lane = lane % ER
    even = lax.axis_index("axial") % 2 == 0
    brackets = [[None] * 5 for _ in range(3)]
    for chan in range(5):
        field = adj_ref[0, chan]
        first = first_ref[chan]
        second = first * 0.0 if second_ref is None else second_ref[chan]
        up_ax = jnp.where(even, first, second)
        down_ax = jnp.where(even, second, first)
        left0 = sweep(field, left_corr, lambda i: (i,))
        right0 = sweep(field, right_corr, lambda i: (i,))
        next0 = lane_roll(jnp.where(flat_lane < ET * ER, up_ax, left0), -ET * ER)
        prev0 = lane_roll(jnp.where(flat_lane >= (EA - 1) * ET * ER, down_ax, right0), ET * ER)
        jump_r = 0.5 * (next0 - right0)
        jump_l = 0.5 * (prev0 - left0)
        slabs = []
        for target in range(4):
            slab = sweep(field, [derivs[i][target] for i in range(4)], lambda i: (i,))
            slabs.append(slab + jump_r * float(right_vals[target]) + jump_l * float(left_vals[target]))
        brackets[0][chan] = jnp.stack(slabs, axis=0)
        points = [jnp.broadcast_to(field[:, :, i : i + 1, :], shape) for i in range(4)]
        left2 = sweep(points, left_corr, lambda i: i)
        right2 = sweep(points, right_corr, lambda i: i)
        next2 = jnp.where(radial_lane == ER - 1, 0.0, lane_roll(left2, -1))
        prev2 = jnp.where(radial_lane == 0, 0.0, lane_roll(right2, 1))
        bracket = 0.5 * (next2 - right2) * column(right_vals, shape)
        bracket = bracket + 0.5 * (prev2 - left2) * column(left_vals, shape)
        for source in range(4):
            bracket = bracket + points[source] * column(derivs[source], shape)
        brackets[2][chan] = bracket
    velocity, enthalpy, vel_sq = flow_terms(flow_ref)
    grad = [None] * 5
    for direction in (0, 2):
        grad = flux_transpose(grad, brackets[direction], direction, velocity, enthalpy, vel_sq)
    for chan in range(5):
        grad_ref[0, chan] = grad[chan]


def late_kernel(adj_ref, flow_ref, grad_ref, up_az_ref, down_az_ref, sides_ref, rate_ref, next_ref):
    derivs, left_vals, right_vals, left_corr, right_corr = basis_tables()
    shape = (4, 4, 4, 128)
    lane = lax.broadcasted_iota(jnp.int32, shape, 3)
    flat_lane = lax.broadcasted_iota(jnp.int32, (4, 4, 128), 2)
    az_flat = flat_lane // ER % ET
    radial_lane = lane % ER
    col = lax.broadcasted_iota(jnp.int32, (16, 128), 1)
    row = lax.broadcasted_iota(jnp.int32, (16, 128), 0)
    sides = sides_ref[...]
    rotor = lax.axis_index("zone") == 0
    spread = [
        exact_dot(sides, jnp.where(row == col // ER % ET * 4 + azim, 1.0, 0.0)) for azim in range(4)
    ]
    group = lax.broadcasted_iota(jnp.int32, (1, 128), 1) // (ET * ER)

    def side_face(chan):
        blocks = []
        for axial in range(4):
            slabs = []
            for azim in range(4):
                base = chan * 16 + axial
                value = spread[azim][base : base + 1]
                for elem in range(1, EA):
                    pos = base + elem * 4
                    value = jnp.where(group == elem, spread[azim][pos : pos + 1], value)
                slabs.append(jnp.broadcast_to(value, (4, 128)))
            blocks.append(jnp.stack(slabs, axis=0))
        return jnp.stack(blocks, axis=0)

    azim_b = [None] * 5
    radial_b = [None] * 5
    for chan in range(5):
        field = adj_ref[0, chan]
        own_face = side_face(chan)
        outer_face = jnp.where(rotor & (radial_lane == ER - 1), own_face, 0.0)
        inner_face = jnp.where(rotor | (radial_lane != 0), 0.0, own_face)
        radial_b[chan] = 0.5 * outer_face * column(right_vals, shape) + 0.5 * inner_face * column(
            left_vals, shape
        )
        up_az = expand_face(up_az_ref[chan], 0)
        down_az = expand_face(down_az_ref[chan], ET - 1)
        pick1 = lambda i: (slice(None), i)
        left1 = sweep(field, left_corr, pick1)
        right1 = sweep(field, right_corr, pick1)
        next1 = lane_roll(jnp.where(az_flat == 0, lane_roll(up_az, ET * ER), left1), -ER)
        prev1 = lane_roll(jnp.where(az_flat == ET - 1, lane_roll(down_az, -ET * ER), right1), ER)
        jump_r = 0.5 * (next1 - right1)
        jump_l = 0.5 * (prev1 - left1)
        slabs = []
        for target in range(4):
            slab = sweep(field, [derivs[i][target] for i in range(4)], pick1)
            slabs.append(slab + jump_r * float(right_vals[target]) + jump_l * float(left_vals[target]))
        azim_b[chan] = jnp.stack(slabs, axis=1)
    velocity, enthalpy, vel_sq = flow_terms(flow_ref)
    grad = [grad_ref[0, chan] for chan in range(5)]
    grad = flux_transpose(grad, azim_b, 1, velocity, enthalpy, vel_sq)
    grad = flux_transpose(grad, radial_b, 2, velocity, enthalpy, vel_sq)
    for chan in range(5):
        rate = -METRIC * grad[chan]
        rate_ref[0, chan] = rate
        next_ref[0, chan] = adj_ref[0, chan] + SECTION_STEP * rate


def local(adjoint, flow_prim, intersection_shift, weight_index, mortar_weights, sector_offset):
    n_axial = lax.axis_size("axial")
    n_azim = lax.axis_size("azim")
    face4 = jax.ShapeDtypeStruct((5, 4, 4, 128), jnp.float32)
    chunk = jax.ShapeDtypeStruct((5, 4, 128), jnp.float32)
    rows16 = jax.ShapeDtypeStruct((5, 16, 128), jnp.float32)
    left_ax, right_ax, upper_face, lower_face, own_face, weights_flat, places = pl.pallas_call(
        moment_kernel,
        out_shape=(face4, face4, chunk, chunk, jax.ShapeDtypeStruct((5, 16, EA * ET), jnp.float32),
            jax.ShapeDtypeStruct(weight_index.shape, jnp.float32),
            jax.ShapeDtypeStruct(intersection_shift.shape, jnp.int32),
        ),
        in_specs=[pl.BlockSpec(memory_space=pltpu.VMEM)] * 3 + [pl.BlockSpec(memory_space=pltpu.SMEM)] * 2,
        scratch_shapes=[pltpu.VMEM((2, 16, 128), jnp.float32)],
    )(adjoint, intersection_shift, weight_index, mortar_weights, sector_offset)
    is_rotor = lax.axis_index("zone") == 0
    even = lax.axis_index("axial") % 2 == 0
    first = [(i, i + 1) for i in range(0, n_axial - 1, 2)] + [(i, i - 1) for i in range(1, n_axial, 2)]
    second = [(i, i + 1) for i in range(1, n_axial - 1, 2)] + [(i, i - 1) for i in range(2, n_axial, 2)]
    got_first = lax.ppermute(jnp.where(even, right_ax, left_ax), "axial", first)
    if second:
        got_second = lax.ppermute(jnp.where(even, left_ax, right_ax), "axial", second)
    else:
        got_second = None
    own_rows = own_face.reshape(5, 4, 4, EA, ET).transpose(0, 3, 1, 4, 2).reshape(5, AP, TP)
    weights_local = weights_flat.reshape(INTERSECTIONS, AP, TP)
    offset = sector_offset[0]
    turn = (offset + TP // 2) // TP
    offsets_k = places.reshape(INTERSECTIONS, AP, TP)
    rel_all = jnp.arange(-TP, TP - 1, dtype=jnp.int32)[:, None, None]
    coef_all = jnp.where(offsets_k[0][None] == rel_all, weights_local[0][None], 0.0)
    for member in range(1, INTERSECTIONS):
        coef_all = coef_all + jnp.where(offsets_k[member][None] == rel_all, weights_local[member][None], 0.0)
    coefs = [(rel, coef_all[rel + TP]) for rel in range(-TP, TP - 1)]
    contrib = None
    for rel, coef in coefs:
        term = jnp.pad(coef[None] * own_rows, ((0, 0), (0, 0), (TP + rel, TP - rel)))
        contrib = term if contrib is None else contrib + term
    zone = lax.axis_index("zone")
    azim = lax.axis_index("azim")
    dest = jnp.arange(2 * n_azim, dtype=jnp.int32)
    dest_azim = dest % n_azim
    gap = ((dest_azim - azim) % n_azim - turn) % n_azim
    gap = gap[:, None, None, None]
    pieces = jnp.where(
        gap == n_azim - 1,
        contrib[None, :, :, :TP],
        jnp.where(gap == 0, contrib[None, :, :, TP : 2 * TP], contrib[None, :, :, 2 * TP :]),
    )
    iface_out = jnp.where(is_rotor, jnp.broadcast_to(own_rows[None], pieces.shape), pieces)
    iface_out = jnp.pad(iface_out.reshape(2 * n_azim, 5, 2, 128), ((0, 0), (0, 0), (0, 2), (0, 0)))
    same_zone = dest // n_azim == zone
    to_prev = (same_zone & (dest_azim == (azim - 1) % n_azim))[:, None, None, None]
    to_next = (same_zone & (dest_azim == (azim + 1) % n_azim))[:, None, None, None]
    chunks = jnp.where(
        to_prev, upper_face[None], jnp.where(to_next, lower_face[None], jnp.where(same_zone[:, None, None, None], 0.0, iface_out))
    )
    got = lax.all_to_all(chunks, ("zone", "azim"), 0, 0)
    base = (1 - zone) * n_azim
    up_az = lax.dynamic_index_in_dim(got, zone * n_azim + (azim + 1) % n_azim, 0, keepdims=False)
    down_az = lax.dynamic_index_in_dim(got, zone * n_azim + (azim - 1) % n_azim, 0, keepdims=False)
    direction = jnp.where(is_rotor, -1, 1)
    picked = [
        lax.dynamic_index_in_dim(
            got, base + (azim + direction * (turn + step)) % n_azim, 0, keepdims=False
        )[:, :2].reshape(5, AP, TP)
        for step in (-1, 0, 1)
    ]
    returned = picked[0] + picked[1] + picked[2]
    window = jnp.concatenate(picked, axis=2)
    incoming = shift_sum(window, coefs, TP)
    sides = jnp.where(is_rotor, returned, incoming).reshape(5 * AP, TP)
    field_shape = jax.ShapeDtypeStruct(adjoint.shape, jnp.float32)
    early_in = (adjoint, flow_prim, got_first) + (() if got_second is None else (got_second,))
    partial = pl.pallas_call(early_kernel, out_shape=field_shape)(*early_in)
    adjoint_rate, next_adjoint = pl.pallas_call(late_kernel, out_shape=(field_shape, field_shape))(
        adjoint, flow_prim, partial, up_az, down_az, sides
    )
    return (adjoint_rate, next_adjoint)


def solution(mesh):
    placed = (
        P("zone", None, None, None, None, ("axial", "azim")),
        P("zone", None, None, None, None, ("axial", "azim")),
        P(None, ("axial", "azim")),
        P(None, ("axial", "azim")),
        P(),
        P(),
    )
    return jax.shard_map(
        local,
        mesh=mesh,
        in_specs=placed,
        out_specs=(
            P("zone", None, None, None, None, ("axial", "azim")),
            P("zone", None, None, None, None, ("axial", "azim")),
        ),
        check_vma=False,
    )
```

```python
import functools
import math

import jax
import jax.numpy as jnp
from jax import lax
from jax.experimental import pallas as pl
from jax.experimental.pallas import tpu as pltpu
from jax.sharding import PartitionSpec as P

EA = 4
ET = 4
ER = 8
INTERSECTIONS = 4
NW = 128
AP = 16
TP = 16


GAMMA = 1.4
METRIC = 0.1
SECTION_STEP = 0.5


def gauss_nodes():
    root_term = math.sqrt(6.0 / 5.0)
    inner_node = math.sqrt(3.0 / 7.0 - 2.0 / 7.0 * root_term)
    outer_node = math.sqrt(3.0 / 7.0 + 2.0 / 7.0 * root_term)
    return [-outer_node, -inner_node, inner_node, outer_node]


def lagrange_value(node_list, column, position):
    result = 1.0
    for factor_index in range(4):
        if factor_index != column:
            result = (
                result
                * (position - node_list[factor_index])
                / (node_list[column] - node_list[factor_index])
            )
    return result


def lagrange_slope(node_list, column, position):
    total = 0.0
    for skipped in range(4):
        if skipped == column:
            continue
        term = 1.0 / (node_list[column] - node_list[skipped])
        for factor_index in range(4):
            if factor_index != column and factor_index != skipped:
                term = (
                    term
                    * (position - node_list[factor_index])
                    / (node_list[column] - node_list[factor_index])
                )
        total = total + term
    return total


def basis_tables():
    node_list = gauss_nodes()
    derivs = [
        [lagrange_slope(node_list, column, node_list[source]) for column in range(4)]
        for source in range(4)
    ]
    left_vals = [lagrange_value(node_list, column, -1.0) for column in range(4)]
    right_vals = [lagrange_value(node_list, column, 1.0) for column in range(4)]
    third_slope = [(15.0 * value * value - 3.0) / 2.0 for value in node_list]
    fourth_slope = [(35.0 * value**3 - 15.0 * value) / 2.0 for value in node_list]
    left_corr = [-0.5 * (third_slope[source] - fourth_slope[source]) for source in range(4)]
    right_corr = [0.5 * (third_slope[source] + fourth_slope[source]) for source in range(4)]
    return (derivs, left_vals, right_vals, left_corr, right_corr)


def apply_points(adj_field, matrix, point_dim):
    slab_list = [
        lax.index_in_dim(adj_field, source, point_dim, keepdims=False) for source in range(4)
    ]
    outputs = []
    for target in range(4):
        running = slab_list[0] * float(matrix[0][target])
        for source in range(1, 4):
            running = running + slab_list[source] * float(matrix[source][target])
        outputs.append(running)
    return jnp.stack(outputs, axis=point_dim)


def face_moment(adj_field, vector, point_dim):
    running = lax.index_in_dim(adj_field, 0, point_dim, keepdims=False) * float(vector[0])
    for source in range(1, 4):
        running = running + lax.index_in_dim(adj_field, source, point_dim, keepdims=False) * float(
            vector[source]
        )
    return running


def lift_face(face_vals, vector, point_dim):
    return jnp.stack([face_vals * float(vector[target]) for target in range(4)], axis=point_dim)


def conserved(primitive):
    density = primitive[0]
    velocity = primitive[1:4]
    pressure = primitive[4]
    energy = pressure / (GAMMA - 1.0) + 0.5 * density * jnp.sum(velocity * velocity, axis=0)
    return jnp.concatenate([density[None], density[None] * velocity, energy[None]], axis=0)


def euler_flux(cons_state, direction):
    density = cons_state[0]
    momentum = cons_state[1:4]
    energy = cons_state[4]
    velocity = momentum / density[None]
    pressure = (GAMMA - 1.0) * (energy - 0.5 * jnp.sum(momentum * velocity, axis=0))
    normal_speed = velocity[direction]
    columns = [momentum[direction]]
    for component in range(3):
        if component == direction:
            columns.append(momentum[component] * normal_speed + pressure)
        else:
            columns.append(momentum[component] * normal_speed)
    columns.append((energy + pressure) * normal_speed)
    return jnp.stack(columns, axis=0)


def transpose_flux(cons_state, cotangent, direction):
    unused, pullback = jax.vjp(lambda current: euler_flux(current, direction), cons_state)
    return pullback(cotangent)[0]


def section_rate(adj_field, cons_state, left_moments, right_moments, next_left, prev_right):
    derivs, left_vals, right_vals, left_corr, right_corr = basis_tables()
    rate_sum = jnp.zeros_like(adj_field)
    for direction in range(3):
        point_dim = 1 + direction
        bracket = apply_points(adj_field, derivs, point_dim)
        bracket = bracket + 0.5 * lift_face(
            next_left[direction] - right_moments[direction], right_vals, point_dim
        )
        bracket = bracket + 0.5 * lift_face(
            prev_right[direction] - left_moments[direction], left_vals, point_dim
        )
        rate_sum = rate_sum - METRIC * transpose_flux(cons_state, bracket, direction)
    return rate_sum


def all_moments(adj_field):
    derivs, left_vals, right_vals, left_corr, right_corr = basis_tables()
    left_moments = [face_moment(adj_field, left_corr, 1 + direction) for direction in range(3)]
    right_moments = [face_moment(adj_field, right_corr, 1 + direction) for direction in range(3)]
    return (left_moments, right_moments)


def faces_to_rows(face_vals):
    axial_elems = face_vals.shape[3]
    azim_elems = face_vals.shape[4]
    return face_vals.transpose(0, 3, 1, 4, 2).reshape(5, 4 * axial_elems, 4 * azim_elems)


def rows_to_face(rows_vals, axial_elems, azim_elems):
    return rows_vals.reshape(5, axial_elems, 4, azim_elems, 4).transpose(0, 2, 4, 1, 3)


def shift_sum(window, coefs, lo):
    total = None
    for offset, coef in coefs:
        term = coef[None] * window[:, :, lo + offset : lo + offset + TP]
        total = term if total is None else total + term
    return total


def lane_roll(value, shift):
    return pltpu.roll(value, shift % 128, value.ndim - 1)


def sweep(field, weights, pick):
    total = field[pick(0)] * float(weights[0])
    for source in range(1, 4):
        total = total + field[pick(source)] * float(weights[source])
    return total


def column(values, shape):
    rows = lax.broadcasted_iota(jnp.int32, shape, 2)
    out = jnp.full(shape, float(values[3]), jnp.float32)
    for index in range(3):
        out = jnp.where(rows == index, float(values[index]), out)
    return out


def compact_face(face, part):
    lane = lax.broadcasted_iota(jnp.int32, (4, 128), 1)
    out = jnp.zeros((4, 128), jnp.float32)
    for block in range(4):
        for group in range(EA):
            shift = block * ET * ER - group * (ET - 1) * ER - part * ER
            start = block * ET * ER + group * ER
            mask = (lane >= start) & (lane < start + ER)
            out = jnp.where(mask, lane_roll(face[block], shift), out)
    return out


def expand_face(chunk, part):
    lane = lax.broadcasted_iota(jnp.int32, (4, 128), 1)
    group_of = lane // (ET * ER)
    in_part = lane // ER % ET == part
    blocks = []
    for block in range(4):
        out = jnp.zeros((4, 128), jnp.float32)
        for group in range(EA):
            shift = block * ET * ER - group * (ET - 1) * ER - part * ER
            out = jnp.where(in_part & (group_of == group), lane_roll(chunk, -shift), out)
        blocks.append(out)
    return jnp.stack(blocks, axis=0)


def selector(rows, cols, lane_of, use_rows):
    row = lax.broadcasted_iota(jnp.int32, (rows, cols), 0)
    col = lax.broadcasted_iota(jnp.int32, (rows, cols), 1)
    if use_rows:
        hit = (row == lane_of(col)) & (row < EA * ET)
    else:
        hit = (row == lane_of(col)) & (col < EA * ET)
    return jnp.where(hit, 1.0, 0.0)


def exact_dot(left, right):
    return jnp.dot(left, right, precision=lax.Precision.HIGHEST, preferred_element_type=jnp.float32)


def moment_kernel(
    adj_ref, shift_ref, index_ref, table_ref, offset_ref,
    left_ax_ref, right_ax_ref, up_ref, down_ref, own_ref, weight_ref, place_ref, scratch_ref,
):
    index = index_ref[...]
    weight = jnp.zeros(index.shape, jnp.float32)
    for entry in range(table_ref.shape[0]):
        weight = jnp.where(index == entry, table_ref[entry], weight)
    weight_ref[...] = weight
    offset = offset_ref[0]
    turn = (offset + TP // 2) // TP
    place_ref[...] = shift_ref[...] + (offset - turn * TP)
    derivs, left_vals, right_vals, left_corr, right_corr = basis_tables()
    pick_outer = selector(128, 128, lambda k: k // ET * ET * ER + k % ET * ER + ER - 1, False)
    pick_inner = selector(128, 128, lambda k: k // ET * ET * ER + k % ET * ER, False)
    rotor = lax.axis_index("zone") == 0
    pick = jnp.where(rotor, pick_outer, pick_inner)
    for chan in range(5):
        field = adj_ref[0, chan]
        left_ax_ref[chan] = sweep(field, left_corr, lambda i: (i,))
        right_ax_ref[chan] = sweep(field, right_corr, lambda i: (i,))
        pick1 = lambda i: (slice(None), i)
        up_ref[chan] = compact_face(sweep(field, left_corr, pick1), 0)
        down_ref[chan] = compact_face(sweep(field, right_corr, pick1), ET - 1)
        pick2 = lambda i: (slice(None), slice(None), slice(i, i + 1))
        outer = sweep(field, right_corr, pick2)
        inner = sweep(field, left_corr, pick2)
        for axial in range(4):
            for azim in range(4):
                row = axial * 4 + azim
                scratch_ref[0, row : row + 1] = outer[axial, azim]
                scratch_ref[1, row : row + 1] = inner[axial, azim]
        rows = jnp.where(rotor, scratch_ref[0], scratch_ref[1])
        own_ref[chan] = exact_dot(rows, pick)[:, : EA * ET]


def flow_terms(flow_ref):
    prim = [flow_ref[0, chan].astype(jnp.float32) for chan in range(5)]
    density = prim[0]
    speed_sq = prim[1] * prim[1] + prim[2] * prim[2] + prim[3] * prim[3]
    energy = prim[4] / (GAMMA - 1.0) + 0.5 * density * speed_sq
    momentum = [density * prim[1 + k] for k in range(3)]
    velocity = [momentum[k] / density for k in range(3)]
    kinetic = momentum[0] * velocity[0] + momentum[1] * velocity[1] + momentum[2] * velocity[2]
    pressure = (GAMMA - 1.0) * (energy - 0.5 * kinetic)
    enthalpy = (energy + pressure) / density
    vel_sq = velocity[0] * velocity[0] + velocity[1] * velocity[1] + velocity[2] * velocity[2]
    return velocity, enthalpy, vel_sq


def flux_transpose(grad, cot, direction, velocity, enthalpy, vel_sq):
    normal = velocity[direction]
    dotted = cot[1] * velocity[0] + cot[2] * velocity[1] + cot[3] * velocity[2] + cot[4] * enthalpy
    weight = cot[1 + direction] + cot[4] * normal
    terms = [
        0.5 * (GAMMA - 1.0) * vel_sq * weight - dotted * normal,
        None,
        None,
        None,
        (GAMMA - 1.0) * weight + cot[4] * normal,
    ]
    for k in range(3):
        term = cot[1 + k] * normal - (GAMMA - 1.0) * weight * velocity[k]
        if k == direction:
            term = term + (cot[0] + dotted)
        terms[1 + k] = term
    return [terms[c] if grad[c] is None else grad[c] + terms[c] for c in range(5)]


def early_kernel(adj_ref, flow_ref, first_ref, *rest):
    if len(rest) == 2:
        second_ref, grad_ref = rest
    else:
        second_ref, grad_ref = None, rest[0]
    derivs, left_vals, right_vals, left_corr, right_corr = basis_tables()
    shape = (4, 4, 4, 128)
    lane = lax.broadcasted_iota(jnp.int32, shape, 3)
    flat_lane = lax.broadcasted_iota(jnp.int32, (4, 4, 128), 2)
    radial_lane = lane % ER
    even = lax.axis_index("axial") % 2 == 0
    brackets = [[None] * 5 for _ in range(3)]
    for chan in range(5):
        field = adj_ref[0, chan]
        first = first_ref[chan]
        second = first * 0.0 if second_ref is None else second_ref[chan]
        up_ax = jnp.where(even, first, second)
        down_ax = jnp.where(even, second, first)
        left0 = sweep(field, left_corr, lambda i: (i,))
        right0 = sweep(field, right_corr, lambda i: (i,))
        next0 = lane_roll(jnp.where(flat_lane < ET * ER, up_ax, left0), -ET * ER)
        prev0 = lane_roll(jnp.where(flat_lane >= (EA - 1) * ET * ER, down_ax, right0), ET * ER)
        jump_r = 0.5 * (next0 - right0)
        jump_l = 0.5 * (prev0 - left0)
        slabs = []
        for target in range(4):
            slab = sweep(field, [derivs[i][target] for i in range(4)], lambda i: (i,))
            slabs.append(slab + jump_r * float(right_vals[target]) + jump_l * float(left_vals[target]))
        brackets[0][chan] = jnp.stack(slabs, axis=0)
        points = [jnp.broadcast_to(field[:, :, i : i + 1, :], shape) for i in range(4)]
        left2 = sweep(points, left_corr, lambda i: i)
        right2 = sweep(points, right_corr, lambda i: i)
        next2 = jnp.where(radial_lane == ER - 1, 0.0, lane_roll(left2, -1))
        prev2 = jnp.where(radial_lane == 0, 0.0, lane_roll(right2, 1))
        bracket = 0.5 * (next2 - right2) * column(right_vals, shape)
        bracket = bracket + 0.5 * (prev2 - left2) * column(left_vals, shape)
        for source in range(4):
            bracket = bracket + points[source] * column(derivs[source], shape)
        brackets[2][chan] = bracket
    velocity, enthalpy, vel_sq = flow_terms(flow_ref)
    grad = [None] * 5
    for direction in (0, 2):
        grad = flux_transpose(grad, brackets[direction], direction, velocity, enthalpy, vel_sq)
    for chan in range(5):
        grad_ref[0, chan] = grad[chan]


def late_kernel(adj_ref, flow_ref, grad_ref, up_az_ref, down_az_ref, window_ref, coef_ref, rate_ref, next_ref):
    derivs, left_vals, right_vals, left_corr, right_corr = basis_tables()
    shape = (4, 4, 4, 128)
    lane = lax.broadcasted_iota(jnp.int32, shape, 3)
    flat_lane = lax.broadcasted_iota(jnp.int32, (4, 4, 128), 2)
    az_flat = flat_lane // ER % ET
    radial_lane = lane % ER
    col = lax.broadcasted_iota(jnp.int32, (16, 128), 1)
    row = lax.broadcasted_iota(jnp.int32, (16, 128), 0)
    rotor = lax.axis_index("zone") == 0
    window = window_ref[...]
    own = []
    for chan in range(5):
        rows = window[chan * AP : (chan + 1) * AP]
        returned = rows[:, :TP] + rows[:, TP : 2 * TP] + rows[:, 2 * TP :]
        incoming = None
        for rel in range(-TP, TP - 1):
            term = coef_ref[rel + TP] * rows[:, TP + rel : 2 * TP + rel]
            incoming = term if incoming is None else incoming + term
        own.append(jnp.where(rotor, returned, incoming))
    sides = jnp.concatenate(own, axis=0)
    spread = [
        exact_dot(sides, jnp.where(row == col // ER % ET * 4 + azim, 1.0, 0.0)) for azim in range(4)
    ]
    group = lax.broadcasted_iota(jnp.int32, (1, 128), 1) // (ET * ER)

    def side_face(chan):
        blocks = []
        for axial in range(4):
            slabs = []
            for azim in range(4):
                base = chan * 16 + axial
                value = spread[azim][base : base + 1]
                for elem in range(1, EA):
                    pos = base + elem * 4
                    value = jnp.where(group == elem, spread[azim][pos : pos + 1], value)
                slabs.append(jnp.broadcast_to(value, (4, 128)))
            blocks.append(jnp.stack(slabs, axis=0))
        return jnp.stack(blocks, axis=0)

    azim_b = [None] * 5
    radial_b = [None] * 5
    for chan in range(5):
        field = adj_ref[0, chan]
        own_face = side_face(chan)
        outer_face = jnp.where(rotor & (radial_lane == ER - 1), own_face, 0.0)
        inner_face = jnp.where(rotor | (radial_lane != 0), 0.0, own_face)
        radial_b[chan] = 0.5 * outer_face * column(right_vals, shape) + 0.5 * inner_face * column(
            left_vals, shape
        )
        up_az = expand_face(up_az_ref[chan], 0)
        down_az = expand_face(down_az_ref[chan], ET - 1)
        pick1 = lambda i: (slice(None), i)
        left1 = sweep(field, left_corr, pick1)
        right1 = sweep(field, right_corr, pick1)
        next1 = lane_roll(jnp.where(az_flat == 0, lane_roll(up_az, ET * ER), left1), -ER)
        prev1 = lane_roll(jnp.where(az_flat == ET - 1, lane_roll(down_az, -ET * ER), right1), ER)
        jump_r = 0.5 * (next1 - right1)
        jump_l = 0.5 * (prev1 - left1)
        slabs = []
        for target in range(4):
            slab = sweep(field, [derivs[i][target] for i in range(4)], pick1)
            slabs.append(slab + jump_r * float(right_vals[target]) + jump_l * float(left_vals[target]))
        azim_b[chan] = jnp.stack(slabs, axis=1)
    velocity, enthalpy, vel_sq = flow_terms(flow_ref)
    grad = [grad_ref[0, chan] for chan in range(5)]
    grad = flux_transpose(grad, azim_b, 1, velocity, enthalpy, vel_sq)
    grad = flux_transpose(grad, radial_b, 2, velocity, enthalpy, vel_sq)
    for chan in range(5):
        rate = -METRIC * grad[chan]
        rate_ref[0, chan] = rate
        next_ref[0, chan] = adj_ref[0, chan] + SECTION_STEP * rate


def local(adjoint, flow_prim, intersection_shift, weight_index, mortar_weights, sector_offset):
    n_axial = lax.axis_size("axial")
    n_azim = lax.axis_size("azim")
    face4 = jax.ShapeDtypeStruct((5, 4, 4, 128), jnp.float32)
    chunk = jax.ShapeDtypeStruct((5, 4, 128), jnp.float32)
    rows16 = jax.ShapeDtypeStruct((5, 16, 128), jnp.float32)
    left_ax, right_ax, upper_face, lower_face, own_face, weights_flat, places = pl.pallas_call(
        moment_kernel,
        out_shape=(face4, face4, chunk, chunk, jax.ShapeDtypeStruct((5, 16, EA * ET), jnp.float32),
            jax.ShapeDtypeStruct(weight_index.shape, jnp.float32),
            jax.ShapeDtypeStruct(intersection_shift.shape, jnp.int32),
        ),
        in_specs=[pl.BlockSpec(memory_space=pltpu.VMEM)] * 3 + [pl.BlockSpec(memory_space=pltpu.SMEM)] * 2,
        scratch_shapes=[pltpu.VMEM((2, 16, 128), jnp.float32)],
    )(adjoint, intersection_shift, weight_index, mortar_weights, sector_offset)
    is_rotor = lax.axis_index("zone") == 0
    even = lax.axis_index("axial") % 2 == 0
    first = [(i, i + 1) for i in range(0, n_axial - 1, 2)] + [(i, i - 1) for i in range(1, n_axial, 2)]
    second = [(i, i + 1) for i in range(1, n_axial - 1, 2)] + [(i, i - 1) for i in range(2, n_axial, 2)]
    got_first = lax.ppermute(jnp.where(even, right_ax, left_ax), "axial", first)
    if second:
        got_second = lax.ppermute(jnp.where(even, left_ax, right_ax), "axial", second)
    else:
        got_second = None
    own_rows = own_face.reshape(5, 4, 4, EA, ET).transpose(0, 3, 1, 4, 2).reshape(5, AP, TP)
    weights_local = weights_flat.reshape(INTERSECTIONS, AP, TP)
    offset = sector_offset[0]
    turn = (offset + TP // 2) // TP
    offsets_k = places.reshape(INTERSECTIONS, AP, TP)
    rel_all = jnp.arange(-TP, TP - 1, dtype=jnp.int32)[:, None, None]
    coef_all = jnp.where(offsets_k[0][None] == rel_all, weights_local[0][None], 0.0)
    for member in range(1, INTERSECTIONS):
        coef_all = coef_all + jnp.where(offsets_k[member][None] == rel_all, weights_local[member][None], 0.0)
    coefs = [(rel, coef_all[rel + TP]) for rel in range(-TP, TP - 1)]
    contrib = None
    for rel, coef in coefs:
        term = jnp.pad(coef[None] * own_rows, ((0, 0), (0, 0), (TP + rel, TP - rel)))
        contrib = term if contrib is None else contrib + term
    zone = lax.axis_index("zone")
    azim = lax.axis_index("azim")
    dest = jnp.arange(2 * n_azim, dtype=jnp.int32)
    dest_azim = dest % n_azim
    gap = ((dest_azim - azim) % n_azim - turn) % n_azim
    gap = gap[:, None, None, None]
    pieces = jnp.where(
        gap == n_azim - 1,
        contrib[None, :, :, :TP],
        jnp.where(gap == 0, contrib[None, :, :, TP : 2 * TP], contrib[None, :, :, 2 * TP :]),
    )
    iface_out = jnp.where(is_rotor, jnp.broadcast_to(own_rows[None], pieces.shape), pieces)
    iface_out = jnp.pad(iface_out.reshape(2 * n_azim, 5, 2, 128), ((0, 0), (0, 0), (0, 2), (0, 0)))
    same_zone = dest // n_azim == zone
    to_prev = (same_zone & (dest_azim == (azim - 1) % n_azim))[:, None, None, None]
    to_next = (same_zone & (dest_azim == (azim + 1) % n_azim))[:, None, None, None]
    chunks = jnp.where(
        to_prev, upper_face[None], jnp.where(to_next, lower_face[None], jnp.where(same_zone[:, None, None, None], 0.0, iface_out))
    )
    got = lax.all_to_all(chunks, ("zone", "azim"), 0, 0)
    base = (1 - zone) * n_azim
    up_az = lax.dynamic_index_in_dim(got, zone * n_azim + (azim + 1) % n_azim, 0, keepdims=False)
    down_az = lax.dynamic_index_in_dim(got, zone * n_azim + (azim - 1) % n_azim, 0, keepdims=False)
    direction = jnp.where(is_rotor, -1, 1)
    picked = [
        lax.dynamic_index_in_dim(
            got, base + (azim + direction * (turn + step)) % n_azim, 0, keepdims=False
        )[:, :2].reshape(5, AP, TP)
        for step in (-1, 0, 1)
    ]
    window = jnp.concatenate(picked, axis=2).reshape(5 * AP, 3 * TP)
    field_shape = jax.ShapeDtypeStruct(adjoint.shape, jnp.float32)
    early_in = (adjoint, flow_prim, got_first) + (() if got_second is None else (got_second,))
    partial = pl.pallas_call(early_kernel, out_shape=field_shape)(*early_in)
    adjoint_rate, next_adjoint = pl.pallas_call(late_kernel, out_shape=(field_shape, field_shape))(
        adjoint, flow_prim, partial, up_az, down_az, window, coef_all
    )
    return (adjoint_rate, next_adjoint)


def solution(mesh):
    placed = (
        P("zone", None, None, None, None, ("axial", "azim")),
        P("zone", None, None, None, None, ("axial", "azim")),
        P(None, ("axial", "azim")),
        P(None, ("axial", "azim")),
        P(),
        P(),
    )
    return jax.shard_map(
        local,
        mesh=mesh,
        in_specs=placed,
        out_specs=(
            P("zone", None, None, None, None, ("axial", "azim")),
            P("zone", None, None, None, None, ("axial", "azim")),
        ),
        check_vma=False,
    )
```

```python
import functools
import math

import jax
import jax.numpy as jnp
from jax import lax
from jax.experimental import pallas as pl
from jax.experimental.pallas import tpu as pltpu
from jax.sharding import PartitionSpec as P

EA = 4
ET = 4
ER = 8
INTERSECTIONS = 4
NW = 128
AP = 16
TP = 16


GAMMA = 1.4
METRIC = 0.1
SECTION_STEP = 0.5


def gauss_nodes():
    root_term = math.sqrt(6.0 / 5.0)
    inner_node = math.sqrt(3.0 / 7.0 - 2.0 / 7.0 * root_term)
    outer_node = math.sqrt(3.0 / 7.0 + 2.0 / 7.0 * root_term)
    return [-outer_node, -inner_node, inner_node, outer_node]


def lagrange_value(node_list, column, position):
    result = 1.0
    for factor_index in range(4):
        if factor_index != column:
            result = (
                result
                * (position - node_list[factor_index])
                / (node_list[column] - node_list[factor_index])
            )
    return result


def lagrange_slope(node_list, column, position):
    total = 0.0
    for skipped in range(4):
        if skipped == column:
            continue
        term = 1.0 / (node_list[column] - node_list[skipped])
        for factor_index in range(4):
            if factor_index != column and factor_index != skipped:
                term = (
                    term
                    * (position - node_list[factor_index])
                    / (node_list[column] - node_list[factor_index])
                )
        total = total + term
    return total


def basis_tables():
    node_list = gauss_nodes()
    derivs = [
        [lagrange_slope(node_list, column, node_list[source]) for column in range(4)]
        for source in range(4)
    ]
    left_vals = [lagrange_value(node_list, column, -1.0) for column in range(4)]
    right_vals = [lagrange_value(node_list, column, 1.0) for column in range(4)]
    third_slope = [(15.0 * value * value - 3.0) / 2.0 for value in node_list]
    fourth_slope = [(35.0 * value**3 - 15.0 * value) / 2.0 for value in node_list]
    left_corr = [-0.5 * (third_slope[source] - fourth_slope[source]) for source in range(4)]
    right_corr = [0.5 * (third_slope[source] + fourth_slope[source]) for source in range(4)]
    return (derivs, left_vals, right_vals, left_corr, right_corr)


def apply_points(adj_field, matrix, point_dim):
    slab_list = [
        lax.index_in_dim(adj_field, source, point_dim, keepdims=False) for source in range(4)
    ]
    outputs = []
    for target in range(4):
        running = slab_list[0] * float(matrix[0][target])
        for source in range(1, 4):
            running = running + slab_list[source] * float(matrix[source][target])
        outputs.append(running)
    return jnp.stack(outputs, axis=point_dim)


def face_moment(adj_field, vector, point_dim):
    running = lax.index_in_dim(adj_field, 0, point_dim, keepdims=False) * float(vector[0])
    for source in range(1, 4):
        running = running + lax.index_in_dim(adj_field, source, point_dim, keepdims=False) * float(
            vector[source]
        )
    return running


def lift_face(face_vals, vector, point_dim):
    return jnp.stack([face_vals * float(vector[target]) for target in range(4)], axis=point_dim)


def conserved(primitive):
    density = primitive[0]
    velocity = primitive[1:4]
    pressure = primitive[4]
    energy = pressure / (GAMMA - 1.0) + 0.5 * density * jnp.sum(velocity * velocity, axis=0)
    return jnp.concatenate([density[None], density[None] * velocity, energy[None]], axis=0)


def euler_flux(cons_state, direction):
    density = cons_state[0]
    momentum = cons_state[1:4]
    energy = cons_state[4]
    velocity = momentum / density[None]
    pressure = (GAMMA - 1.0) * (energy - 0.5 * jnp.sum(momentum * velocity, axis=0))
    normal_speed = velocity[direction]
    columns = [momentum[direction]]
    for component in range(3):
        if component == direction:
            columns.append(momentum[component] * normal_speed + pressure)
        else:
            columns.append(momentum[component] * normal_speed)
    columns.append((energy + pressure) * normal_speed)
    return jnp.stack(columns, axis=0)


def transpose_flux(cons_state, cotangent, direction):
    unused, pullback = jax.vjp(lambda current: euler_flux(current, direction), cons_state)
    return pullback(cotangent)[0]


def section_rate(adj_field, cons_state, left_moments, right_moments, next_left, prev_right):
    derivs, left_vals, right_vals, left_corr, right_corr = basis_tables()
    rate_sum = jnp.zeros_like(adj_field)
    for direction in range(3):
        point_dim = 1 + direction
        bracket = apply_points(adj_field, derivs, point_dim)
        bracket = bracket + 0.5 * lift_face(
            next_left[direction] - right_moments[direction], right_vals, point_dim
        )
        bracket = bracket + 0.5 * lift_face(
            prev_right[direction] - left_moments[direction], left_vals, point_dim
        )
        rate_sum = rate_sum - METRIC * transpose_flux(cons_state, bracket, direction)
    return rate_sum


def all_moments(adj_field):
    derivs, left_vals, right_vals, left_corr, right_corr = basis_tables()
    left_moments = [face_moment(adj_field, left_corr, 1 + direction) for direction in range(3)]
    right_moments = [face_moment(adj_field, right_corr, 1 + direction) for direction in range(3)]
    return (left_moments, right_moments)


def faces_to_rows(face_vals):
    axial_elems = face_vals.shape[3]
    azim_elems = face_vals.shape[4]
    return face_vals.transpose(0, 3, 1, 4, 2).reshape(5, 4 * axial_elems, 4 * azim_elems)


def rows_to_face(rows_vals, axial_elems, azim_elems):
    return rows_vals.reshape(5, axial_elems, 4, azim_elems, 4).transpose(0, 2, 4, 1, 3)


def shift_sum(window, coefs, lo):
    total = None
    for offset, coef in coefs:
        term = coef[None] * window[:, :, lo + offset : lo + offset + TP]
        total = term if total is None else total + term
    return total


def lane_roll(value, shift):
    return pltpu.roll(value, shift % 128, value.ndim - 1)


def sweep(field, weights, pick):
    total = field[pick(0)] * float(weights[0])
    for source in range(1, 4):
        total = total + field[pick(source)] * float(weights[source])
    return total


def column(values, shape):
    rows = lax.broadcasted_iota(jnp.int32, shape, 2)
    out = jnp.full(shape, float(values[3]), jnp.float32)
    for index in range(3):
        out = jnp.where(rows == index, float(values[index]), out)
    return out


def compact_face(face, part):
    lane = lax.broadcasted_iota(jnp.int32, (4, 128), 1)
    out = jnp.zeros((4, 128), jnp.float32)
    for block in range(4):
        for group in range(EA):
            shift = block * ET * ER - group * (ET - 1) * ER - part * ER
            start = block * ET * ER + group * ER
            mask = (lane >= start) & (lane < start + ER)
            out = jnp.where(mask, lane_roll(face[block], shift), out)
    return out


def expand_face(chunk, part):
    lane = lax.broadcasted_iota(jnp.int32, (4, 128), 1)
    group_of = lane // (ET * ER)
    in_part = lane // ER % ET == part
    blocks = []
    for block in range(4):
        out = jnp.zeros((4, 128), jnp.float32)
        for group in range(EA):
            shift = block * ET * ER - group * (ET - 1) * ER - part * ER
            out = jnp.where(in_part & (group_of == group), lane_roll(chunk, -shift), out)
        blocks.append(out)
    return jnp.stack(blocks, axis=0)


def selector(rows, cols, lane_of, use_rows):
    row = lax.broadcasted_iota(jnp.int32, (rows, cols), 0)
    col = lax.broadcasted_iota(jnp.int32, (rows, cols), 1)
    if use_rows:
        hit = (row == lane_of(col)) & (row < EA * ET)
    else:
        hit = (row == lane_of(col)) & (col < EA * ET)
    return jnp.where(hit, 1.0, 0.0)


def exact_dot(left, right):
    return jnp.dot(left, right, precision=lax.Precision.HIGHEST, preferred_element_type=jnp.float32)


def moment_kernel(
    adj_ref, shift_ref, index_ref, table_ref, offset_ref,
    left_ax_ref, right_ax_ref, up_ref, down_ref, own_ref, weight_ref, place_ref, scratch_ref,
):
    index = index_ref[...]
    weight = jnp.zeros(index.shape, jnp.float32)
    for entry in range(table_ref.shape[0]):
        weight = jnp.where(index == entry, table_ref[entry], weight)
    weight_ref[...] = weight
    offset = offset_ref[0]
    turn = (offset + TP // 2) // TP
    place_ref[...] = shift_ref[...] + (offset - turn * TP)
    derivs, left_vals, right_vals, left_corr, right_corr = basis_tables()
    pick_outer = selector(128, 128, lambda k: k // ET * ET * ER + k % ET * ER + ER - 1, False)
    pick_inner = selector(128, 128, lambda k: k // ET * ET * ER + k % ET * ER, False)
    rotor = lax.axis_index("zone") == 0
    pick = jnp.where(rotor, pick_outer, pick_inner)
    for chan in range(5):
        field = adj_ref[0, chan]
        left_ax_ref[chan] = sweep(field, left_corr, lambda i: (i,))
        right_ax_ref[chan] = sweep(field, right_corr, lambda i: (i,))
        pick1 = lambda i: (slice(None), i)
        up_ref[chan] = compact_face(sweep(field, left_corr, pick1), 0)
        down_ref[chan] = compact_face(sweep(field, right_corr, pick1), ET - 1)
        pick2 = lambda i: (slice(None), slice(None), slice(i, i + 1))
        outer = sweep(field, right_corr, pick2)
        inner = sweep(field, left_corr, pick2)
        for axial in range(4):
            for azim in range(4):
                row = axial * 4 + azim
                scratch_ref[0, row : row + 1] = outer[axial, azim]
                scratch_ref[1, row : row + 1] = inner[axial, azim]
        rows = jnp.where(rotor, scratch_ref[0], scratch_ref[1])
        own_ref[chan] = exact_dot(rows, pick)[:, : EA * ET]


def flow_terms(flow_ref):
    prim = [flow_ref[0, chan].astype(jnp.float32) for chan in range(5)]
    density = prim[0]
    speed_sq = prim[1] * prim[1] + prim[2] * prim[2] + prim[3] * prim[3]
    energy = prim[4] / (GAMMA - 1.0) + 0.5 * density * speed_sq
    momentum = [density * prim[1 + k] for k in range(3)]
    inverse = 1.0 / density
    velocity = [momentum[k] * inverse for k in range(3)]
    kinetic = momentum[0] * velocity[0] + momentum[1] * velocity[1] + momentum[2] * velocity[2]
    pressure = (GAMMA - 1.0) * (energy - 0.5 * kinetic)
    enthalpy = (energy + pressure) * inverse
    vel_sq = velocity[0] * velocity[0] + velocity[1] * velocity[1] + velocity[2] * velocity[2]
    return velocity, enthalpy, vel_sq


def flux_transpose(grad, cot, direction, velocity, enthalpy, vel_sq):
    normal = velocity[direction]
    dotted = cot[1] * velocity[0] + cot[2] * velocity[1] + cot[3] * velocity[2] + cot[4] * enthalpy
    weight = cot[1 + direction] + cot[4] * normal
    terms = [
        0.5 * (GAMMA - 1.0) * vel_sq * weight - dotted * normal,
        None,
        None,
        None,
        (GAMMA - 1.0) * weight + cot[4] * normal,
    ]
    for k in range(3):
        term = cot[1 + k] * normal - (GAMMA - 1.0) * weight * velocity[k]
        if k == direction:
            term = term + (cot[0] + dotted)
        terms[1 + k] = term
    return [terms[c] if grad[c] is None else grad[c] + terms[c] for c in range(5)]


def early_kernel(adj_ref, flow_ref, first_ref, *rest):
    if len(rest) == 2:
        second_ref, grad_ref = rest
    else:
        second_ref, grad_ref = None, rest[0]
    derivs, left_vals, right_vals, left_corr, right_corr = basis_tables()
    shape = (4, 4, 4, 128)
    lane = lax.broadcasted_iota(jnp.int32, shape, 3)
    flat_lane = lax.broadcasted_iota(jnp.int32, (4, 4, 128), 2)
    radial_lane = lane % ER
    even = lax.axis_index("axial") % 2 == 0
    brackets = [[None] * 5 for _ in range(3)]
    for chan in range(5):
        field = adj_ref[0, chan]
        first = first_ref[chan]
        second = first * 0.0 if second_ref is None else second_ref[chan]
        up_ax = jnp.where(even, first, second)
        down_ax = jnp.where(even, second, first)
        left0 = sweep(field, left_corr, lambda i: (i,))
        right0 = sweep(field, right_corr, lambda i: (i,))
        next0 = lane_roll(jnp.where(flat_lane < ET * ER, up_ax, left0), -ET * ER)
        prev0 = lane_roll(jnp.where(flat_lane >= (EA - 1) * ET * ER, down_ax, right0), ET * ER)
        jump_r = 0.5 * (next0 - right0)
        jump_l = 0.5 * (prev0 - left0)
        slabs = []
        for target in range(4):
            slab = sweep(field, [derivs[i][target] for i in range(4)], lambda i: (i,))
            slabs.append(slab + jump_r * float(right_vals[target]) + jump_l * float(left_vals[target]))
        brackets[0][chan] = jnp.stack(slabs, axis=0)
        points = [jnp.broadcast_to(field[:, :, i : i + 1, :], shape) for i in range(4)]
        left2 = sweep(points, left_corr, lambda i: i)
        right2 = sweep(points, right_corr, lambda i: i)
        next2 = jnp.where(radial_lane == ER - 1, 0.0, lane_roll(left2, -1))
        prev2 = jnp.where(radial_lane == 0, 0.0, lane_roll(right2, 1))
        bracket = 0.5 * (next2 - right2) * column(right_vals, shape)
        bracket = bracket + 0.5 * (prev2 - left2) * column(left_vals, shape)
        for source in range(4):
            bracket = bracket + points[source] * column(derivs[source], shape)
        brackets[2][chan] = bracket
    velocity, enthalpy, vel_sq = flow_terms(flow_ref)
    grad = [None] * 5
    for direction in (0, 2):
        grad = flux_transpose(grad, brackets[direction], direction, velocity, enthalpy, vel_sq)
    for chan in range(5):
        grad_ref[0, chan] = grad[chan]


def late_kernel(adj_ref, flow_ref, grad_ref, up_az_ref, down_az_ref, sides_ref, rate_ref, next_ref):
    derivs, left_vals, right_vals, left_corr, right_corr = basis_tables()
    shape = (4, 4, 4, 128)
    lane = lax.broadcasted_iota(jnp.int32, shape, 3)
    flat_lane = lax.broadcasted_iota(jnp.int32, (4, 4, 128), 2)
    az_flat = flat_lane // ER % ET
    radial_lane = lane % ER
    col = lax.broadcasted_iota(jnp.int32, (16, 128), 1)
    row = lax.broadcasted_iota(jnp.int32, (16, 128), 0)
    sides = sides_ref[...]
    rotor = lax.axis_index("zone") == 0
    spread = [
        exact_dot(sides, jnp.where(row == col // ER % ET * 4 + azim, 1.0, 0.0)) for azim in range(4)
    ]
    group = lax.broadcasted_iota(jnp.int32, (1, 128), 1) // (ET * ER)

    def side_face(chan):
        blocks = []
        for axial in range(4):
            slabs = []
            for azim in range(4):
                base = chan * 16 + axial
                value = spread[azim][base : base + 1]
                for elem in range(1, EA):
                    pos = base + elem * 4
                    value = jnp.where(group == elem, spread[azim][pos : pos + 1], value)
                slabs.append(jnp.broadcast_to(value, (4, 128)))
            blocks.append(jnp.stack(slabs, axis=0))
        return jnp.stack(blocks, axis=0)

    azim_b = [None] * 5
    radial_b = [None] * 5
    for chan in range(5):
        field = adj_ref[0, chan]
        own_face = side_face(chan)
        outer_face = jnp.where(rotor & (radial_lane == ER - 1), own_face, 0.0)
        inner_face = jnp.where(rotor | (radial_lane != 0), 0.0, own_face)
        radial_b[chan] = 0.5 * outer_face * column(right_vals, shape) + 0.5 * inner_face * column(
            left_vals, shape
        )
        up_az = expand_face(up_az_ref[chan], 0)
        down_az = expand_face(down_az_ref[chan], ET - 1)
        pick1 = lambda i: (slice(None), i)
        left1 = sweep(field, left_corr, pick1)
        right1 = sweep(field, right_corr, pick1)
        next1 = lane_roll(jnp.where(az_flat == 0, lane_roll(up_az, ET * ER), left1), -ER)
        prev1 = lane_roll(jnp.where(az_flat == ET - 1, lane_roll(down_az, -ET * ER), right1), ER)
        jump_r = 0.5 * (next1 - right1)
        jump_l = 0.5 * (prev1 - left1)
        slabs = []
        for target in range(4):
            slab = sweep(field, [derivs[i][target] for i in range(4)], pick1)
            slabs.append(slab + jump_r * float(right_vals[target]) + jump_l * float(left_vals[target]))
        azim_b[chan] = jnp.stack(slabs, axis=1)
    velocity, enthalpy, vel_sq = flow_terms(flow_ref)
    grad = [grad_ref[0, chan] for chan in range(5)]
    grad = flux_transpose(grad, azim_b, 1, velocity, enthalpy, vel_sq)
    grad = flux_transpose(grad, radial_b, 2, velocity, enthalpy, vel_sq)
    for chan in range(5):
        rate = -METRIC * grad[chan]
        rate_ref[0, chan] = rate
        next_ref[0, chan] = adj_ref[0, chan] + SECTION_STEP * rate


def local(adjoint, flow_prim, intersection_shift, weight_index, mortar_weights, sector_offset):
    n_axial = lax.axis_size("axial")
    n_azim = lax.axis_size("azim")
    face4 = jax.ShapeDtypeStruct((5, 4, 4, 128), jnp.float32)
    chunk = jax.ShapeDtypeStruct((5, 4, 128), jnp.float32)
    rows16 = jax.ShapeDtypeStruct((5, 16, 128), jnp.float32)
    left_ax, right_ax, upper_face, lower_face, own_face, weights_flat, places = pl.pallas_call(
        moment_kernel,
        out_shape=(face4, face4, chunk, chunk, jax.ShapeDtypeStruct((5, 16, EA * ET), jnp.float32),
            jax.ShapeDtypeStruct(weight_index.shape, jnp.float32),
            jax.ShapeDtypeStruct(intersection_shift.shape, jnp.int32),
        ),
        in_specs=[pl.BlockSpec(memory_space=pltpu.VMEM)] * 3 + [pl.BlockSpec(memory_space=pltpu.SMEM)] * 2,
        scratch_shapes=[pltpu.VMEM((2, 16, 128), jnp.float32)],
    )(adjoint, intersection_shift, weight_index, mortar_weights, sector_offset)
    is_rotor = lax.axis_index("zone") == 0
    even = lax.axis_index("axial") % 2 == 0
    first = [(i, i + 1) for i in range(0, n_axial - 1, 2)] + [(i, i - 1) for i in range(1, n_axial, 2)]
    second = [(i, i + 1) for i in range(1, n_axial - 1, 2)] + [(i, i - 1) for i in range(2, n_axial, 2)]
    got_first = lax.ppermute(jnp.where(even, right_ax, left_ax), "axial", first)
    if second:
        got_second = lax.ppermute(jnp.where(even, left_ax, right_ax), "axial", second)
    else:
        got_second = None
    own_rows = own_face.reshape(5, 4, 4, EA, ET).transpose(0, 3, 1, 4, 2).reshape(5, AP, TP)
    weights_local = weights_flat.reshape(INTERSECTIONS, AP, TP)
    offset = sector_offset[0]
    turn = (offset + TP // 2) // TP
    offsets_k = places.reshape(INTERSECTIONS, AP, TP)
    rel_all = jnp.arange(-TP, TP - 1, dtype=jnp.int32)[:, None, None]
    coef_all = jnp.where(offsets_k[0][None] == rel_all, weights_local[0][None], 0.0)
    for member in range(1, INTERSECTIONS):
        coef_all = coef_all + jnp.where(offsets_k[member][None] == rel_all, weights_local[member][None], 0.0)
    coefs = [(rel, coef_all[rel + TP]) for rel in range(-TP, TP - 1)]
    contrib = None
    for rel, coef in coefs:
        term = jnp.pad(coef[None] * own_rows, ((0, 0), (0, 0), (TP + rel, TP - rel)))
        contrib = term if contrib is None else contrib + term
    zone = lax.axis_index("zone")
    azim = lax.axis_index("azim")
    dest = jnp.arange(2 * n_azim, dtype=jnp.int32)
    dest_azim = dest % n_azim
    gap = ((dest_azim - azim) % n_azim - turn) % n_azim
    gap = gap[:, None, None, None]
    pieces = jnp.where(
        gap == n_azim - 1,
        contrib[None, :, :, :TP],
        jnp.where(gap == 0, contrib[None, :, :, TP : 2 * TP], contrib[None, :, :, 2 * TP :]),
    )
    iface_out = jnp.where(is_rotor, jnp.broadcast_to(own_rows[None], pieces.shape), pieces)
    iface_out = jnp.pad(iface_out.reshape(2 * n_azim, 5, 2, 128), ((0, 0), (0, 0), (0, 2), (0, 0)))
    same_zone = dest // n_azim == zone
    to_prev = (same_zone & (dest_azim == (azim - 1) % n_azim))[:, None, None, None]
    to_next = (same_zone & (dest_azim == (azim + 1) % n_azim))[:, None, None, None]
    chunks = jnp.where(
        to_prev, upper_face[None], jnp.where(to_next, lower_face[None], jnp.where(same_zone[:, None, None, None], 0.0, iface_out))
    )
    got = lax.all_to_all(chunks, ("zone", "azim"), 0, 0)
    base = (1 - zone) * n_azim
    up_az = lax.dynamic_index_in_dim(got, zone * n_azim + (azim + 1) % n_azim, 0, keepdims=False)
    down_az = lax.dynamic_index_in_dim(got, zone * n_azim + (azim - 1) % n_azim, 0, keepdims=False)
    direction = jnp.where(is_rotor, -1, 1)
    picked = [
        lax.dynamic_index_in_dim(
            got, base + (azim + direction * (turn + step)) % n_azim, 0, keepdims=False
        )[:, :2].reshape(5, AP, TP)
        for step in (-1, 0, 1)
    ]
    returned = picked[0] + picked[1] + picked[2]
    window = jnp.concatenate(picked, axis=2)
    incoming = shift_sum(window, coefs, TP)
    sides = jnp.where(is_rotor, returned, incoming).reshape(5 * AP, TP)
    field_shape = jax.ShapeDtypeStruct(adjoint.shape, jnp.float32)
    early_in = (adjoint, flow_prim, got_first) + (() if got_second is None else (got_second,))
    partial = pl.pallas_call(early_kernel, out_shape=field_shape)(*early_in)
    adjoint_rate, next_adjoint = pl.pallas_call(late_kernel, out_shape=(field_shape, field_shape))(
        adjoint, flow_prim, partial, up_az, down_az, sides
    )
    return (adjoint_rate, next_adjoint)


def solution(mesh):
    placed = (
        P("zone", None, None, None, None, ("axial", "azim")),
        P("zone", None, None, None, None, ("axial", "azim")),
        P(None, ("axial", "azim")),
        P(None, ("axial", "azim")),
        P(),
        P(),
    )
    return jax.shard_map(
        local,
        mesh=mesh,
        in_specs=placed,
        out_specs=(
            P("zone", None, None, None, None, ("axial", "azim")),
            P("zone", None, None, None, None, ("axial", "azim")),
        ),
        check_vma=False,
    )
```
